128 devices in a mesh: box: 16 (over x, z_hi, core), group: 8 (over y, z_lo).
Axes of the slice: x: 4, y: 4, z: 4 (z_hi: 2, z_lo: 2; z = z_hi * 2 + z_lo), core: 2. Of those that a mesh axis runs over, the one named last changes fastest.
Arguments:
- right_side: float32 [256, 256, 512], P('box', 'group'), may hold values from -6 to 6
- inv_density: float32 [256, 256, 512], P('box', 'group'), may hold values from 0.2 to 5
- pressure: float32 [256, 256, 512], P('box', 'group'), may hold values from -6 to 6
Outputs:
- corrected: float32 [256, 256, 512], P('box', 'group')
The draws below stay inside these ranges and needn't reach their ends.
All inputs are finite; a program needn't handle non-finite values.
Results may differ from the reference program's by a relative error of at most 0.0003.
Values sent between devices are 32-bit elements; how exact they have to be, the bound alone decides.
No kernel may reach another device: no remote copies, remote signals or barrier semaphores. Data moves between devices by JAX's collectives and lax.ppermute only.
A program may use at most 128 MiB of HBM per device.

```python
import math
import jax
import jax.numpy as jnp

CZ = 512
SWEEPS = 2
CHEB = 8
NX = 256
NY = 256


def block_scale(rng, extent, shards, low, high):
    gain, own = 1.0, jax.random.fold_in(rng, 6)
    for position, blocks in shards:
        steps = jnp.exp(jax.random.uniform(jax.random.fold_in(own, position), (blocks,), jnp.float32, low / len(shards), high / len(shards)))
        gain = gain * jnp.repeat(steps, extent[position] // blocks).reshape([-1 if axis == position else 1 for axis in range(len(extent))])
    return gain


def bell_draw(own_key, dims, scale, reach, pieces=(), held_as=jnp.bfloat16):
    factor_of = block_scale(own_key, dims, pieces, -0.22, 0.18) if pieces else 1.0
    drawn = jax.random.normal(own_key, dims, jnp.float32) * scale * factor_of
    return jnp.minimum(jnp.maximum(drawn, -reach), reach).astype(held_as)


def setup_inputs(seed: int = 0) -> dict:
    splits = jax.random.split(jax.random.key(seed), 4)
    right_side = bell_draw(splits[0], (NX, NY, CZ), 1.0, 6.0, ((0, 16), (1, 8)), jnp.float32)
    inv_density = jnp.clip(jnp.exp(math.log(5.0) - 3.218876 * jax.random.uniform(splits[1], (NX, NY, CZ), jnp.float32) ** block_scale(splits[1], (NX, NY, CZ), ((0, 16), (1, 8)), -0.2, 0.2)), 0.2, 5.0)
    pressure = bell_draw(splits[2], (NX, NY, CZ), 1.0, 6.0, ((0, 16), (1, 8)), jnp.float32)
    return {"right_side": right_side, "inv_density": inv_density, "pressure": pressure}


def neighbours(padded):
    return [padded[:-2, 1:-1, 1:-1], padded[2:, 1:-1, 1:-1],
            padded[1:-1, :-2, 1:-1], padded[1:-1, 2:, 1:-1],
            padded[1:-1, 1:-1, :-2], padded[1:-1, 1:-1, 2:]]


def face_coefs(field, padded):
    return [jnp.where(near > 0, 2.0 * field * near / (field + near), field) for near in neighbours(padded)]


def stencil(field, padded, coefs):
    total = jnp.zeros_like(field)
    for coef, near in zip(coefs, neighbours(padded)):
        total = total + coef * (field - near)
    return total


def block_mean(field):
    sx, sy, sz = field.shape
    return field.reshape(sx // 4, 4, sy // 4, 4, sz // 4, 4).mean(axis=(1, 3, 5))


def chebyshev(rhs_c, coefs, diag, padder):
    low, high = 0.05, 2.0
    theta = (high + low) / 2.0
    delta = (high - low) / 2.0
    sigma = theta / delta
    rho = 1.0 / sigma
    solution = jnp.zeros_like(rhs_c)
    remain = rhs_c
    direction = remain / (diag * theta)
    for step in range(CHEB):
        solution = solution + direction
        if step + 1 < CHEB:
            remain = remain - stencil(direction, padder(direction), coefs)
            rho_next = 1.0 / (2.0 * sigma - rho)
            direction = rho_next * rho * direction + (2.0 * rho_next / delta) * remain / diag
            rho = rho_next
    return solution


def zero_pad(field):
    return jnp.pad(field, 1)


def reference(right_side, inv_density, pressure):
    coefs = face_coefs(inv_density, zero_pad(inv_density))
    diag = sum(coefs)
    fine = pressure
    for sweep in range(SWEEPS):
        fine = fine + (2.0 / 3.0) * (right_side - stencil(fine, zero_pad(fine), coefs)) / diag
    res = right_side - stencil(fine, zero_pad(fine), coefs)
    coarse_rhs = block_mean(res)
    coarse_b = block_mean(inv_density)
    coarse_coefs = [c * 0.0625 for c in face_coefs(coarse_b, zero_pad(coarse_b))]
    coarse_diag = sum(coarse_coefs)
    corr = chebyshev(coarse_rhs, coarse_coefs, coarse_diag, zero_pad)
    expanded = jnp.repeat(jnp.repeat(jnp.repeat(corr, 4, axis=0), 4, axis=1), 4, axis=2)
    return fine + expanded
```

```python
import jax
import jax.numpy as jnp
from jax import lax
from jax.sharding import PartitionSpec as P

SWEEPS = 2
CHEB = 8
HIGHEST = lax.Precision.HIGHEST


def shifted_pairs(count, hop):
    return [(i, i + hop) for i in range(count - hop)]


def halo_from(block, axis, dim, width, hop):
    count = lax.axis_size(axis)
    n = block.shape[dim]
    if hop >= count:
        shape = list(block.shape)
        shape[dim] = width
        zeros = jnp.zeros(shape, block.dtype)
        return zeros, zeros
    forward = shifted_pairs(count, hop)
    backward = [(t, s) for s, t in forward]
    low = lax.ppermute(lax.slice_in_dim(block, n - width, n, axis=dim), axis, forward)
    high = lax.ppermute(lax.slice_in_dim(block, 0, width, axis=dim), axis, backward)
    return low, high


def deep_extend(block, axis, dim, depth):
    n = block.shape[dim]
    lows, highs = [], []
    need, hop = depth, 1
    while need > 0:
        width = min(n, need)
        low, high = halo_from(block, axis, dim, width, hop)
        lows.insert(0, low)
        highs.append(high)
        need -= width
        hop += 1
    return jnp.concatenate(lows + [block] + highs, axis=dim)


def shift_z(field, side):
    zeros = jnp.zeros_like(field[:, :, :1])
    if side < 0:
        return jnp.concatenate([zeros, field[:, :, :-1]], axis=2)
    return jnp.concatenate([field[:, :, 1:], zeros], axis=2)


def fine_neighbours(field):
    xl, xh = halo_from(field, "box", 0, 1, 1)
    yl, yh = halo_from(field, "group", 1, 1, 1)
    return [
        jnp.concatenate([xl, field[:-1]], axis=0),
        jnp.concatenate([field[1:], xh], axis=0),
        jnp.concatenate([yl, field[:, :-1]], axis=1),
        jnp.concatenate([field[:, 1:], yh], axis=1),
        shift_z(field, -1),
        shift_z(field, 1),
    ]


def padded_neighbours(padded):
    return [
        padded[:-2, 1:-1, 1:-1],
        padded[2:, 1:-1, 1:-1],
        padded[1:-1, :-2, 1:-1],
        padded[1:-1, 2:, 1:-1],
        padded[1:-1, 1:-1, :-2],
        padded[1:-1, 1:-1, 2:],
    ]


def coefs_of(field, nears):
    return [jnp.where(near > 0, 2.0 * field * near / (field + near), field) for near in nears]


def apply_op(field, nears, coefs):
    total = jnp.zeros_like(field)
    for coef, near in zip(coefs, nears):
        total = total + coef * (field - near)
    return total


def group_matrix(n, k):
    rows = lax.broadcasted_iota(jnp.int32, (n, n // k), 0) // k
    cols = lax.broadcasted_iota(jnp.int32, (n, n // k), 1)
    return (rows == cols).astype(jnp.float32)


def block_mean(field):
    sx, sy, sz = field.shape
    fx = field.reshape(sx // 4, 4, sy, sz).sum(axis=1)
    fz = jnp.einsum("xyz,zc->xyc", fx, group_matrix(sz, 4), precision=HIGHEST)
    fy = jnp.einsum("xyc,yb->xbc", fz, group_matrix(sy, 4), precision=HIGHEST)
    return fy * (1.0 / 64.0)


def expand(coarse, shape):
    sx, sy, sz = shape
    cz = jnp.einsum("xbc,zc->xbz", coarse, group_matrix(sz, 4), precision=HIGHEST)
    cy = jnp.einsum("xbz,yb->xyz", cz, group_matrix(sy, 4), precision=HIGHEST)
    return jnp.broadcast_to(cy[:, None], (sx // 4, 4, sy, sz)).reshape(sx, sy, sz)


def inside_mask(shape, depth, totals):
    ex, ey, ez = shape
    cx, cy = ex - 2 * depth, ey - 2 * depth
    gx = lax.axis_index("box") * cx - depth + lax.broadcasted_iota(jnp.int32, shape, 0)
    gy = lax.axis_index("group") * cy - depth + lax.broadcasted_iota(jnp.int32, shape, 1)
    return (gx >= 0) & (gx < totals[0]) & (gy >= 0) & (gy < totals[1])


def chebyshev_local(rhs_c, b_c):
    depth = CHEB
    cx, cy, cz = rhs_c.shape
    both = jnp.stack([b_c, rhs_c])
    both = deep_extend(both, "box", 1, depth)
    both = deep_extend(both, "group", 2, depth)
    b_ext, rhs_ext = both[0], both[1]
    totals = (cx * lax.axis_size("box"), cy * lax.axis_size("group"))
    inside = inside_mask(b_ext.shape, depth, totals)
    coefs = [c * 0.0625 for c in coefs_of(b_ext, padded_neighbours(jnp.pad(b_ext, 1)))]
    diag = sum(coefs)
    inv_diag = jnp.where(inside, 1.0 / jnp.where(inside, diag, 1.0), 0.0)

    low, high = (0.05, 2.0)
    theta = (high + low) / 2.0
    delta = (high - low) / 2.0
    sigma = theta / delta
    rho = 1.0 / sigma
    solution = jnp.zeros_like(rhs_ext)
    remain = jnp.where(inside, rhs_ext, 0.0)
    direction = remain * inv_diag / theta
    for step in range(CHEB):
        solution = solution + direction
        if step + 1 < CHEB:
            nears = padded_neighbours(jnp.pad(direction, 1))
            remain = remain - apply_op(direction, nears, coefs)
            rho_next = 1.0 / (2.0 * sigma - rho)
            direction = rho_next * rho * direction + 2.0 * rho_next / delta * remain * inv_diag
            rho = rho_next
    return solution[depth:depth + cx, depth:depth + cy]


def per_device(right_side, inv_density, pressure):
    coefs = coefs_of(inv_density, fine_neighbours(inv_density))
    diag = sum(coefs)
    fine = pressure
    for sweep in range(SWEEPS):
        fine = fine + 2.0 / 3.0 * (right_side - apply_op(fine, fine_neighbours(fine), coefs)) / diag
    res = right_side - apply_op(fine, fine_neighbours(fine), coefs)
    coarse_rhs = block_mean(res)
    coarse_b = block_mean(inv_density)
    corr = chebyshev_local(coarse_rhs, coarse_b)
    return fine + expand(corr, fine.shape)


def solution(mesh):
    return jax.shard_map(
        per_device,
        mesh=mesh,
        in_specs=(P("box", "group", None), P("box", "group", None), P("box", "group", None)),
        out_specs=P("box", "group", None),
        check_vma=False,
    )
```

```python
import jax
import jax.numpy as jnp
from jax import lax
from jax.sharding import PartitionSpec as P

SWEEPS = 2
CHEB = 8
HIGHEST = lax.Precision.HIGHEST


def shifted_pairs(count, hop):
    return [(i, i + hop) for i in range(count - hop)]


def halo_from(block, axis, dim, width, hop):
    count = lax.axis_size(axis)
    n = block.shape[dim]
    if hop >= count:
        shape = list(block.shape)
        shape[dim] = width
        zeros = jnp.zeros(shape, block.dtype)
        return zeros, zeros
    forward = shifted_pairs(count, hop)
    backward = [(t, s) for s, t in forward]
    low = lax.ppermute(lax.slice_in_dim(block, n - width, n, axis=dim), axis, forward)
    high = lax.ppermute(lax.slice_in_dim(block, 0, width, axis=dim), axis, backward)
    return low, high


def deep_extend(block, axis, dim, depth):
    n = block.shape[dim]
    lows, highs = [], []
    need, hop = depth, 1
    while need > 0:
        width = min(n, need)
        low, high = halo_from(block, axis, dim, width, hop)
        lows.insert(0, low)
        highs.append(high)
        need -= width
        hop += 1
    return jnp.concatenate(lows + [block] + highs, axis=dim)


def shift_z(field, side):
    zeros = jnp.zeros_like(field[:, :, :1])
    if side < 0:
        return jnp.concatenate([zeros, field[:, :, :-1]], axis=2)
    return jnp.concatenate([field[:, :, 1:], zeros], axis=2)


def fine_neighbours(field):
    xl, xh = halo_from(field, "box", 0, 1, 1)
    yl, yh = halo_from(field, "group", 1, 1, 1)
    return [
        jnp.concatenate([xl, field[:-1]], axis=0),
        jnp.concatenate([field[1:], xh], axis=0),
        jnp.concatenate([yl, field[:, :-1]], axis=1),
        jnp.concatenate([field[:, 1:], yh], axis=1),
        shift_z(field, -1),
        shift_z(field, 1),
    ]


def padded_neighbours(padded):
    return [
        padded[:-2, 1:-1, 1:-1],
        padded[2:, 1:-1, 1:-1],
        padded[1:-1, :-2, 1:-1],
        padded[1:-1, 2:, 1:-1],
        padded[1:-1, 1:-1, :-2],
        padded[1:-1, 1:-1, 2:],
    ]


def coefs_of(field, nears):
    return [jnp.where(near > 0, 2.0 * field * near / (field + near), field) for near in nears]


def apply_op(field, nears, coefs):
    total = jnp.zeros_like(field)
    for coef, near in zip(coefs, nears):
        total = total + coef * (field - near)
    return total


def group_matrix(n, k):
    rows = lax.broadcasted_iota(jnp.int32, (n, n // k), 0) // k
    cols = lax.broadcasted_iota(jnp.int32, (n, n // k), 1)
    return (rows == cols).astype(jnp.float32)


def block_mean(field):
    sx, sy, sz = field.shape
    fx = field.reshape(sx // 4, 4, sy, sz).sum(axis=1)
    fz = jnp.einsum("xyz,zc->xyc", fx, group_matrix(sz, 4), precision=HIGHEST)
    fy = jnp.einsum("xyc,yb->xbc", fz, group_matrix(sy, 4), precision=HIGHEST)
    return fy * (1.0 / 64.0)


def expand(coarse, shape):
    sx, sy, sz = shape
    cz = jnp.einsum("xbc,zc->xbz", coarse, group_matrix(sz, 4), precision=HIGHEST)
    cy = jnp.einsum("xbz,yb->xyz", cz, group_matrix(sy, 4), precision=HIGHEST)
    return jnp.broadcast_to(cy[:, None], (sx // 4, 4, sy, sz)).reshape(sx, sy, sz)


def inside_mask(shape, depth, totals):
    ex, ey, ez = shape
    cx, cy = ex - 2 * depth, ey - 2 * depth
    gx = lax.axis_index("box") * cx - depth + lax.broadcasted_iota(jnp.int32, shape, 0)
    gy = lax.axis_index("group") * cy - depth + lax.broadcasted_iota(jnp.int32, shape, 1)
    return (gx >= 0) & (gx < totals[0]) & (gy >= 0) & (gy < totals[1])


def chebyshev_local(rhs_c, b_c):
    depth = CHEB
    cx, cy, cz = rhs_c.shape
    both = jnp.stack([b_c, rhs_c])
    both = deep_extend(both, "box", 1, depth)
    both = deep_extend(both, "group", 2, depth)
    b_ext, rhs_ext = both[0], both[1]
    totals = (cx * lax.axis_size("box"), cy * lax.axis_size("group"))
    inside = inside_mask(b_ext.shape, depth, totals)
    coefs = [c * 0.0625 for c in coefs_of(b_ext, padded_neighbours(jnp.pad(b_ext, 1)))]
    diag = sum(coefs)
    inv_diag = jnp.where(inside, 1.0 / jnp.where(inside, diag, 1.0), 0.0)

    low, high = (0.05, 2.0)
    theta = (high + low) / 2.0
    delta = (high - low) / 2.0
    sigma = theta / delta
    rho = 1.0 / sigma
    solution = jnp.zeros_like(rhs_ext)
    remain = jnp.where(inside, rhs_ext, 0.0)
    direction = remain * inv_diag / theta
    for step in range(CHEB):
        solution = solution + direction
        if step + 1 < CHEB:
            nears = padded_neighbours(jnp.pad(direction, 1))
            remain = remain - apply_op(direction, nears, coefs)
            rho_next = 1.0 / (2.0 * sigma - rho)
            direction = rho_next * rho * direction + 2.0 * rho_next / delta * remain * inv_diag
            rho = rho_next
    return solution[depth:depth + cx, depth:depth + cy]


def grid_mask(shape, depth, axes, totals):
    inside = None
    for dim, (axis, total) in enumerate(zip(axes, totals)):
        own = shape[dim] - 2 * depth
        g = lax.axis_index(axis) * own - depth + lax.broadcasted_iota(jnp.int32, shape, dim)
        ok = (g >= 0) & (g < total)
        inside = ok if inside is None else inside & ok
    return inside


def per_device(right_side, inv_density, pressure):
    depth = SWEEPS + 1
    sx, sy, sz = pressure.shape
    both = jnp.stack([right_side, inv_density, pressure])
    both = deep_extend(both, "box", 1, depth)
    both = deep_extend(both, "group", 2, depth)
    rhs_e, b_e, fine = both[0], both[1], both[2]
    totals = (sx * lax.axis_size("box"), sy * lax.axis_size("group"))
    inside = grid_mask(fine.shape, depth, ("box", "group"), totals)
    coefs = coefs_of(b_e, padded_neighbours(jnp.pad(b_e, 1)))
    diag = sum(coefs)
    for sweep in range(SWEEPS):
        step = 2.0 / 3.0 * (rhs_e - apply_op(fine, padded_neighbours(jnp.pad(fine, 1)), coefs)) / diag
        fine = jnp.where(inside, fine + step, 0.0)
    res = rhs_e - apply_op(fine, padded_neighbours(jnp.pad(fine, 1)), coefs)
    own = (slice(depth, depth + sx), slice(depth, depth + sy))
    fine, res = fine[own], res[own]
    coarse_rhs = block_mean(res)
    coarse_b = block_mean(inv_density)
    corr = chebyshev_local(coarse_rhs, coarse_b)
    return fine + expand(corr, fine.shape)


def solution(mesh):
    return jax.shard_map(
        per_device,
        mesh=mesh,
        in_specs=(P("box", "group", None), P("box", "group", None), P("box", "group", None)),
        out_specs=P("box", "group", None),
        check_vma=False,
    )
```

```python
import jax
import jax.numpy as jnp
from jax import lax
from jax.sharding import PartitionSpec as P

SWEEPS = 2
CHEB = 8
HIGHEST = lax.Precision.HIGHEST


def shifted_pairs(count, hop):
    return [(i, i + hop) for i in range(count - hop)]


def halo_from(block, axis, dim, width, hop):
    count = lax.axis_size(axis)
    n = block.shape[dim]
    if hop >= count:
        shape = list(block.shape)
        shape[dim] = width
        zeros = jnp.zeros(shape, block.dtype)
        return zeros, zeros
    forward = shifted_pairs(count, hop)
    backward = [(t, s) for s, t in forward]
    low = lax.ppermute(lax.slice_in_dim(block, n - width, n, axis=dim), axis, forward)
    high = lax.ppermute(lax.slice_in_dim(block, 0, width, axis=dim), axis, backward)
    return low, high


def deep_extend(block, axis, dim, depth):
    n = block.shape[dim]
    lows, highs = [], []
    need, hop = depth, 1
    while need > 0:
        width = min(n, need)
        low, high = halo_from(block, axis, dim, width, hop)
        lows.insert(0, low)
        highs.append(high)
        need -= width
        hop += 1
    return jnp.concatenate(lows + [block] + highs, axis=dim)


def shift_z(field, side):
    zeros = jnp.zeros_like(field[:, :, :1])
    if side < 0:
        return jnp.concatenate([zeros, field[:, :, :-1]], axis=2)
    return jnp.concatenate([field[:, :, 1:], zeros], axis=2)


def padded_neighbours(padded):
    return [
        padded[:-2, 1:-1, 1:-1],
        padded[2:, 1:-1, 1:-1],
        padded[1:-1, :-2, 1:-1],
        padded[1:-1, 2:, 1:-1],
        padded[1:-1, 1:-1, :-2],
        padded[1:-1, 1:-1, 2:],
    ]


def coefs_of(field, nears):
    return [jnp.where(near > 0, 2.0 * field * near / (field + near), field) for near in nears]


def apply_op(field, nears, coefs):
    total = jnp.zeros_like(field)
    for coef, near in zip(coefs, nears):
        total = total + coef * (field - near)
    return total


def group_matrix(n, k):
    rows = lax.broadcasted_iota(jnp.int32, (n, n // k), 0) // k
    cols = lax.broadcasted_iota(jnp.int32, (n, n // k), 1)
    return (rows == cols).astype(jnp.float32)


def block_mean(field):
    sx, sy, sz = field.shape
    fx = field.reshape(sx // 4, 4, sy, sz).sum(axis=1)
    fz = jnp.einsum("xyz,zc->xyc", fx, group_matrix(sz, 4), precision=HIGHEST)
    fy = jnp.einsum("xyc,yb->xbc", fz, group_matrix(sy, 4), precision=HIGHEST)
    return fy * (1.0 / 64.0)


def expand(coarse, shape):
    sx, sy, sz = shape
    cz = jnp.einsum("xbc,zc->xbz", coarse, group_matrix(sz, 4), precision=HIGHEST)
    cy = jnp.einsum("xbz,yb->xyz", cz, group_matrix(sy, 4), precision=HIGHEST)
    return jnp.broadcast_to(cy[:, None], (sx // 4, 4, sy, sz)).reshape(sx, sy, sz)


def inside_mask(shape, depth, totals):
    ex, ey, ez = shape
    cx, cy = ex - 2 * depth, ey - 2 * depth
    gx = lax.axis_index("box") * cx - depth + lax.broadcasted_iota(jnp.int32, shape, 0)
    gy = lax.axis_index("group") * cy - depth + lax.broadcasted_iota(jnp.int32, shape, 1)
    return (gx >= 0) & (gx < totals[0]) & (gy >= 0) & (gy < totals[1])


def chebyshev_local(rhs_c, b_c):
    depth = CHEB
    cx, cy, cz = rhs_c.shape
    both = jnp.stack([b_c, rhs_c])
    both = deep_extend(both, "box", 1, depth)
    both = deep_extend(both, "group", 2, depth)
    b_ext, rhs_ext = both[0], both[1]
    totals = (cx * lax.axis_size("box"), cy * lax.axis_size("group"))
    inside = inside_mask(b_ext.shape, depth, totals)
    coefs = [c * 0.0625 for c in coefs_of(b_ext, padded_neighbours(jnp.pad(b_ext, 1)))]
    diag = sum(coefs)
    inv_diag = jnp.where(inside, 1.0 / jnp.where(inside, diag, 1.0), 0.0)

    low, high = (0.05, 2.0)
    theta = (high + low) / 2.0
    delta = (high - low) / 2.0
    sigma = theta / delta
    rho = 1.0 / sigma
    solution = jnp.zeros_like(rhs_ext)
    remain = jnp.where(inside, rhs_ext, 0.0)
    direction = remain * inv_diag / theta
    for step in range(CHEB):
        solution = solution + direction
        if step + 1 < CHEB:
            nears = padded_neighbours(jnp.pad(direction, 1))
            remain = remain - apply_op(direction, nears, coefs)
            rho_next = 1.0 / (2.0 * sigma - rho)
            direction = rho_next * rho * direction + 2.0 * rho_next / delta * remain * inv_diag
            rho = rho_next
    return solution[depth:depth + cx, depth:depth + cy]


def grid_mask(shape, depth, axes, totals):
    inside = None
    for dim, (axis, total) in enumerate(zip(axes, totals)):
        own = shape[dim] - 2 * depth
        g = lax.axis_index(axis) * own - depth + lax.broadcasted_iota(jnp.int32, shape, dim)
        ok = (g >= 0) & (g < total)
        inside = ok if inside is None else inside & ok
    return inside


def shift_both(block, dx, dy):
    nb, ng = lax.axis_size("box"), lax.axis_size("group")
    pairs = [
        (i * ng + j, (i + dx) * ng + (j + dy))
        for i in range(nb)
        for j in range(ng)
        if 0 <= i + dx < nb and 0 <= j + dy < ng
    ]
    if not pairs:
        return jnp.zeros_like(block)
    return lax.ppermute(block, ("box", "group"), pairs)


def halo_ring(block, depth):
    sx, sy = block.shape[1], block.shape[2]
    parts = {
        -1: slice(0, depth),
        0: slice(0, sx),
        1: slice(sx - depth, sx),
    }
    parts_y = {
        -1: slice(0, depth),
        0: slice(0, sy),
        1: slice(sy - depth, sy),
    }
    rows = []
    for ox in (-1, 0, 1):
        row = []
        for oy in (-1, 0, 1):
            if ox == 0 and oy == 0:
                row.append(block)
                continue
            piece = block[:, parts[-ox], parts_y[-oy]]
            row.append(shift_both(piece, -ox, -oy))
        rows.append(jnp.concatenate(row, axis=2))
    return jnp.concatenate(rows, axis=1)


def low_faces(b):
    faces = []
    for dim in range(3):
        n = b.shape[dim]
        lo = lax.slice_in_dim(b, 0, n - 1, axis=dim)
        hi = lax.slice_in_dim(b, 1, n, axis=dim)
        inner = jnp.where((lo > 0) & (hi > 0), 2.0 * hi * lo / (hi + lo), hi + lo)
        faces.append(jnp.concatenate([lax.slice_in_dim(b, 0, 1, axis=dim), inner], axis=dim))
    return faces


def face_pairs(b, faces):
    pairs = []
    for dim, lo in enumerate(faces):
        n = b.shape[dim]
        hi = jnp.concatenate(
            [lax.slice_in_dim(lo, 1, n, axis=dim), lax.slice_in_dim(b, n - 1, n, axis=dim)], axis=dim
        )
        pairs += [lo, hi]
    return pairs


def per_device(right_side, inv_density, pressure):
    depth = SWEEPS + 1
    sx, sy, sz = pressure.shape
    both = halo_ring(jnp.stack([right_side, inv_density, pressure]), depth)
    rhs_e, b_e, fine = both[0], both[1], both[2]
    totals = (sx * lax.axis_size("box"), sy * lax.axis_size("group"))
    inside = grid_mask(fine.shape, depth, ("box", "group"), totals)
    coefs = face_pairs(b_e, low_faces(b_e))
    diag = sum(coefs)
    for sweep in range(SWEEPS):
        step = 2.0 / 3.0 * (rhs_e - apply_op(fine, padded_neighbours(jnp.pad(fine, 1)), coefs)) / diag
        fine = jnp.where(inside, fine + step, 0.0)
    res = rhs_e - apply_op(fine, padded_neighbours(jnp.pad(fine, 1)), coefs)
    own = (slice(depth, depth + sx), slice(depth, depth + sy))
    fine, res = fine[own], res[own]
    coarse_rhs = block_mean(res)
    coarse_b = block_mean(inv_density)
    corr = chebyshev_local(coarse_rhs, coarse_b)
    return fine + expand(corr, fine.shape)


def solution(mesh):
    return jax.shard_map(
        per_device,
        mesh=mesh,
        in_specs=(P("box", "group", None), P("box", "group", None), P("box", "group", None)),
        out_specs=P("box", "group", None),
        check_vma=False,
    )
```

```python
import jax
import jax.numpy as jnp
from jax import lax
from jax.sharding import PartitionSpec as P

SWEEPS = 2
CHEB = 8
HIGHEST = lax.Precision.HIGHEST


def shifted_pairs(count, hop):
    return [(i, i + hop) for i in range(count - hop)]


def halo_from(block, axis, dim, width, hop):
    count = lax.axis_size(axis)
    n = block.shape[dim]
    if hop >= count:
        shape = list(block.shape)
        shape[dim] = width
        zeros = jnp.zeros(shape, block.dtype)
        return zeros, zeros
    forward = shifted_pairs(count, hop)
    backward = [(t, s) for s, t in forward]
    low = lax.ppermute(lax.slice_in_dim(block, n - width, n, axis=dim), axis, forward)
    high = lax.ppermute(lax.slice_in_dim(block, 0, width, axis=dim), axis, backward)
    return low, high


def deep_extend(block, axis, dim, depth):
    n = block.shape[dim]
    lows, highs = [], []
    need, hop = depth, 1
    while need > 0:
        width = min(n, need)
        low, high = halo_from(block, axis, dim, width, hop)
        lows.insert(0, low)
        highs.append(high)
        need -= width
        hop += 1
    return jnp.concatenate(lows + [block] + highs, axis=dim)


def shift_z(field, side):
    zeros = jnp.zeros_like(field[:, :, :1])
    if side < 0:
        return jnp.concatenate([zeros, field[:, :, :-1]], axis=2)
    return jnp.concatenate([field[:, :, 1:], zeros], axis=2)


def padded_neighbours(padded):
    return [
        padded[:-2, 1:-1, 1:-1],
        padded[2:, 1:-1, 1:-1],
        padded[1:-1, :-2, 1:-1],
        padded[1:-1, 2:, 1:-1],
        padded[1:-1, 1:-1, :-2],
        padded[1:-1, 1:-1, 2:],
    ]


def coefs_of(field, nears):
    return [jnp.where(near > 0, 2.0 * field * near / (field + near), field) for near in nears]


def apply_op(field, nears, coefs):
    total = jnp.zeros_like(field)
    for coef, near in zip(coefs, nears):
        total = total + coef * (field - near)
    return total


def group_matrix(n, k):
    rows = lax.broadcasted_iota(jnp.int32, (n, n // k), 0) // k
    cols = lax.broadcasted_iota(jnp.int32, (n, n // k), 1)
    return (rows == cols).astype(jnp.float32)


def block_mean(field):
    sx, sy, sz = field.shape
    fx = field.reshape(sx // 4, 4, sy, sz).sum(axis=1)
    fz = jnp.einsum("xyz,zc->xyc", fx, group_matrix(sz, 4), precision=HIGHEST)
    fy = jnp.einsum("xyc,yb->xbc", fz, group_matrix(sy, 4), precision=HIGHEST)
    return fy * (1.0 / 64.0)


def expand(coarse, shape):
    sx, sy, sz = shape
    cz = jnp.einsum("xbc,zc->xbz", coarse, group_matrix(sz, 4), precision=HIGHEST)
    cy = jnp.einsum("xbz,yb->xyz", cz, group_matrix(sy, 4), precision=HIGHEST)
    return jnp.broadcast_to(cy[:, None], (sx // 4, 4, sy, sz)).reshape(sx, sy, sz)


def inside_mask(shape, depth, totals):
    ex, ey, ez = shape
    cx, cy = ex - 2 * depth, ey - 2 * depth
    gx = lax.axis_index("box") * cx - depth + lax.broadcasted_iota(jnp.int32, shape, 0)
    gy = lax.axis_index("group") * cy - depth + lax.broadcasted_iota(jnp.int32, shape, 1)
    return (gx >= 0) & (gx < totals[0]) & (gy >= 0) & (gy < totals[1])


def chebyshev_local(rhs_c, b_c):
    depth = CHEB
    cx, cy, cz = rhs_c.shape
    both = jnp.stack([b_c, rhs_c])
    both = deep_extend(both, "box", 1, depth)
    both = deep_extend(both, "group", 2, depth)
    b_ext, rhs_ext = both[0], both[1]
    totals = (cx * lax.axis_size("box"), cy * lax.axis_size("group"))
    inside = inside_mask(b_ext.shape, depth, totals)
    coefs = [c * 0.0625 for c in coefs_of(b_ext, padded_neighbours(jnp.pad(b_ext, 1)))]
    diag = sum(coefs)
    inv_diag = jnp.where(inside, 1.0 / jnp.where(inside, diag, 1.0), 0.0)

    low, high = (0.05, 2.0)
    theta = (high + low) / 2.0
    delta = (high - low) / 2.0
    sigma = theta / delta
    rho = 1.0 / sigma
    solution = jnp.zeros_like(rhs_ext)
    remain = jnp.where(inside, rhs_ext, 0.0)
    direction = remain * inv_diag / theta
    for step in range(CHEB):
        solution = solution + direction
        if step + 1 < CHEB:
            nears = padded_neighbours(jnp.pad(direction, 1))
            remain = remain - apply_op(direction, nears, coefs)
            rho_next = 1.0 / (2.0 * sigma - rho)
            direction = rho_next * rho * direction + 2.0 * rho_next / delta * remain * inv_diag
            rho = rho_next
    return solution[depth:depth + cx, depth:depth + cy]


def grid_mask(shape, depth, axes, totals):
    inside = None
    for dim, (axis, total) in enumerate(zip(axes, totals)):
        own = shape[dim] - 2 * depth
        g = lax.axis_index(axis) * own - depth + lax.broadcasted_iota(jnp.int32, shape, dim)
        ok = (g >= 0) & (g < total)
        inside = ok if inside is None else inside & ok
    return inside


def low_faces(b):
    faces = []
    for dim in range(3):
        n = b.shape[dim]
        lo = lax.slice_in_dim(b, 0, n - 1, axis=dim)
        hi = lax.slice_in_dim(b, 1, n, axis=dim)
        inner = jnp.where((lo > 0) & (hi > 0), 2.0 * hi * lo / (hi + lo), hi + lo)
        faces.append(jnp.concatenate([lax.slice_in_dim(b, 0, 1, axis=dim), inner], axis=dim))
    return faces


def face_pairs(b, faces):
    pairs = []
    for dim, lo in enumerate(faces):
        n = b.shape[dim]
        hi = jnp.concatenate(
            [lax.slice_in_dim(lo, 1, n, axis=dim), lax.slice_in_dim(b, n - 1, n, axis=dim)], axis=dim
        )
        pairs += [lo, hi]
    return pairs


def per_device(right_side, inv_density, pressure):
    depth = SWEEPS + 1
    sx, sy, sz = pressure.shape
    both = jnp.stack([right_side, inv_density, pressure])
    both = deep_extend(deep_extend(both, "box", 1, depth), "group", 2, depth)
    rhs_e, b_e, fine = both[0], both[1], both[2]
    totals = (sx * lax.axis_size("box"), sy * lax.axis_size("group"))
    inside = grid_mask(fine.shape, depth, ("box", "group"), totals)
    coefs = face_pairs(b_e, low_faces(b_e))
    diag = sum(coefs)
    for sweep in range(SWEEPS):
        step = 2.0 / 3.0 * (rhs_e - apply_op(fine, padded_neighbours(jnp.pad(fine, 1)), coefs)) / diag
        fine = jnp.where(inside, fine + step, 0.0)
    res = rhs_e - apply_op(fine, padded_neighbours(jnp.pad(fine, 1)), coefs)
    own = (slice(depth, depth + sx), slice(depth, depth + sy))
    fine, res = fine[own], res[own]
    coarse_rhs = block_mean(res)
    coarse_b = block_mean(inv_density)
    corr = chebyshev_local(coarse_rhs, coarse_b)
    return fine + expand(corr, fine.shape)


def solution(mesh):
    return jax.shard_map(
        per_device,
        mesh=mesh,
        in_specs=(P("box", "group", None), P("box", "group", None), P("box", "group", None)),
        out_specs=P("box", "group", None),
        check_vma=False,
    )
```

```python
import jax
import jax.numpy as jnp
from jax import lax
from jax.sharding import PartitionSpec as P

SWEEPS = 2
CHEB = 8
HIGHEST = lax.Precision.HIGHEST


def shifted_pairs(count, hop):
    return [(i, i + hop) for i in range(count - hop)]


def halo_from(block, axis, dim, width, hop):
    count = lax.axis_size(axis)
    n = block.shape[dim]
    if hop >= count:
        shape = list(block.shape)
        shape[dim] = width
        zeros = jnp.zeros(shape, block.dtype)
        return zeros, zeros
    forward = shifted_pairs(count, hop)
    backward = [(t, s) for s, t in forward]
    low = lax.ppermute(lax.slice_in_dim(block, n - width, n, axis=dim), axis, forward)
    high = lax.ppermute(lax.slice_in_dim(block, 0, width, axis=dim), axis, backward)
    return low, high


def deep_extend(block, axis, dim, depth):
    n = block.shape[dim]
    lows, highs = [], []
    need, hop = depth, 1
    while need > 0:
        width = min(n, need)
        low, high = halo_from(block, axis, dim, width, hop)
        lows.insert(0, low)
        highs.append(high)
        need -= width
        hop += 1
    return jnp.concatenate(lows + [block] + highs, axis=dim)


def halo_with_corners(block, depth):
    assert depth <= block.shape[1] and depth <= block.shape[2]
    xl, xh = halo_from(block, "box", 1, depth, 1)
    yl, yh = halo_from(block, "group", 2, depth, 1)
    sides = jnp.concatenate([yl, yh], axis=2)
    low, high = halo_from(sides, "box", 1, depth, 1)
    low_l, low_h = low[:, :, :depth], low[:, :, depth:]
    high_l, high_h = high[:, :, :depth], high[:, :, depth:]
    rows = [
        jnp.concatenate([low_l, xl, low_h], axis=2),
        jnp.concatenate([yl, block, yh], axis=2),
        jnp.concatenate([high_l, xh, high_h], axis=2),
    ]
    return jnp.concatenate(rows, axis=1)


def shift_z(field, side):
    zeros = jnp.zeros_like(field[:, :, :1])
    if side < 0:
        return jnp.concatenate([zeros, field[:, :, :-1]], axis=2)
    return jnp.concatenate([field[:, :, 1:], zeros], axis=2)


def padded_neighbours(padded):
    return [
        padded[:-2, 1:-1, 1:-1],
        padded[2:, 1:-1, 1:-1],
        padded[1:-1, :-2, 1:-1],
        padded[1:-1, 2:, 1:-1],
        padded[1:-1, 1:-1, :-2],
        padded[1:-1, 1:-1, 2:],
    ]


def coefs_of(field, nears):
    return [jnp.where(near > 0, 2.0 * field * near / (field + near), field) for near in nears]


def apply_op(field, nears, coefs):
    total = jnp.zeros_like(field)
    for coef, near in zip(coefs, nears):
        total = total + coef * (field - near)
    return total


def group_matrix(n, k):
    rows = lax.broadcasted_iota(jnp.int32, (n, n // k), 0) // k
    cols = lax.broadcasted_iota(jnp.int32, (n, n // k), 1)
    return (rows == cols).astype(jnp.float32)


def block_mean(field):
    sx, sy, sz = field.shape
    fx = field.reshape(sx // 4, 4, sy, sz).sum(axis=1)
    fz = jnp.einsum("xyz,zc->xyc", fx, group_matrix(sz, 4), precision=HIGHEST)
    fy = jnp.einsum("xyc,yb->xbc", fz, group_matrix(sy, 4), precision=HIGHEST)
    return fy * (1.0 / 64.0)


def expand(coarse, shape):
    sx, sy, sz = shape
    cz = jnp.einsum("xbc,zc->xbz", coarse, group_matrix(sz, 4), precision=HIGHEST)
    cy = jnp.einsum("xbz,yb->xyz", cz, group_matrix(sy, 4), precision=HIGHEST)
    return jnp.broadcast_to(cy[:, None], (sx // 4, 4, sy, sz)).reshape(sx, sy, sz)


def inside_mask(shape, depth, totals):
    ex, ey, ez = shape
    cx, cy = ex - 2 * depth, ey - 2 * depth
    gx = lax.axis_index("box") * cx - depth + lax.broadcasted_iota(jnp.int32, shape, 0)
    gy = lax.axis_index("group") * cy - depth + lax.broadcasted_iota(jnp.int32, shape, 1)
    return (gx >= 0) & (gx < totals[0]) & (gy >= 0) & (gy < totals[1])


def chebyshev_local(rhs_c, b_c):
    depth = CHEB
    cx, cy, cz = rhs_c.shape
    both = jnp.stack([b_c, rhs_c])
    both = deep_extend(both, "box", 1, depth)
    both = deep_extend(both, "group", 2, depth)
    b_ext, rhs_ext = both[0], both[1]
    totals = (cx * lax.axis_size("box"), cy * lax.axis_size("group"))
    inside = inside_mask(b_ext.shape, depth, totals)
    coefs = [c * 0.0625 for c in coefs_of(b_ext, padded_neighbours(jnp.pad(b_ext, 1)))]
    diag = sum(coefs)
    inv_diag = jnp.where(inside, 1.0 / jnp.where(inside, diag, 1.0), 0.0)

    low, high = (0.05, 2.0)
    theta = (high + low) / 2.0
    delta = (high - low) / 2.0
    sigma = theta / delta
    rho = 1.0 / sigma
    solution = jnp.zeros_like(rhs_ext)
    remain = jnp.where(inside, rhs_ext, 0.0)
    direction = remain * inv_diag / theta
    for step in range(CHEB):
        solution = solution + direction
        if step + 1 < CHEB:
            nears = padded_neighbours(jnp.pad(direction, 1))
            remain = remain - apply_op(direction, nears, coefs)
            rho_next = 1.0 / (2.0 * sigma - rho)
            direction = rho_next * rho * direction + 2.0 * rho_next / delta * remain * inv_diag
            rho = rho_next
    return solution[depth:depth + cx, depth:depth + cy]


def grid_mask(shape, depth, axes, totals):
    inside = None
    for dim, (axis, total) in enumerate(zip(axes, totals)):
        own = shape[dim] - 2 * depth
        g = lax.axis_index(axis) * own - depth + lax.broadcasted_iota(jnp.int32, shape, dim)
        ok = (g >= 0) & (g < total)
        inside = ok if inside is None else inside & ok
    return inside


def low_faces(b):
    faces = []
    for dim in range(3):
        n = b.shape[dim]
        lo = lax.slice_in_dim(b, 0, n - 1, axis=dim)
        hi = lax.slice_in_dim(b, 1, n, axis=dim)
        inner = jnp.where((lo > 0) & (hi > 0), 2.0 * hi * lo / (hi + lo), hi + lo)
        faces.append(jnp.concatenate([lax.slice_in_dim(b, 0, 1, axis=dim), inner], axis=dim))
    return faces


def face_pairs(b, faces):
    pairs = []
    for dim, lo in enumerate(faces):
        n = b.shape[dim]
        hi = jnp.concatenate(
            [lax.slice_in_dim(lo, 1, n, axis=dim), lax.slice_in_dim(b, n - 1, n, axis=dim)], axis=dim
        )
        pairs += [lo, hi]
    return pairs


def per_device(right_side, inv_density, pressure):
    depth = SWEEPS + 1
    sx, sy, sz = pressure.shape
    both = halo_with_corners(jnp.stack([right_side, inv_density, pressure]), depth)
    rhs_e, b_e, fine = both[0], both[1], both[2]
    totals = (sx * lax.axis_size("box"), sy * lax.axis_size("group"))
    inside = grid_mask(fine.shape, depth, ("box", "group"), totals)
    coefs = face_pairs(b_e, low_faces(b_e))
    diag = sum(coefs)
    for sweep in range(SWEEPS):
        step = 2.0 / 3.0 * (rhs_e - apply_op(fine, padded_neighbours(jnp.pad(fine, 1)), coefs)) / diag
        fine = jnp.where(inside, fine + step, 0.0)
    res = rhs_e - apply_op(fine, padded_neighbours(jnp.pad(fine, 1)), coefs)
    own = (slice(depth, depth + sx), slice(depth, depth + sy))
    fine, res = fine[own], res[own]
    coarse_rhs = block_mean(res)
    coarse_b = block_mean(inv_density)
    corr = chebyshev_local(coarse_rhs, coarse_b)
    return fine + expand(corr, fine.shape)


def solution(mesh):
    return jax.shard_map(
        per_device,
        mesh=mesh,
        in_specs=(P("box", "group", None), P("box", "group", None), P("box", "group", None)),
        out_specs=P("box", "group", None),
        check_vma=False,
    )
```

```python
import jax
import jax.numpy as jnp
from jax import lax
from jax.sharding import PartitionSpec as P

SWEEPS = 2
CHEB = 8
HIGHEST = lax.Precision.HIGHEST


def shifted_pairs(count, hop):
    return [(i, i + hop) for i in range(count - hop)]


def halo_from(block, axis, dim, width, hop):
    count = lax.axis_size(axis)
    n = block.shape[dim]
    if hop >= count:
        shape = list(block.shape)
        shape[dim] = width
        zeros = jnp.zeros(shape, block.dtype)
        return zeros, zeros
    forward = shifted_pairs(count, hop)
    backward = [(t, s) for s, t in forward]
    low = lax.ppermute(lax.slice_in_dim(block, n - width, n, axis=dim), axis, forward)
    high = lax.ppermute(lax.slice_in_dim(block, 0, width, axis=dim), axis, backward)
    return low, high


def deep_extend(block, axis, dim, depth):
    n = block.shape[dim]
    lows, highs = [], []
    need, hop = depth, 1
    while need > 0:
        width = min(n, need)
        low, high = halo_from(block, axis, dim, width, hop)
        lows.insert(0, low)
        highs.append(high)
        need -= width
        hop += 1
    return jnp.concatenate(lows + [block] + highs, axis=dim)


def packed_halo(fields, depths):
    top = max(depths)
    assert top <= fields[0].shape[0] and top <= fields[0].shape[1]
    offs = [sum(depths[:k]) for k in range(len(depths))]
    up = lambda f, d, dim: lax.slice_in_dim(f, f.shape[dim] - d, f.shape[dim], axis=dim)
    down = lambda f, d, dim: lax.slice_in_dim(f, 0, d, axis=dim)
    nb, ng = lax.axis_size("box"), lax.axis_size("group")
    fb, bb = shifted_pairs(nb, 1), [(t, s) for s, t in shifted_pairs(nb, 1)]
    fg, bg = shifted_pairs(ng, 1), [(t, s) for s, t in shifted_pairs(ng, 1)]

    def send(pieces, axis, pairs, dim):
        msg = jnp.concatenate(pieces, axis=dim)
        if not pairs:
            return jnp.zeros_like(msg)
        return lax.ppermute(msg, axis, pairs)

    xl = send([up(f, d, 0) for f, d in zip(fields, depths)], "box", fb, 0)
    xh = send([down(f, d, 0) for f, d in zip(fields, depths)], "box", bb, 0)
    yl = send([up(f, d, 1) for f, d in zip(fields, depths)], "group", fg, 1)
    yh = send([down(f, d, 1) for f, d in zip(fields, depths)], "group", bg, 1)
    width = yl.shape[1]
    low = send([up(yl, top, 0), up(yh, top, 0)], "box", fb, 1)
    high = send([down(yl, top, 0), down(yh, top, 0)], "box", bb, 1)
    out = []
    for f, d, o in zip(fields, depths, offs):
        ys = slice(o, o + d)
        ys2 = slice(width + o, width + o + d)
        rows = [
            jnp.concatenate([low[top - d:, ys], xl[o:o + d], low[top - d:, ys2]], axis=1),
            jnp.concatenate([yl[:, ys], f, yh[:, ys]], axis=1),
            jnp.concatenate([high[:d, ys], xh[o:o + d], high[:d, ys2]], axis=1),
        ]
        out.append(jnp.concatenate(rows, axis=0))
    return out


def shift_z(field, side):
    zeros = jnp.zeros_like(field[:, :, :1])
    if side < 0:
        return jnp.concatenate([zeros, field[:, :, :-1]], axis=2)
    return jnp.concatenate([field[:, :, 1:], zeros], axis=2)


def padded_neighbours(padded):
    return [
        padded[:-2, 1:-1, 1:-1],
        padded[2:, 1:-1, 1:-1],
        padded[1:-1, :-2, 1:-1],
        padded[1:-1, 2:, 1:-1],
        padded[1:-1, 1:-1, :-2],
        padded[1:-1, 1:-1, 2:],
    ]


def coefs_of(field, nears):
    return [jnp.where(near > 0, 2.0 * field * near / (field + near), field) for near in nears]


def apply_op(field, nears, coefs):
    total = jnp.zeros_like(field)
    for coef, near in zip(coefs, nears):
        total = total + coef * (field - near)
    return total


def group_matrix(n, k):
    rows = lax.broadcasted_iota(jnp.int32, (n, n // k), 0) // k
    cols = lax.broadcasted_iota(jnp.int32, (n, n // k), 1)
    return (rows == cols).astype(jnp.float32)


def block_mean(field):
    sx, sy, sz = field.shape
    fx = field.reshape(sx // 4, 4, sy, sz).sum(axis=1)
    fz = jnp.einsum("xyz,zc->xyc", fx, group_matrix(sz, 4), precision=HIGHEST)
    fy = jnp.einsum("xyc,yb->xbc", fz, group_matrix(sy, 4), precision=HIGHEST)
    return fy * (1.0 / 64.0)


def expand(coarse, shape):
    sx, sy, sz = shape
    cz = jnp.einsum("xbc,zc->xbz", coarse, group_matrix(sz, 4), precision=HIGHEST)
    cy = jnp.einsum("xbz,yb->xyz", cz, group_matrix(sy, 4), precision=HIGHEST)
    return jnp.broadcast_to(cy[:, None], (sx // 4, 4, sy, sz)).reshape(sx, sy, sz)


def inside_mask(shape, depth, totals):
    ex, ey, ez = shape
    cx, cy = ex - 2 * depth, ey - 2 * depth
    gx = lax.axis_index("box") * cx - depth + lax.broadcasted_iota(jnp.int32, shape, 0)
    gy = lax.axis_index("group") * cy - depth + lax.broadcasted_iota(jnp.int32, shape, 1)
    return (gx >= 0) & (gx < totals[0]) & (gy >= 0) & (gy < totals[1])


def chebyshev_local(rhs_c, b_c):
    depth = CHEB
    cx, cy, cz = rhs_c.shape
    both = jnp.stack([b_c, rhs_c])
    both = deep_extend(both, "box", 1, depth)
    both = deep_extend(both, "group", 2, depth)
    b_ext, rhs_ext = both[0], both[1]
    totals = (cx * lax.axis_size("box"), cy * lax.axis_size("group"))
    inside = inside_mask(b_ext.shape, depth, totals)
    coefs = [c * 0.0625 for c in coefs_of(b_ext, padded_neighbours(jnp.pad(b_ext, 1)))]
    diag = sum(coefs)
    inv_diag = jnp.where(inside, 1.0 / jnp.where(inside, diag, 1.0), 0.0)

    low, high = (0.05, 2.0)
    theta = (high + low) / 2.0
    delta = (high - low) / 2.0
    sigma = theta / delta
    rho = 1.0 / sigma
    solution = jnp.zeros_like(rhs_ext)
    remain = jnp.where(inside, rhs_ext, 0.0)
    direction = remain * inv_diag / theta
    for step in range(CHEB):
        solution = solution + direction
        if step + 1 < CHEB:
            nears = padded_neighbours(jnp.pad(direction, 1))
            remain = remain - apply_op(direction, nears, coefs)
            rho_next = 1.0 / (2.0 * sigma - rho)
            direction = rho_next * rho * direction + 2.0 * rho_next / delta * remain * inv_diag
            rho = rho_next
    return solution[depth:depth + cx, depth:depth + cy]


def grid_mask(shape, depth, axes, totals):
    inside = None
    for dim, (axis, total) in enumerate(zip(axes, totals)):
        own = shape[dim] - 2 * depth
        g = lax.axis_index(axis) * own - depth + lax.broadcasted_iota(jnp.int32, shape, dim)
        ok = (g >= 0) & (g < total)
        inside = ok if inside is None else inside & ok
    return inside


def low_faces(b):
    faces = []
    for dim in range(3):
        n = b.shape[dim]
        lo = lax.slice_in_dim(b, 0, n - 1, axis=dim)
        hi = lax.slice_in_dim(b, 1, n, axis=dim)
        inner = jnp.where((lo > 0) & (hi > 0), 2.0 * hi * lo / (hi + lo), hi + lo)
        faces.append(jnp.concatenate([lax.slice_in_dim(b, 0, 1, axis=dim), inner], axis=dim))
    return faces


def face_pairs(b, faces):
    pairs = []
    for dim, lo in enumerate(faces):
        n = b.shape[dim]
        hi = jnp.concatenate(
            [lax.slice_in_dim(lo, 1, n, axis=dim), lax.slice_in_dim(b, n - 1, n, axis=dim)], axis=dim
        )
        pairs += [lo, hi]
    return pairs


def per_device(right_side, inv_density, pressure):
    depth = SWEEPS + 1
    sx, sy, sz = pressure.shape
    rhs_e, b_e, fine = packed_halo([right_side, inv_density, pressure], [depth - 1, depth, depth])
    rhs_e = jnp.pad(rhs_e, ((1, 1), (1, 1), (0, 0)))
    totals = (sx * lax.axis_size("box"), sy * lax.axis_size("group"))
    inside = grid_mask(fine.shape, depth, ("box", "group"), totals)
    coefs = face_pairs(b_e, low_faces(b_e))
    diag = sum(coefs)
    for sweep in range(SWEEPS):
        step = 2.0 / 3.0 * (rhs_e - apply_op(fine, padded_neighbours(jnp.pad(fine, 1)), coefs)) / diag
        fine = jnp.where(inside, fine + step, 0.0)
    res = rhs_e - apply_op(fine, padded_neighbours(jnp.pad(fine, 1)), coefs)
    own = (slice(depth, depth + sx), slice(depth, depth + sy))
    fine, res = fine[own], res[own]
    coarse_rhs = block_mean(res)
    coarse_b = block_mean(inv_density)
    corr = chebyshev_local(coarse_rhs, coarse_b)
    return fine + expand(corr, fine.shape)


def solution(mesh):
    return jax.shard_map(
        per_device,
        mesh=mesh,
        in_specs=(P("box", "group", None), P("box", "group", None), P("box", "group", None)),
        out_specs=P("box", "group", None),
        check_vma=False,
    )
```

```python
import jax
import jax.numpy as jnp
from jax import lax
from jax.sharding import PartitionSpec as P

SWEEPS = 2
CHEB = 8
HIGHEST = lax.Precision.HIGHEST


def shifted_pairs(count, hop):
    return [(i, i + hop) for i in range(count - hop)]


def halo_from(block, axis, dim, width, hop):
    count = lax.axis_size(axis)
    n = block.shape[dim]
    if hop >= count:
        shape = list(block.shape)
        shape[dim] = width
        zeros = jnp.zeros(shape, block.dtype)
        return zeros, zeros
    forward = shifted_pairs(count, hop)
    backward = [(t, s) for s, t in forward]
    low = lax.ppermute(lax.slice_in_dim(block, n - width, n, axis=dim), axis, forward)
    high = lax.ppermute(lax.slice_in_dim(block, 0, width, axis=dim), axis, backward)
    return low, high


def deep_extend(block, axis, dim, depth):
    n = block.shape[dim]
    lows, highs = [], []
    need, hop = depth, 1
    while need > 0:
        width = min(n, need)
        low, high = halo_from(block, axis, dim, width, hop)
        lows.insert(0, low)
        highs.append(high)
        need -= width
        hop += 1
    return jnp.concatenate(lows + [block] + highs, axis=dim)


def packed_halo(fields, depths):
    top = max(depths)
    assert top <= fields[0].shape[0] and top <= fields[0].shape[1]
    offs = [sum(depths[:k]) for k in range(len(depths))]
    up = lambda f, d, dim: lax.slice_in_dim(f, f.shape[dim] - d, f.shape[dim], axis=dim)
    down = lambda f, d, dim: lax.slice_in_dim(f, 0, d, axis=dim)
    nb, ng = lax.axis_size("box"), lax.axis_size("group")
    fb, bb = shifted_pairs(nb, 1), [(t, s) for s, t in shifted_pairs(nb, 1)]
    fg, bg = shifted_pairs(ng, 1), [(t, s) for s, t in shifted_pairs(ng, 1)]

    def send(pieces, axis, pairs, dim):
        msg = jnp.concatenate(pieces, axis=dim)
        if not pairs:
            return jnp.zeros_like(msg)
        return lax.ppermute(msg, axis, pairs)

    xl = send([up(f, d, 0) for f, d in zip(fields, depths)], "box", fb, 0)
    xh = send([down(f, d, 0) for f, d in zip(fields, depths)], "box", bb, 0)
    yl = send([up(f, d, 1) for f, d in zip(fields, depths)], "group", fg, 1)
    yh = send([down(f, d, 1) for f, d in zip(fields, depths)], "group", bg, 1)
    width = yl.shape[1]
    low = send([up(yl, top, 0), up(yh, top, 0)], "box", fb, 1)
    high = send([down(yl, top, 0), down(yh, top, 0)], "box", bb, 1)
    out = []
    for f, d, o in zip(fields, depths, offs):
        ys = slice(o, o + d)
        ys2 = slice(width + o, width + o + d)
        rows = [
            jnp.concatenate([low[top - d:, ys], xl[o:o + d], low[top - d:, ys2]], axis=1),
            jnp.concatenate([yl[:, ys], f, yh[:, ys]], axis=1),
            jnp.concatenate([high[:d, ys], xh[o:o + d], high[:d, ys2]], axis=1),
        ]
        out.append(jnp.concatenate(rows, axis=0))
    return out


def shift_z(field, side):
    zeros = jnp.zeros_like(field[:, :, :1])
    if side < 0:
        return jnp.concatenate([zeros, field[:, :, :-1]], axis=2)
    return jnp.concatenate([field[:, :, 1:], zeros], axis=2)


def padded_neighbours(padded):
    return [
        padded[:-2, 1:-1, 1:-1],
        padded[2:, 1:-1, 1:-1],
        padded[1:-1, :-2, 1:-1],
        padded[1:-1, 2:, 1:-1],
        padded[1:-1, 1:-1, :-2],
        padded[1:-1, 1:-1, 2:],
    ]


def coefs_of(field, nears):
    return [jnp.where(near > 0, 2.0 * field * near / (field + near), field) for near in nears]


def apply_op(field, nears, coefs):
    total = jnp.zeros_like(field)
    for coef, near in zip(coefs, nears):
        total = total + coef * (field - near)
    return total


def group_matrix(n, k):
    rows = lax.broadcasted_iota(jnp.int32, (n, n // k), 0) // k
    cols = lax.broadcasted_iota(jnp.int32, (n, n // k), 1)
    return (rows == cols).astype(jnp.float32)


def block_mean(field):
    sx, sy, sz = field.shape
    fx = field.reshape(sx // 4, 4, sy, sz).sum(axis=1)
    fz = jnp.einsum("xyz,zc->xyc", fx, group_matrix(sz, 4), precision=HIGHEST)
    fy = jnp.einsum("xyc,yb->xbc", fz, group_matrix(sy, 4), precision=HIGHEST)
    return fy * (1.0 / 64.0)


def expand(coarse, shape):
    sx, sy, sz = shape
    cz = jnp.einsum("xbc,zc->xbz", coarse, group_matrix(sz, 4), precision=HIGHEST)
    cy = jnp.einsum("xbz,yb->xyz", cz, group_matrix(sy, 4), precision=HIGHEST)
    return jnp.broadcast_to(cy[:, None], (sx // 4, 4, sy, sz)).reshape(sx, sy, sz)


def inside_mask(shape, depth, totals):
    ex, ey, ez = shape
    cx, cy = ex - 2 * depth, ey - 2 * depth
    gx = lax.axis_index("box") * cx - depth + lax.broadcasted_iota(jnp.int32, shape, 0)
    gy = lax.axis_index("group") * cy - depth + lax.broadcasted_iota(jnp.int32, shape, 1)
    return (gx >= 0) & (gx < totals[0]) & (gy >= 0) & (gy < totals[1])


def chebyshev_local(rhs_c, b_c):
    depth = CHEB
    cx, cy, cz = rhs_c.shape
    both = jnp.stack([b_c, rhs_c])
    both = deep_extend(both, "box", 1, depth)
    both = deep_extend(both, "group", 2, depth)
    b_ext, rhs_ext = both[0], both[1]
    totals = (cx * lax.axis_size("box"), cy * lax.axis_size("group"))
    inside = inside_mask(b_ext.shape, depth, totals)
    coefs = [c * 0.0625 for c in coefs_of(b_ext, padded_neighbours(jnp.pad(b_ext, 1)))]
    diag = sum(coefs)
    inv_diag = jnp.where(inside, 1.0 / jnp.where(inside, diag, 1.0), 0.0)

    low, high = (0.05, 2.0)
    theta = (high + low) / 2.0
    delta = (high - low) / 2.0
    sigma = theta / delta
    rho = 1.0 / sigma
    solution = jnp.zeros_like(rhs_ext)
    remain = jnp.where(inside, rhs_ext, 0.0)
    direction = remain * inv_diag / theta
    for step in range(CHEB):
        solution = solution + direction
        if step + 1 < CHEB:
            nears = padded_neighbours(jnp.pad(direction, 1))
            remain = remain - apply_op(direction, nears, coefs)
            rho_next = 1.0 / (2.0 * sigma - rho)
            direction = rho_next * rho * direction + 2.0 * rho_next / delta * remain * inv_diag
            rho = rho_next
    return solution[depth:depth + cx, depth:depth + cy]


def grid_mask(shape, depth, axes, totals):
    inside = None
    for dim, (axis, total) in enumerate(zip(axes, totals)):
        own = shape[dim] - 2 * depth
        g = lax.axis_index(axis) * own - depth + lax.broadcasted_iota(jnp.int32, shape, dim)
        ok = (g >= 0) & (g < total)
        inside = ok if inside is None else inside & ok
    return inside


def low_faces(b):
    faces = []
    for dim in range(3):
        n = b.shape[dim]
        lo = lax.slice_in_dim(b, 0, n - 1, axis=dim)
        hi = lax.slice_in_dim(b, 1, n, axis=dim)
        inner = jnp.where((lo > 0) & (hi > 0), 2.0 * hi * lo / (hi + lo), hi + lo)
        faces.append(jnp.concatenate([lax.slice_in_dim(b, 0, 1, axis=dim), inner], axis=dim))
    return faces


def face_pairs(b, faces):
    pairs = []
    for dim, lo in enumerate(faces):
        n = b.shape[dim]
        hi = jnp.concatenate(
            [lax.slice_in_dim(lo, 1, n, axis=dim), lax.slice_in_dim(b, n - 1, n, axis=dim)], axis=dim
        )
        pairs += [lo, hi]
    return pairs


def per_device(right_side, inv_density, pressure):
    depth = SWEEPS + 1
    sx, sy, sz = pressure.shape
    rhs_e, b_e, fine = packed_halo([right_side, inv_density, pressure], [depth - 1, depth, depth])
    rhs_e = jnp.pad(rhs_e, ((1, 1), (1, 1), (0, 0)))
    rhs_e, b_e, fine = lax.optimization_barrier((rhs_e, b_e, fine))
    totals = (sx * lax.axis_size("box"), sy * lax.axis_size("group"))
    inside = grid_mask(fine.shape, depth, ("box", "group"), totals)
    coefs = face_pairs(b_e, low_faces(b_e))
    diag = sum(coefs)
    for sweep in range(SWEEPS):
        step = 2.0 / 3.0 * (rhs_e - apply_op(fine, padded_neighbours(jnp.pad(fine, 1)), coefs)) / diag
        fine = jnp.where(inside, fine + step, 0.0)
    res = rhs_e - apply_op(fine, padded_neighbours(jnp.pad(fine, 1)), coefs)
    own = (slice(depth, depth + sx), slice(depth, depth + sy))
    fine, res = fine[own], res[own]
    coarse_rhs = block_mean(res)
    coarse_b = block_mean(inv_density)
    corr = chebyshev_local(coarse_rhs, coarse_b)
    return fine + expand(corr, fine.shape)


def solution(mesh):
    return jax.shard_map(
        per_device,
        mesh=mesh,
        in_specs=(P("box", "group", None), P("box", "group", None), P("box", "group", None)),
        out_specs=P("box", "group", None),
        check_vma=False,
    )
```

```python
import jax
import jax.numpy as jnp
from jax import lax
from jax.sharding import PartitionSpec as P

SWEEPS = 2
CHEB = 8
HIGHEST = lax.Precision.HIGHEST


def shifted_pairs(count, hop):
    return [(i, i + hop) for i in range(count - hop)]


def halo_from(block, axis, dim, width, hop):
    count = lax.axis_size(axis)
    n = block.shape[dim]
    if hop >= count:
        shape = list(block.shape)
        shape[dim] = width
        zeros = jnp.zeros(shape, block.dtype)
        return zeros, zeros
    forward = shifted_pairs(count, hop)
    backward = [(t, s) for s, t in forward]
    low = lax.ppermute(lax.slice_in_dim(block, n - width, n, axis=dim), axis, forward)
    high = lax.ppermute(lax.slice_in_dim(block, 0, width, axis=dim), axis, backward)
    return low, high


def deep_extend(block, axis, dim, depth):
    n = block.shape[dim]
    lows, highs = [], []
    need, hop = depth, 1
    while need > 0:
        width = min(n, need)
        low, high = halo_from(block, axis, dim, width, hop)
        lows.insert(0, low)
        highs.append(high)
        need -= width
        hop += 1
    return jnp.concatenate(lows + [block] + highs, axis=dim)


def packed_halo(fields, depths):
    top = max(depths)
    assert top <= fields[0].shape[0] and top <= fields[0].shape[1]
    offs = [sum(depths[:k]) for k in range(len(depths))]
    up = lambda f, d, dim: lax.slice_in_dim(f, f.shape[dim] - d, f.shape[dim], axis=dim)
    down = lambda f, d, dim: lax.slice_in_dim(f, 0, d, axis=dim)
    nb, ng = lax.axis_size("box"), lax.axis_size("group")
    fb, bb = shifted_pairs(nb, 1), [(t, s) for s, t in shifted_pairs(nb, 1)]
    fg, bg = shifted_pairs(ng, 1), [(t, s) for s, t in shifted_pairs(ng, 1)]

    def send(pieces, axis, pairs, dim):
        msg = jnp.concatenate(pieces, axis=dim)
        if not pairs:
            return jnp.zeros_like(msg)
        return lax.ppermute(msg, axis, pairs)

    xl = send([up(f, d, 0) for f, d in zip(fields, depths)], "box", fb, 0)
    xh = send([down(f, d, 0) for f, d in zip(fields, depths)], "box", bb, 0)
    yl = send([up(f, d, 1) for f, d in zip(fields, depths)], "group", fg, 1)
    yh = send([down(f, d, 1) for f, d in zip(fields, depths)], "group", bg, 1)
    width = yl.shape[1]
    low = send([up(yl, top, 0), up(yh, top, 0)], "box", fb, 1)
    high = send([down(yl, top, 0), down(yh, top, 0)], "box", bb, 1)
    out = []
    for f, d, o in zip(fields, depths, offs):
        ys = slice(o, o + d)
        ys2 = slice(width + o, width + o + d)
        rows = [
            jnp.concatenate([low[top - d:, ys], xl[o:o + d], low[top - d:, ys2]], axis=1),
            jnp.concatenate([yl[:, ys], f, yh[:, ys]], axis=1),
            jnp.concatenate([high[:d, ys], xh[o:o + d], high[:d, ys2]], axis=1),
        ]
        out.append(jnp.concatenate(rows, axis=0))
    return out


def shift_z(field, side):
    zeros = jnp.zeros_like(field[:, :, :1])
    if side < 0:
        return jnp.concatenate([zeros, field[:, :, :-1]], axis=2)
    return jnp.concatenate([field[:, :, 1:], zeros], axis=2)


def padded_neighbours(padded):
    return [
        padded[:-2, 1:-1, 1:-1],
        padded[2:, 1:-1, 1:-1],
        padded[1:-1, :-2, 1:-1],
        padded[1:-1, 2:, 1:-1],
        padded[1:-1, 1:-1, :-2],
        padded[1:-1, 1:-1, 2:],
    ]


def coefs_of(field, nears):
    return [jnp.where(near > 0, 2.0 * field * near / (field + near), field) for near in nears]


def apply_op(field, nears, coefs):
    total = jnp.zeros_like(field)
    for coef, near in zip(coefs, nears):
        total = total + coef * (field - near)
    return total


def group_matrix(n, k):
    rows = lax.broadcasted_iota(jnp.int32, (n, n // k), 0) // k
    cols = lax.broadcasted_iota(jnp.int32, (n, n // k), 1)
    return (rows == cols).astype(jnp.float32)


def block_mean(field):
    sx, sy, sz = field.shape
    fx = field.reshape(sx // 4, 4, sy, sz).sum(axis=1)
    fz = jnp.einsum("xyz,zc->xyc", fx, group_matrix(sz, 4), precision=HIGHEST)
    fy = jnp.einsum("xyc,yb->xbc", fz, group_matrix(sy, 4), precision=HIGHEST)
    return fy * (1.0 / 64.0)


def expand(coarse, shape):
    sx, sy, sz = shape
    cz = jnp.einsum("xbc,zc->xbz", coarse, group_matrix(sz, 4), precision=HIGHEST)
    cy = jnp.einsum("xbz,yb->xyz", cz, group_matrix(sy, 4), precision=HIGHEST)
    return jnp.broadcast_to(cy[:, None], (sx // 4, 4, sy, sz)).reshape(sx, sy, sz)


def inside_mask(shape, depth, totals):
    ex, ey, ez = shape
    cx, cy = ex - 2 * depth, ey - 2 * depth
    gx = lax.axis_index("box") * cx - depth + lax.broadcasted_iota(jnp.int32, shape, 0)
    gy = lax.axis_index("group") * cy - depth + lax.broadcasted_iota(jnp.int32, shape, 1)
    return (gx >= 0) & (gx < totals[0]) & (gy >= 0) & (gy < totals[1])


def coarse_extend(field):
    return deep_extend(deep_extend(field, "box", 0, CHEB), "group", 1, CHEB)


def chebyshev_local(rhs_c, b_ext):
    depth = CHEB
    cx, cy, cz = rhs_c.shape
    rhs_ext = coarse_extend(rhs_c)
    totals = (cx * lax.axis_size("box"), cy * lax.axis_size("group"))
    inside = inside_mask(b_ext.shape, depth, totals)
    coefs = [c * 0.0625 for c in coefs_of(b_ext, padded_neighbours(jnp.pad(b_ext, 1)))]
    diag = sum(coefs)
    inv_diag = jnp.where(inside, 1.0 / jnp.where(inside, diag, 1.0), 0.0)

    low, high = (0.05, 2.0)
    theta = (high + low) / 2.0
    delta = (high - low) / 2.0
    sigma = theta / delta
    rho = 1.0 / sigma
    solution = jnp.zeros_like(rhs_ext)
    remain = jnp.where(inside, rhs_ext, 0.0)
    direction = remain * inv_diag / theta
    for step in range(CHEB):
        solution = solution + direction
        if step + 1 < CHEB:
            nears = padded_neighbours(jnp.pad(direction, 1))
            remain = remain - apply_op(direction, nears, coefs)
            rho_next = 1.0 / (2.0 * sigma - rho)
            direction = rho_next * rho * direction + 2.0 * rho_next / delta * remain * inv_diag
            rho = rho_next
    return solution[depth:depth + cx, depth:depth + cy]


def grid_mask(shape, depth, axes, totals):
    inside = None
    for dim, (axis, total) in enumerate(zip(axes, totals)):
        own = shape[dim] - 2 * depth
        g = lax.axis_index(axis) * own - depth + lax.broadcasted_iota(jnp.int32, shape, dim)
        ok = (g >= 0) & (g < total)
        inside = ok if inside is None else inside & ok
    return inside


def low_faces(b):
    faces = []
    for dim in range(3):
        n = b.shape[dim]
        lo = lax.slice_in_dim(b, 0, n - 1, axis=dim)
        hi = lax.slice_in_dim(b, 1, n, axis=dim)
        inner = jnp.where((lo > 0) & (hi > 0), 2.0 * hi * lo / (hi + lo), hi + lo)
        faces.append(jnp.concatenate([lax.slice_in_dim(b, 0, 1, axis=dim), inner], axis=dim))
    return faces


def face_pairs(b, faces):
    pairs = []
    for dim, lo in enumerate(faces):
        n = b.shape[dim]
        hi = jnp.concatenate(
            [lax.slice_in_dim(lo, 1, n, axis=dim), lax.slice_in_dim(b, n - 1, n, axis=dim)], axis=dim
        )
        pairs += [lo, hi]
    return pairs


def per_device(right_side, inv_density, pressure):
    depth = SWEEPS + 1
    sx, sy, sz = pressure.shape
    coarse_b_ext = coarse_extend(block_mean(inv_density))
    rhs_e, b_e, fine = packed_halo([right_side, inv_density, pressure], [depth - 1, depth, depth])
    rhs_e = jnp.pad(rhs_e, ((1, 1), (1, 1), (0, 0)))
    rhs_e, b_e, fine, coarse_b_ext = lax.optimization_barrier((rhs_e, b_e, fine, coarse_b_ext))
    totals = (sx * lax.axis_size("box"), sy * lax.axis_size("group"))
    inside = grid_mask(fine.shape, depth, ("box", "group"), totals)
    coefs = face_pairs(b_e, low_faces(b_e))
    diag = sum(coefs)
    for sweep in range(SWEEPS):
        step = 2.0 / 3.0 * (rhs_e - apply_op(fine, padded_neighbours(jnp.pad(fine, 1)), coefs)) / diag
        fine = jnp.where(inside, fine + step, 0.0)
    res = rhs_e - apply_op(fine, padded_neighbours(jnp.pad(fine, 1)), coefs)
    own = (slice(depth, depth + sx), slice(depth, depth + sy))
    fine, res = fine[own], res[own]
    coarse_rhs = block_mean(res)
    corr = chebyshev_local(coarse_rhs, coarse_b_ext)
    return fine + expand(corr, fine.shape)


def solution(mesh):
    return jax.shard_map(
        per_device,
        mesh=mesh,
        in_specs=(P("box", "group", None), P("box", "group", None), P("box", "group", None)),
        out_specs=P("box", "group", None),
        check_vma=False,
    )
```

```python
import jax
import jax.numpy as jnp
from jax import lax
from jax.experimental import pallas as pl
from jax.experimental.pallas import tpu as pltpu
from jax.sharding import PartitionSpec as P

SWEEPS = 2
CHEB = 8
HIGHEST = lax.Precision.HIGHEST
INTERPRET = False


def shifted_pairs(count, hop):
    return [(i, i + hop) for i in range(count - hop)]


def halo_from(block, axis, dim, width, hop):
    count = lax.axis_size(axis)
    n = block.shape[dim]
    if hop >= count:
        shape = list(block.shape)
        shape[dim] = width
        zeros = jnp.zeros(shape, block.dtype)
        return zeros, zeros
    forward = shifted_pairs(count, hop)
    backward = [(t, s) for s, t in forward]
    low = lax.ppermute(lax.slice_in_dim(block, n - width, n, axis=dim), axis, forward)
    high = lax.ppermute(lax.slice_in_dim(block, 0, width, axis=dim), axis, backward)
    return low, high


def deep_extend(block, axis, dim, depth):
    n = block.shape[dim]
    lows, highs = [], []
    need, hop = depth, 1
    while need > 0:
        width = min(n, need)
        low, high = halo_from(block, axis, dim, width, hop)
        lows.insert(0, low)
        highs.append(high)
        need -= width
        hop += 1
    return jnp.concatenate(lows + [block] + highs, axis=dim)


def packed_halo(fields, depths):
    top = max(depths)
    assert top <= fields[0].shape[0] and top <= fields[0].shape[1]
    offs = [sum(depths[:k]) for k in range(len(depths))]
    up = lambda f, d, dim: lax.slice_in_dim(f, f.shape[dim] - d, f.shape[dim], axis=dim)
    down = lambda f, d, dim: lax.slice_in_dim(f, 0, d, axis=dim)
    nb, ng = lax.axis_size("box"), lax.axis_size("group")
    fb, bb = shifted_pairs(nb, 1), [(t, s) for s, t in shifted_pairs(nb, 1)]
    fg, bg = shifted_pairs(ng, 1), [(t, s) for s, t in shifted_pairs(ng, 1)]

    def send(pieces, axis, pairs, dim):
        msg = jnp.concatenate(pieces, axis=dim)
        if not pairs:
            return jnp.zeros_like(msg)
        return lax.ppermute(msg, axis, pairs)

    xl = send([up(f, d, 0) for f, d in zip(fields, depths)], "box", fb, 0)
    xh = send([down(f, d, 0) for f, d in zip(fields, depths)], "box", bb, 0)
    yl = send([up(f, d, 1) for f, d in zip(fields, depths)], "group", fg, 1)
    yh = send([down(f, d, 1) for f, d in zip(fields, depths)], "group", bg, 1)
    width = yl.shape[1]
    low = send([up(yl, top, 0), up(yh, top, 0)], "box", fb, 1)
    high = send([down(yl, top, 0), down(yh, top, 0)], "box", bb, 1)
    out = []
    for f, d, o in zip(fields, depths, offs):
        ys = slice(o, o + d)
        ys2 = slice(width + o, width + o + d)
        rows = [
            jnp.concatenate([low[top - d:, ys], xl[o:o + d], low[top - d:, ys2]], axis=1),
            jnp.concatenate([yl[:, ys], f, yh[:, ys]], axis=1),
            jnp.concatenate([high[:d, ys], xh[o:o + d], high[:d, ys2]], axis=1),
        ]
        out.append(jnp.concatenate(rows, axis=0))
    return out


def shift_z(field, side):
    zeros = jnp.zeros_like(field[:, :, :1])
    if side < 0:
        return jnp.concatenate([zeros, field[:, :, :-1]], axis=2)
    return jnp.concatenate([field[:, :, 1:], zeros], axis=2)


def padded_neighbours(padded):
    return [
        padded[:-2, 1:-1, 1:-1],
        padded[2:, 1:-1, 1:-1],
        padded[1:-1, :-2, 1:-1],
        padded[1:-1, 2:, 1:-1],
        padded[1:-1, 1:-1, :-2],
        padded[1:-1, 1:-1, 2:],
    ]


def coefs_of(field, nears):
    return [jnp.where(near > 0, 2.0 * field * near / (field + near), field) for near in nears]


def apply_op(field, nears, coefs):
    total = jnp.zeros_like(field)
    for coef, near in zip(coefs, nears):
        total = total + coef * (field - near)
    return total


def group_matrix(n, k):
    rows = lax.broadcasted_iota(jnp.int32, (n, n // k), 0) // k
    cols = lax.broadcasted_iota(jnp.int32, (n, n // k), 1)
    return (rows == cols).astype(jnp.float32)


def block_mean(field):
    sx, sy, sz = field.shape
    return block_mean_x(field.reshape(sx // 4, 4, sy, sz).sum(axis=1))


def block_mean_x(fx):
    sx, sy, sz = fx.shape
    fz = jnp.einsum("xyz,zc->xyc", fx, group_matrix(sz, 4), precision=HIGHEST)
    fy = jnp.einsum("xyc,yb->xbc", fz, group_matrix(sy, 4), precision=HIGHEST)
    return fy * (1.0 / 64.0)


def expand(coarse, shape):
    sx, sy, sz = shape
    cz = jnp.einsum("xbc,zc->xbz", coarse, group_matrix(sz, 4), precision=HIGHEST)
    cy = jnp.einsum("xbz,yb->xyz", cz, group_matrix(sy, 4), precision=HIGHEST)
    return jnp.broadcast_to(cy[:, None], (sx // 4, 4, sy, sz)).reshape(sx, sy, sz)


def inside_mask(shape, depth, totals):
    ex, ey, ez = shape
    cx, cy = ex - 2 * depth, ey - 2 * depth
    gx = lax.axis_index("box") * cx - depth + lax.broadcasted_iota(jnp.int32, shape, 0)
    gy = lax.axis_index("group") * cy - depth + lax.broadcasted_iota(jnp.int32, shape, 1)
    return (gx >= 0) & (gx < totals[0]) & (gy >= 0) & (gy < totals[1])


def chebyshev_local(rhs_c, b_c):
    depth = CHEB
    cx, cy, cz = rhs_c.shape
    both = jnp.stack([b_c, rhs_c])
    both = deep_extend(both, "box", 1, depth)
    both = deep_extend(both, "group", 2, depth)
    b_ext, rhs_ext = both[0], both[1]
    totals = (cx * lax.axis_size("box"), cy * lax.axis_size("group"))
    inside = inside_mask(b_ext.shape, depth, totals)
    coefs = [c * 0.0625 for c in coefs_of(b_ext, padded_neighbours(jnp.pad(b_ext, 1)))]
    diag = sum(coefs)
    inv_diag = jnp.where(inside, 1.0 / jnp.where(inside, diag, 1.0), 0.0)

    low, high = (0.05, 2.0)
    theta = (high + low) / 2.0
    delta = (high - low) / 2.0
    sigma = theta / delta
    rho = 1.0 / sigma
    solution = jnp.zeros_like(rhs_ext)
    remain = jnp.where(inside, rhs_ext, 0.0)
    direction = remain * inv_diag / theta
    for step in range(CHEB):
        solution = solution + direction
        if step + 1 < CHEB:
            nears = padded_neighbours(jnp.pad(direction, 1))
            remain = remain - apply_op(direction, nears, coefs)
            rho_next = 1.0 / (2.0 * sigma - rho)
            direction = rho_next * rho * direction + 2.0 * rho_next / delta * remain * inv_diag
            rho = rho_next
    return solution[depth:depth + cx, depth:depth + cy]


def grid_mask(shape, depth, axes, totals):
    inside = None
    for dim, (axis, total) in enumerate(zip(axes, totals)):
        own = shape[dim] - 2 * depth
        g = lax.axis_index(axis) * own - depth + lax.broadcasted_iota(jnp.int32, shape, dim)
        ok = (g >= 0) & (g < total)
        inside = ok if inside is None else inside & ok
    return inside


def low_faces(b):
    faces = []
    for dim in range(3):
        n = b.shape[dim]
        lo = lax.slice_in_dim(b, 0, n - 1, axis=dim)
        hi = lax.slice_in_dim(b, 1, n, axis=dim)
        inner = jnp.where((lo > 0) & (hi > 0), 2.0 * hi * lo / (hi + lo), hi + lo)
        faces.append(jnp.concatenate([lax.slice_in_dim(b, 0, 1, axis=dim), inner], axis=dim))
    return faces


def face_pairs(b, faces):
    pairs = []
    for dim, lo in enumerate(faces):
        n = b.shape[dim]
        hi = jnp.concatenate(
            [lax.slice_in_dim(lo, 1, n, axis=dim), lax.slice_in_dim(b, n - 1, n, axis=dim)], axis=dim
        )
        pairs += [lo, hi]
    return pairs


def fine_kernel(bounds, rhs_ref, b_ref, p_ref, fine_out, resx_out,
                lx_ref, ly_ref, lz_ref, d_ref, f1_ref, f2_ref, plane_ref):
    ex, ey, nz = b_ref.shape
    sx, sy = fine_out.shape[0], fine_out.shape[1]
    depth = (ex - sx) // 2
    row = lax.broadcasted_iota(jnp.int32, (ey, nz), 0)
    lane = lax.broadcasted_iota(jnp.int32, (ey, nz), 1)
    x_lo, x_hi, y_lo, y_hi = bounds[0], bounds[1], bounds[2], bounds[3]
    rows_in = (row >= y_lo) & (row < y_hi)

    def face(a, n):
        return jnp.where((a > 0) & (n > 0), 2.0 * a * n / (a + n), a + n)

    def below(ref, x):
        return jnp.where(x > 0, ref[jnp.maximum(x - 1, 0)], 0.0)

    def above(ref, x):
        return jnp.where(x < ex - 1, ref[jnp.minimum(x + 1, ex - 1)], 0.0)

    def faces_body(x, carry):
        b0 = b_ref[x]
        lx_ref[x] = face(b0, below(b_ref, x))
        ly_ref[x] = face(b0, pltpu.roll(b0, 1, 0))
        lz_ref[x] = face(b0, jnp.where(lane == 0, 0.0, pltpu.roll(b0, 1, 1)))
        return carry

    lax.fori_loop(0, ex, faces_body, 0)

    def coefs(x):
        b0 = b_ref[x]
        lx_hi = jnp.where(x < ex - 1, lx_ref[jnp.minimum(x + 1, ex - 1)], b0)
        ly = ly_ref[x]
        lz = lz_ref[x]
        ly_hi = pltpu.roll(ly, ey - 1, 0)
        lz_hi = jnp.where(lane == nz - 1, b0, pltpu.roll(lz, nz - 1, 1))
        return [lx_ref[x], lx_hi, ly, ly_hi, lz, lz_hi]

    def diag_body(x, carry):
        total = jnp.zeros((ey, nz), jnp.float32)
        for c in coefs(x):
            total = total + c
        d_ref[x] = total
        return carry

    lax.fori_loop(0, ex, diag_body, 0)

    def apply_at(src, x):
        v = src[x]
        nears = [
            below(src, x),
            above(src, x),
            pltpu.roll(v, 1, 0),
            pltpu.roll(v, ey - 1, 0),
            jnp.where(lane == 0, 0.0, pltpu.roll(v, 1, 1)),
            jnp.where(lane == nz - 1, 0.0, pltpu.roll(v, nz - 1, 1)),
        ]
        total = jnp.zeros((ey, nz), jnp.float32)
        for c, n in zip(coefs(x), nears):
            total = total + c * (v - n)
        return v, total

    def sweep(src, dst):
        def body(x, carry):
            v, av = apply_at(src, x)
            new = v + 2.0 / 3.0 * (rhs_ref[x] - av) / d_ref[x]
            inside = rows_in & (x >= x_lo) & (x < x_hi)
            dst[x] = jnp.where(inside, new, 0.0)
            return carry

        lax.fori_loop(0, ex, body, 0)

    sweep(p_ref, f1_ref)
    sweep(f1_ref, f2_ref)

    def res_body(xc, carry):
        acc = jnp.zeros((sy, nz), jnp.float32)
        for k in range(4):
            xo = xc * 4 + k
            x = xo + depth
            v, av = apply_at(f2_ref, x)
            plane_ref[...] = rhs_ref[x] - av
            acc = acc + plane_ref[pl.ds(depth + 1, sy), :]
            fine_out[xo] = f2_ref[x, pl.ds(depth + 1, sy), :]
        resx_out[xc] = acc
        return carry

    lax.fori_loop(0, sx // 4, res_body, 0)


def fine_stage(rhs_e, b_e, p_e, bounds, own_shape):
    sx, sy, sz = own_shape
    ex, ey, _ = b_e.shape
    vmem = pl.BlockSpec(memory_space=pltpu.VMEM)
    plane = jax.ShapeDtypeStruct
    return pl.pallas_call(
        fine_kernel,
        out_shape=(plane((sx, sy, sz), jnp.float32), plane((sx // 4, sy, sz), jnp.float32)),
        in_specs=[pl.BlockSpec(memory_space=pltpu.SMEM), vmem, vmem, vmem],
        out_specs=(vmem, vmem),
        scratch_shapes=[pltpu.VMEM((ex, ey, sz), jnp.float32) for _ in range(6)]
        + [pltpu.VMEM((ey, sz), jnp.float32)],
        compiler_params=pltpu.CompilerParams(vmem_limit_bytes=100 * 1024 * 1024),
        interpret=INTERPRET,
    )(bounds, rhs_e, b_e, p_e)


def per_device(right_side, inv_density, pressure):
    depth = SWEEPS + 1
    sx, sy, sz = pressure.shape
    rhs_e, b_e, fine = packed_halo([right_side, inv_density, pressure], [depth - 1, depth, depth])
    rows = ((0, 0), (1, 1), (0, 0))
    rhs_e = jnp.pad(rhs_e, ((1, 1), (2, 2), (0, 0)))
    b_e, fine = jnp.pad(b_e, rows), jnp.pad(fine, rows)
    rhs_e, b_e, fine = lax.optimization_barrier((rhs_e, b_e, fine))
    ex, ey = b_e.shape[0], b_e.shape[1]
    bi, gi = lax.axis_index("box"), lax.axis_index("group")
    nb, ng = lax.axis_size("box"), lax.axis_size("group")
    bounds = jnp.stack([
        jnp.maximum(depth - bi * sx, 0),
        jnp.minimum(nb * sx + depth - bi * sx, ex),
        jnp.maximum(depth + 1 - gi * sy, 1),
        jnp.minimum(ng * sy + depth + 1 - gi * sy, ey - 1),
    ]).astype(jnp.int32)
    fine, resx = fine_stage(rhs_e, b_e, fine, bounds, pressure.shape)
    coarse_rhs = block_mean_x(resx)
    coarse_b = block_mean(inv_density)
    corr = chebyshev_local(coarse_rhs, coarse_b)
    return fine + expand(corr, fine.shape)


def solution(mesh):
    return jax.shard_map(
        per_device,
        mesh=mesh,
        in_specs=(P("box", "group", None), P("box", "group", None), P("box", "group", None)),
        out_specs=P("box", "group", None),
        check_vma=False,
    )
```

```python
import jax
import jax.numpy as jnp
from jax import lax
from jax.experimental import pallas as pl
from jax.experimental.pallas import tpu as pltpu
from jax.sharding import PartitionSpec as P

SWEEPS = 2
CHEB = 8
HIGHEST = lax.Precision.HIGHEST
INTERPRET = False


def shifted_pairs(count, hop):
    return [(i, i + hop) for i in range(count - hop)]


def halo_from(block, axis, dim, width, hop):
    count = lax.axis_size(axis)
    n = block.shape[dim]
    if hop >= count:
        shape = list(block.shape)
        shape[dim] = width
        zeros = jnp.zeros(shape, block.dtype)
        return zeros, zeros
    forward = shifted_pairs(count, hop)
    backward = [(t, s) for s, t in forward]
    low = lax.ppermute(lax.slice_in_dim(block, n - width, n, axis=dim), axis, forward)
    high = lax.ppermute(lax.slice_in_dim(block, 0, width, axis=dim), axis, backward)
    return low, high


def deep_extend(block, axis, dim, depth):
    n = block.shape[dim]
    lows, highs = [], []
    need, hop = depth, 1
    while need > 0:
        width = min(n, need)
        low, high = halo_from(block, axis, dim, width, hop)
        lows.insert(0, low)
        highs.append(high)
        need -= width
        hop += 1
    return jnp.concatenate(lows + [block] + highs, axis=dim)


def packed_halo(fields, depths):
    top = max(depths)
    assert top <= fields[0].shape[0] and top <= fields[0].shape[1]
    offs = [sum(depths[:k]) for k in range(len(depths))]
    up = lambda f, d, dim: lax.slice_in_dim(f, f.shape[dim] - d, f.shape[dim], axis=dim)
    down = lambda f, d, dim: lax.slice_in_dim(f, 0, d, axis=dim)
    nb, ng = lax.axis_size("box"), lax.axis_size("group")
    fb, bb = shifted_pairs(nb, 1), [(t, s) for s, t in shifted_pairs(nb, 1)]
    fg, bg = shifted_pairs(ng, 1), [(t, s) for s, t in shifted_pairs(ng, 1)]

    def send(pieces, axis, pairs, dim):
        msg = jnp.concatenate(pieces, axis=dim)
        if not pairs:
            return jnp.zeros_like(msg)
        return lax.ppermute(msg, axis, pairs)

    xl = send([up(f, d, 0) for f, d in zip(fields, depths)], "box", fb, 0)
    xh = send([down(f, d, 0) for f, d in zip(fields, depths)], "box", bb, 0)
    yl = send([up(f, d, 1) for f, d in zip(fields, depths)], "group", fg, 1)
    yh = send([down(f, d, 1) for f, d in zip(fields, depths)], "group", bg, 1)
    width = yl.shape[1]
    low = send([up(yl, top, 0), up(yh, top, 0)], "box", fb, 1)
    high = send([down(yl, top, 0), down(yh, top, 0)], "box", bb, 1)
    out = []
    for f, d, o in zip(fields, depths, offs):
        ys = slice(o, o + d)
        ys2 = slice(width + o, width + o + d)
        rows = [
            jnp.concatenate([low[top - d:, ys], xl[o:o + d], low[top - d:, ys2]], axis=1),
            jnp.concatenate([yl[:, ys], f, yh[:, ys]], axis=1),
            jnp.concatenate([high[:d, ys], xh[o:o + d], high[:d, ys2]], axis=1),
        ]
        out.append(jnp.concatenate(rows, axis=0))
    return out


def shift_z(field, side):
    zeros = jnp.zeros_like(field[:, :, :1])
    if side < 0:
        return jnp.concatenate([zeros, field[:, :, :-1]], axis=2)
    return jnp.concatenate([field[:, :, 1:], zeros], axis=2)


def padded_neighbours(padded):
    return [
        padded[:-2, 1:-1, 1:-1],
        padded[2:, 1:-1, 1:-1],
        padded[1:-1, :-2, 1:-1],
        padded[1:-1, 2:, 1:-1],
        padded[1:-1, 1:-1, :-2],
        padded[1:-1, 1:-1, 2:],
    ]


def coefs_of(field, nears):
    return [jnp.where(near > 0, 2.0 * field * near / (field + near), field) for near in nears]


def apply_op(field, nears, coefs):
    total = jnp.zeros_like(field)
    for coef, near in zip(coefs, nears):
        total = total + coef * (field - near)
    return total


def group_matrix(n, k):
    rows = lax.broadcasted_iota(jnp.int32, (n, n // k), 0) // k
    cols = lax.broadcasted_iota(jnp.int32, (n, n // k), 1)
    return (rows == cols).astype(jnp.float32)


def block_mean(field):
    sx, sy, sz = field.shape
    return block_mean_x(field.reshape(sx // 4, 4, sy, sz).sum(axis=1))


def block_mean_x(fx):
    sx, sy, sz = fx.shape
    fz = jnp.einsum("xyz,zc->xyc", fx, group_matrix(sz, 4), precision=HIGHEST)
    fy = jnp.einsum("xyc,yb->xbc", fz, group_matrix(sy, 4), precision=HIGHEST)
    return fy * (1.0 / 64.0)


def expand(coarse, shape):
    sx, sy, sz = shape
    cz = jnp.einsum("xbc,zc->xbz", coarse, group_matrix(sz, 4), precision=HIGHEST)
    cy = jnp.einsum("xbz,yb->xyz", cz, group_matrix(sy, 4), precision=HIGHEST)
    return jnp.broadcast_to(cy[:, None], (sx // 4, 4, sy, sz)).reshape(sx, sy, sz)


def inside_mask(shape, depth, totals):
    ex, ey, ez = shape
    cx, cy = ex - 2 * depth, ey - 2 * depth
    gx = lax.axis_index("box") * cx - depth + lax.broadcasted_iota(jnp.int32, shape, 0)
    gy = lax.axis_index("group") * cy - depth + lax.broadcasted_iota(jnp.int32, shape, 1)
    return (gx >= 0) & (gx < totals[0]) & (gy >= 0) & (gy < totals[1])


def chebyshev_local(rhs_c, b_c):
    depth = CHEB
    cx, cy, cz = rhs_c.shape
    both = jnp.stack([b_c, rhs_c])
    both = deep_extend(both, "box", 1, depth)
    both = deep_extend(both, "group", 2, depth)
    b_ext, rhs_ext = both[0], both[1]
    totals = (cx * lax.axis_size("box"), cy * lax.axis_size("group"))
    inside = inside_mask(b_ext.shape, depth, totals)
    coefs = [c * 0.0625 for c in coefs_of(b_ext, padded_neighbours(jnp.pad(b_ext, 1)))]
    diag = sum(coefs)
    inv_diag = jnp.where(inside, 1.0 / jnp.where(inside, diag, 1.0), 0.0)

    low, high = (0.05, 2.0)
    theta = (high + low) / 2.0
    delta = (high - low) / 2.0
    sigma = theta / delta
    rho = 1.0 / sigma
    solution = jnp.zeros_like(rhs_ext)
    remain = jnp.where(inside, rhs_ext, 0.0)
    direction = remain * inv_diag / theta
    for step in range(CHEB):
        solution = solution + direction
        if step + 1 < CHEB:
            nears = padded_neighbours(jnp.pad(direction, 1))
            remain = remain - apply_op(direction, nears, coefs)
            rho_next = 1.0 / (2.0 * sigma - rho)
            direction = rho_next * rho * direction + 2.0 * rho_next / delta * remain * inv_diag
            rho = rho_next
    return solution[depth:depth + cx, depth:depth + cy]


def grid_mask(shape, depth, axes, totals):
    inside = None
    for dim, (axis, total) in enumerate(zip(axes, totals)):
        own = shape[dim] - 2 * depth
        g = lax.axis_index(axis) * own - depth + lax.broadcasted_iota(jnp.int32, shape, dim)
        ok = (g >= 0) & (g < total)
        inside = ok if inside is None else inside & ok
    return inside


def low_faces(b):
    faces = []
    for dim in range(3):
        n = b.shape[dim]
        lo = lax.slice_in_dim(b, 0, n - 1, axis=dim)
        hi = lax.slice_in_dim(b, 1, n, axis=dim)
        inner = jnp.where((lo > 0) & (hi > 0), 2.0 * hi * lo / (hi + lo), hi + lo)
        faces.append(jnp.concatenate([lax.slice_in_dim(b, 0, 1, axis=dim), inner], axis=dim))
    return faces


def face_pairs(b, faces):
    pairs = []
    for dim, lo in enumerate(faces):
        n = b.shape[dim]
        hi = jnp.concatenate(
            [lax.slice_in_dim(lo, 1, n, axis=dim), lax.slice_in_dim(b, n - 1, n, axis=dim)], axis=dim
        )
        pairs += [lo, hi]
    return pairs


def fine_kernel(bounds, rhs_ref, b_ref, p_ref, fine_out, resx_out,
                lx_ref, ly_ref, lz_ref, w_ref, f1_ref, f2_ref, plane_ref):
    ex, ey, nz = b_ref.shape
    sx, sy = fine_out.shape[0], fine_out.shape[1]
    depth = (ex - sx) // 2
    row = lax.broadcasted_iota(jnp.int32, (ey, nz), 0)
    lane = lax.broadcasted_iota(jnp.int32, (ey, nz), 1)
    first_z, last_z = lane == 0, lane == nz - 1
    x_lo, x_hi, y_lo, y_hi = bounds[0], bounds[1], bounds[2], bounds[3]
    rows_in = (row >= y_lo) & (row < y_hi)

    def face(a, n):
        return jnp.where((a > 0) & (n > 0), 2.0 * a * n / (a + n), a + n)

    def faces_at(x, b0, bxm):
        lx_ref[x] = face(b0, bxm)
        ly_ref[x] = face(b0, pltpu.roll(b0, 1, 0))
        lz_ref[x] = face(b0, jnp.where(first_z, 0.0, pltpu.roll(b0, 1, 1)))

    faces_at(0, b_ref[0], jnp.zeros((ey, nz), jnp.float32))

    def faces_body(x, carry):
        faces_at(x, b_ref[x], b_ref[x - 1])
        return carry

    lax.fori_loop(1, ex, faces_body, 0)

    def coefs(x):
        b0 = b_ref[x]
        ly = ly_ref[x]
        lz = lz_ref[x]
        ly_hi = pltpu.roll(ly, ey - 1, 0)
        lz_hi = jnp.where(last_z, b0, pltpu.roll(lz, nz - 1, 1))
        return [lx_ref[x], lx_ref[x + 1], ly, ly_hi, lz, lz_hi]

    def diag_body(x, carry):
        c = coefs(x)
        total = ((c[0] + c[1]) + (c[2] + c[3])) + (c[4] + c[5])
        w_ref[x] = (2.0 / 3.0) / total
        return carry

    lax.fori_loop(1, ex - 1, diag_body, 0)

    def apply_at(src, x):
        v = src[x]
        nears = [
            src[x - 1],
            src[x + 1],
            pltpu.roll(v, 1, 0),
            pltpu.roll(v, ey - 1, 0),
            jnp.where(first_z, 0.0, pltpu.roll(v, 1, 1)),
            jnp.where(last_z, 0.0, pltpu.roll(v, nz - 1, 1)),
        ]
        terms = [c * (v - n) for c, n in zip(coefs(x), nears)]
        return v, ((terms[0] + terms[1]) + (terms[2] + terms[3])) + (terms[4] + terms[5])

    zero_plane = jnp.zeros((ey, nz), jnp.float32)

    def sweep(src, dst, edge):
        for x in list(range(edge)) + list(range(ex - edge, ex)):
            dst[x] = zero_plane

        def body(x, carry):
            v, av = apply_at(src, x)
            new = v + (rhs_ref[x] - av) * w_ref[x]
            inside = rows_in & (x >= x_lo) & (x < x_hi)
            dst[x] = jnp.where(inside, new, 0.0)
            return carry

        lax.fori_loop(edge, ex - edge, body, 0)

    sweep(p_ref, f1_ref, 1)
    sweep(f1_ref, f2_ref, 2)

    def res_body(xc, carry):
        acc = jnp.zeros((sy, nz), jnp.float32)
        for k in range(4):
            xo = xc * 4 + k
            x = xo + depth
            v, av = apply_at(f2_ref, x)
            plane_ref[...] = rhs_ref[x] - av
            acc = acc + plane_ref[pl.ds(depth + 1, sy), :]
            fine_out[xo] = f2_ref[x, pl.ds(depth + 1, sy), :]
        resx_out[xc] = acc
        return carry

    lax.fori_loop(0, sx // 4, res_body, 0)


def fine_stage(rhs_e, b_e, p_e, bounds, own_shape):
    sx, sy, sz = own_shape
    ex, ey, _ = b_e.shape
    vmem = pl.BlockSpec(memory_space=pltpu.VMEM)
    plane = jax.ShapeDtypeStruct
    return pl.pallas_call(
        fine_kernel,
        out_shape=(plane((sx, sy, sz), jnp.float32), plane((sx // 4, sy, sz), jnp.float32)),
        in_specs=[pl.BlockSpec(memory_space=pltpu.SMEM), vmem, vmem, vmem],
        out_specs=(vmem, vmem),
        scratch_shapes=[pltpu.VMEM((ex, ey, sz), jnp.float32) for _ in range(6)]
        + [pltpu.VMEM((ey, sz), jnp.float32)],
        compiler_params=pltpu.CompilerParams(vmem_limit_bytes=100 * 1024 * 1024),
        interpret=INTERPRET,
    )(bounds, rhs_e, b_e, p_e)


def per_device(right_side, inv_density, pressure):
    depth = SWEEPS + 1
    sx, sy, sz = pressure.shape
    rhs_e, b_e, fine = packed_halo([right_side, inv_density, pressure], [depth - 1, depth, depth])
    rows = ((0, 0), (1, 1), (0, 0))
    rhs_e = jnp.pad(rhs_e, ((1, 1), (2, 2), (0, 0)))
    b_e, fine = jnp.pad(b_e, rows), jnp.pad(fine, rows)
    ex, ey = b_e.shape[0], b_e.shape[1]
    bi, gi = lax.axis_index("box"), lax.axis_index("group")
    nb, ng = lax.axis_size("box"), lax.axis_size("group")
    bounds = jnp.stack([
        jnp.maximum(depth - bi * sx, 0),
        jnp.minimum(nb * sx + depth - bi * sx, ex),
        jnp.maximum(depth + 1 - gi * sy, 1),
        jnp.minimum(ng * sy + depth + 1 - gi * sy, ey - 1),
    ]).astype(jnp.int32)
    fine, resx = fine_stage(rhs_e, b_e, fine, bounds, pressure.shape)
    coarse_rhs = block_mean_x(resx)
    coarse_b = block_mean(inv_density)
    corr = chebyshev_local(coarse_rhs, coarse_b)
    return fine + expand(corr, fine.shape)


def solution(mesh):
    return jax.shard_map(
        per_device,
        mesh=mesh,
        in_specs=(P("box", "group", None), P("box", "group", None), P("box", "group", None)),
        out_specs=P("box", "group", None),
        check_vma=False,
    )
```

```python
import jax
import jax.numpy as jnp
from jax import lax
from jax.sharding import PartitionSpec as P

SWEEPS = 2
CHEB = 8
HIGHEST = lax.Precision.HIGHEST


def shifted_pairs(count, hop):
    return [(i, i + hop) for i in range(count - hop)]


def halo_from(block, axis, dim, width, hop):
    count = lax.axis_size(axis)
    n = block.shape[dim]
    if hop >= count:
        shape = list(block.shape)
        shape[dim] = width
        zeros = jnp.zeros(shape, block.dtype)
        return zeros, zeros
    forward = shifted_pairs(count, hop)
    backward = [(t, s) for s, t in forward]
    low = lax.ppermute(lax.slice_in_dim(block, n - width, n, axis=dim), axis, forward)
    high = lax.ppermute(lax.slice_in_dim(block, 0, width, axis=dim), axis, backward)
    return low, high


def deep_extend(block, axis, dim, depth):
    n = block.shape[dim]
    lows, highs = [], []
    need, hop = depth, 1
    while need > 0:
        width = min(n, need)
        low, high = halo_from(block, axis, dim, width, hop)
        lows.insert(0, low)
        highs.append(high)
        need -= width
        hop += 1
    return jnp.concatenate(lows + [block] + highs, axis=dim)


def packed_halo(fields, depths):
    top = max(depths)
    assert top <= fields[0].shape[0] and top <= fields[0].shape[1]
    offs = [sum(depths[:k]) for k in range(len(depths))]
    up = lambda f, d, dim: lax.slice_in_dim(f, f.shape[dim] - d, f.shape[dim], axis=dim)
    down = lambda f, d, dim: lax.slice_in_dim(f, 0, d, axis=dim)
    nb, ng = lax.axis_size("box"), lax.axis_size("group")
    fb, bb = shifted_pairs(nb, 1), [(t, s) for s, t in shifted_pairs(nb, 1)]
    fg, bg = shifted_pairs(ng, 1), [(t, s) for s, t in shifted_pairs(ng, 1)]

    def send(pieces, axis, pairs, dim):
        msg = jnp.concatenate(pieces, axis=dim)
        if not pairs:
            return jnp.zeros_like(msg)
        return lax.ppermute(msg, axis, pairs)

    xl = send([up(f, d, 0) for f, d in zip(fields, depths)], "box", fb, 0)
    xh = send([down(f, d, 0) for f, d in zip(fields, depths)], "box", bb, 0)
    yl = send([up(f, d, 1) for f, d in zip(fields, depths)], "group", fg, 1)
    yh = send([down(f, d, 1) for f, d in zip(fields, depths)], "group", bg, 1)
    width = yl.shape[1]
    low = send([up(yl, top, 0), up(yh, top, 0)], "box", fb, 1)
    high = send([down(yl, top, 0), down(yh, top, 0)], "box", bb, 1)
    out = []
    for f, d, o in zip(fields, depths, offs):
        ys = slice(o, o + d)
        ys2 = slice(width + o, width + o + d)
        rows = [
            jnp.concatenate([low[top - d:, ys], xl[o:o + d], low[top - d:, ys2]], axis=1),
            jnp.concatenate([yl[:, ys], f, yh[:, ys]], axis=1),
            jnp.concatenate([high[:d, ys], xh[o:o + d], high[:d, ys2]], axis=1),
        ]
        out.append(jnp.concatenate(rows, axis=0))
    return out


def shift_z(field, side):
    zeros = jnp.zeros_like(field[:, :, :1])
    if side < 0:
        return jnp.concatenate([zeros, field[:, :, :-1]], axis=2)
    return jnp.concatenate([field[:, :, 1:], zeros], axis=2)


def padded_neighbours(padded):
    return [
        padded[:-2, 1:-1, 1:-1],
        padded[2:, 1:-1, 1:-1],
        padded[1:-1, :-2, 1:-1],
        padded[1:-1, 2:, 1:-1],
        padded[1:-1, 1:-1, :-2],
        padded[1:-1, 1:-1, 2:],
    ]


def coefs_of(field, nears):
    return [jnp.where(near > 0, 2.0 * field * near / (field + near), field) for near in nears]


def apply_op(field, nears, coefs):
    total = jnp.zeros_like(field)
    for coef, near in zip(coefs, nears):
        total = total + coef * (field - near)
    return total


def group_matrix(n, k):
    rows = lax.broadcasted_iota(jnp.int32, (n, n // k), 0) // k
    cols = lax.broadcasted_iota(jnp.int32, (n, n // k), 1)
    return (rows == cols).astype(jnp.float32)


def block_mean(field):
    sx, sy, sz = field.shape
    fx = field.reshape(sx // 4, 4, sy, sz).sum(axis=1)
    fz = jnp.einsum("xyz,zc->xyc", fx, group_matrix(sz, 4), precision=HIGHEST)
    fy = jnp.einsum("xyc,yb->xbc", fz, group_matrix(sy, 4), precision=HIGHEST)
    return fy * (1.0 / 64.0)


def expand(coarse, shape):
    sx, sy, sz = shape
    cz = jnp.einsum("xbc,zc->xbz", coarse, group_matrix(sz, 4), precision=HIGHEST)
    cy = jnp.einsum("xbz,yb->xyz", cz, group_matrix(sy, 4), precision=HIGHEST)
    return jnp.broadcast_to(cy[:, None], (sx // 4, 4, sy, sz)).reshape(sx, sy, sz)


def inside_mask(shape, depth, totals):
    ex, ey, ez = shape
    cx, cy = ex - 2 * depth, ey - 2 * depth
    gx = lax.axis_index("box") * cx - depth + lax.broadcasted_iota(jnp.int32, shape, 0)
    gy = lax.axis_index("group") * cy - depth + lax.broadcasted_iota(jnp.int32, shape, 1)
    return (gx >= 0) & (gx < totals[0]) & (gy >= 0) & (gy < totals[1])


def chebyshev_local(rhs_c, b_c):
    depth = CHEB
    cx, cy, cz = rhs_c.shape
    both = jnp.stack([b_c, rhs_c])
    both = deep_extend(both, "box", 1, depth)
    both = deep_extend(both, "group", 2, depth)
    b_ext, rhs_ext = both[0], both[1]
    totals = (cx * lax.axis_size("box"), cy * lax.axis_size("group"))
    inside = inside_mask(b_ext.shape, depth, totals)
    coefs = [c * 0.0625 for c in coefs_of(b_ext, padded_neighbours(jnp.pad(b_ext, 1)))]
    diag = sum(coefs)
    inv_diag = jnp.where(inside, 1.0 / jnp.where(inside, diag, 1.0), 0.0)

    low, high = (0.05, 2.0)
    theta = (high + low) / 2.0
    delta = (high - low) / 2.0
    sigma = theta / delta
    rho = 1.0 / sigma
    solution = jnp.zeros_like(rhs_ext)
    remain = jnp.where(inside, rhs_ext, 0.0)
    direction = remain * inv_diag / theta
    for step in range(CHEB):
        solution = solution + direction
        if step + 1 < CHEB:
            nears = padded_neighbours(jnp.pad(direction, 1))
            remain = remain - apply_op(direction, nears, coefs)
            rho_next = 1.0 / (2.0 * sigma - rho)
            direction = rho_next * rho * direction + 2.0 * rho_next / delta * remain * inv_diag
            rho = rho_next
    return solution[depth:depth + cx, depth:depth + cy]


def grid_mask(shape, depth, axes, totals):
    inside = None
    for dim, (axis, total) in enumerate(zip(axes, totals)):
        own = shape[dim] - 2 * depth
        g = lax.axis_index(axis) * own - depth + lax.broadcasted_iota(jnp.int32, shape, dim)
        ok = (g >= 0) & (g < total)
        inside = ok if inside is None else inside & ok
    return inside


def shared_faces(b):
    def face(a, n):
        return jnp.where((a > 0) & (n > 0), 2.0 * a * n / (a + n), a + n)

    nears = padded_neighbours(jnp.pad(b, 1))
    lx, ly, lz = face(b, nears[0]), face(b, nears[2]), face(b, nears[4])
    hx = jnp.pad(lx, ((0, 1), (0, 0), (0, 0)))[1:]
    hy = jnp.pad(ly, ((0, 0), (0, 1), (0, 0)))[:, 1:]
    hz = jnp.pad(lz, ((0, 0), (0, 0), (0, 1)))[:, :, 1:]
    top = lax.broadcasted_iota(jnp.int32, b.shape, 2) == b.shape[2] - 1
    return [lx, hx, ly, hy, lz, jnp.where(top, b, hz)]


def low_faces(b):
    faces = []
    for dim in range(3):
        n = b.shape[dim]
        lo = lax.slice_in_dim(b, 0, n - 1, axis=dim)
        hi = lax.slice_in_dim(b, 1, n, axis=dim)
        inner = jnp.where((lo > 0) & (hi > 0), 2.0 * hi * lo / (hi + lo), hi + lo)
        faces.append(jnp.concatenate([lax.slice_in_dim(b, 0, 1, axis=dim), inner], axis=dim))
    return faces


def face_pairs(b, faces):
    pairs = []
    for dim, lo in enumerate(faces):
        n = b.shape[dim]
        hi = jnp.concatenate(
            [lax.slice_in_dim(lo, 1, n, axis=dim), lax.slice_in_dim(b, n - 1, n, axis=dim)], axis=dim
        )
        pairs += [lo, hi]
    return pairs


def per_device(right_side, inv_density, pressure):
    depth = SWEEPS + 1
    sx, sy, sz = pressure.shape
    rhs_e, b_e, fine = packed_halo([right_side, inv_density, pressure], [depth - 1, depth, depth])
    rhs_e = jnp.pad(rhs_e, ((1, 1), (1, 1), (0, 0)))
    rhs_e, b_e, fine = lax.optimization_barrier((rhs_e, b_e, fine))
    totals = (sx * lax.axis_size("box"), sy * lax.axis_size("group"))
    inside = grid_mask(fine.shape, depth, ("box", "group"), totals)
    coefs = shared_faces(b_e)
    diag = sum(coefs)
    for sweep in range(SWEEPS):
        step = 2.0 / 3.0 * (rhs_e - apply_op(fine, padded_neighbours(jnp.pad(fine, 1)), coefs)) / diag
        fine = jnp.where(inside, fine + step, 0.0)
    res = rhs_e - apply_op(fine, padded_neighbours(jnp.pad(fine, 1)), coefs)
    own = (slice(depth, depth + sx), slice(depth, depth + sy))
    fine, res = fine[own], res[own]
    coarse_rhs = block_mean(res)
    coarse_b = block_mean(inv_density)
    corr = chebyshev_local(coarse_rhs, coarse_b)
    return fine + expand(corr, fine.shape)


def solution(mesh):
    return jax.shard_map(
        per_device,
        mesh=mesh,
        in_specs=(P("box", "group", None), P("box", "group", None), P("box", "group", None)),
        out_specs=P("box", "group", None),
        check_vma=False,
    )
```

```python
import jax
import jax.numpy as jnp
from jax import lax
from jax.sharding import PartitionSpec as P

SWEEPS = 2
CHEB = 8
HIGHEST = lax.Precision.HIGHEST


def shifted_pairs(count, hop):
    return [(i, i + hop) for i in range(count - hop)]


def halo_from(block, axis, dim, width, hop):
    count = lax.axis_size(axis)
    n = block.shape[dim]
    if hop >= count:
        shape = list(block.shape)
        shape[dim] = width
        zeros = jnp.zeros(shape, block.dtype)
        return zeros, zeros
    forward = shifted_pairs(count, hop)
    backward = [(t, s) for s, t in forward]
    low = lax.ppermute(lax.slice_in_dim(block, n - width, n, axis=dim), axis, forward)
    high = lax.ppermute(lax.slice_in_dim(block, 0, width, axis=dim), axis, backward)
    return low, high


def deep_extend(block, axis, dim, depth):
    n = block.shape[dim]
    lows, highs = [], []
    need, hop = depth, 1
    while need > 0:
        width = min(n, need)
        low, high = halo_from(block, axis, dim, width, hop)
        lows.insert(0, low)
        highs.append(high)
        need -= width
        hop += 1
    return jnp.concatenate(lows + [block] + highs, axis=dim)


def packed_halo(fields, depths):
    top = max(depths)
    assert top <= fields[0].shape[0] and top <= fields[0].shape[1]
    offs = [sum(depths[:k]) for k in range(len(depths))]
    up = lambda f, d, dim: lax.slice_in_dim(f, f.shape[dim] - d, f.shape[dim], axis=dim)
    down = lambda f, d, dim: lax.slice_in_dim(f, 0, d, axis=dim)
    nb, ng = lax.axis_size("box"), lax.axis_size("group")
    fb, bb = shifted_pairs(nb, 1), [(t, s) for s, t in shifted_pairs(nb, 1)]
    fg, bg = shifted_pairs(ng, 1), [(t, s) for s, t in shifted_pairs(ng, 1)]

    def send(pieces, axis, pairs, dim):
        msg = jnp.concatenate(pieces, axis=dim)
        if not pairs:
            return jnp.zeros_like(msg)
        return lax.ppermute(msg, axis, pairs)

    xl = send([up(f, d, 0) for f, d in zip(fields, depths)], "box", fb, 0)
    xh = send([down(f, d, 0) for f, d in zip(fields, depths)], "box", bb, 0)
    yl = send([up(f, d, 1) for f, d in zip(fields, depths)], "group", fg, 1)
    yh = send([down(f, d, 1) for f, d in zip(fields, depths)], "group", bg, 1)
    width = yl.shape[1]
    low = send([up(yl, top, 0), up(yh, top, 0)], "box", fb, 1)
    high = send([down(yl, top, 0), down(yh, top, 0)], "box", bb, 1)
    out = []
    for f, d, o in zip(fields, depths, offs):
        ys = slice(o, o + d)
        ys2 = slice(width + o, width + o + d)
        rows = [
            jnp.concatenate([low[top - d:, ys], xl[o:o + d], low[top - d:, ys2]], axis=1),
            jnp.concatenate([yl[:, ys], f, yh[:, ys]], axis=1),
            jnp.concatenate([high[:d, ys], xh[o:o + d], high[:d, ys2]], axis=1),
        ]
        out.append(jnp.concatenate(rows, axis=0))
    return out


def shift_z(field, side):
    zeros = jnp.zeros_like(field[:, :, :1])
    if side < 0:
        return jnp.concatenate([zeros, field[:, :, :-1]], axis=2)
    return jnp.concatenate([field[:, :, 1:], zeros], axis=2)


def padded_neighbours(padded):
    return [
        padded[:-2, 1:-1, 1:-1],
        padded[2:, 1:-1, 1:-1],
        padded[1:-1, :-2, 1:-1],
        padded[1:-1, 2:, 1:-1],
        padded[1:-1, 1:-1, :-2],
        padded[1:-1, 1:-1, 2:],
    ]


def coefs_of(field, nears):
    return [jnp.where(near > 0, 2.0 * field * near / (field + near), field) for near in nears]


def apply_op(field, nears, coefs):
    total = jnp.zeros_like(field)
    for coef, near in zip(coefs, nears):
        total = total + coef * (field - near)
    return total


def group_matrix(n, k):
    rows = lax.broadcasted_iota(jnp.int32, (n, n // k), 0) // k
    cols = lax.broadcasted_iota(jnp.int32, (n, n // k), 1)
    return (rows == cols).astype(jnp.float32)


def block_mean(field):
    sx, sy, sz = field.shape
    fx = field.reshape(sx // 4, 4, sy, sz).sum(axis=1)
    fz = jnp.einsum("xyz,zc->xyc", fx, group_matrix(sz, 4), precision=HIGHEST)
    fy = jnp.einsum("xyc,yb->xbc", fz, group_matrix(sy, 4), precision=HIGHEST)
    return fy * (1.0 / 64.0)


def expand(coarse, shape):
    sx, sy, sz = shape
    cz = jnp.einsum("xbc,zc->xbz", coarse, group_matrix(sz, 4), precision=HIGHEST)
    cy = jnp.einsum("xbz,yb->xyz", cz, group_matrix(sy, 4), precision=HIGHEST)
    return jnp.broadcast_to(cy[:, None], (sx // 4, 4, sy, sz)).reshape(sx, sy, sz)


def inside_mask(shape, depth, totals):
    ex, ey, ez = shape
    cx, cy = ex - 2 * depth, ey - 2 * depth
    gx = lax.axis_index("box") * cx - depth + lax.broadcasted_iota(jnp.int32, shape, 0)
    gy = lax.axis_index("group") * cy - depth + lax.broadcasted_iota(jnp.int32, shape, 1)
    return (gx >= 0) & (gx < totals[0]) & (gy >= 0) & (gy < totals[1])


def chebyshev_local(rhs_c, b_c):
    depth = CHEB
    cx, cy, cz = rhs_c.shape
    both = jnp.stack([b_c, rhs_c])
    both = deep_extend(both, "group", 2, depth)
    both = deep_extend(both, "box", 1, depth)
    b_ext, rhs_ext = both[0], both[1]
    totals = (cx * lax.axis_size("box"), cy * lax.axis_size("group"))
    inside = inside_mask(b_ext.shape, depth, totals)
    coefs = [c * 0.0625 for c in coefs_of(b_ext, padded_neighbours(jnp.pad(b_ext, 1)))]
    diag = sum(coefs)
    inv_diag = jnp.where(inside, 1.0 / jnp.where(inside, diag, 1.0), 0.0)

    low, high = (0.05, 2.0)
    theta = (high + low) / 2.0
    delta = (high - low) / 2.0
    sigma = theta / delta
    rho = 1.0 / sigma
    solution = jnp.zeros_like(rhs_ext)
    remain = jnp.where(inside, rhs_ext, 0.0)
    direction = remain * inv_diag / theta
    for step in range(CHEB):
        solution = solution + direction
        if step + 1 < CHEB:
            nears = padded_neighbours(jnp.pad(direction, 1))
            remain = remain - apply_op(direction, nears, coefs)
            rho_next = 1.0 / (2.0 * sigma - rho)
            direction = rho_next * rho * direction + 2.0 * rho_next / delta * remain * inv_diag
            rho = rho_next
    return solution[depth:depth + cx, depth:depth + cy]


def grid_mask(shape, depth, axes, totals):
    inside = None
    for dim, (axis, total) in enumerate(zip(axes, totals)):
        own = shape[dim] - 2 * depth
        g = lax.axis_index(axis) * own - depth + lax.broadcasted_iota(jnp.int32, shape, dim)
        ok = (g >= 0) & (g < total)
        inside = ok if inside is None else inside & ok
    return inside


def shared_faces(b):
    def face(a, n):
        return jnp.where((a > 0) & (n > 0), 2.0 * a * n / (a + n), a + n)

    nears = padded_neighbours(jnp.pad(b, 1))
    lx, ly, lz = face(b, nears[0]), face(b, nears[2]), face(b, nears[4])
    hx = jnp.pad(lx, ((0, 1), (0, 0), (0, 0)))[1:]
    hy = jnp.pad(ly, ((0, 0), (0, 1), (0, 0)))[:, 1:]
    hz = jnp.pad(lz, ((0, 0), (0, 0), (0, 1)))[:, :, 1:]
    top = lax.broadcasted_iota(jnp.int32, b.shape, 2) == b.shape[2] - 1
    return [lx, hx, ly, hy, lz, jnp.where(top, b, hz)]


def low_faces(b):
    faces = []
    for dim in range(3):
        n = b.shape[dim]
        lo = lax.slice_in_dim(b, 0, n - 1, axis=dim)
        hi = lax.slice_in_dim(b, 1, n, axis=dim)
        inner = jnp.where((lo > 0) & (hi > 0), 2.0 * hi * lo / (hi + lo), hi + lo)
        faces.append(jnp.concatenate([lax.slice_in_dim(b, 0, 1, axis=dim), inner], axis=dim))
    return faces


def face_pairs(b, faces):
    pairs = []
    for dim, lo in enumerate(faces):
        n = b.shape[dim]
        hi = jnp.concatenate(
            [lax.slice_in_dim(lo, 1, n, axis=dim), lax.slice_in_dim(b, n - 1, n, axis=dim)], axis=dim
        )
        pairs += [lo, hi]
    return pairs


def per_device(right_side, inv_density, pressure):
    depth = SWEEPS + 1
    sx, sy, sz = pressure.shape
    rhs_e, b_e, fine = packed_halo([right_side, inv_density, pressure], [depth - 1, depth, depth])
    rhs_e = jnp.pad(rhs_e, ((1, 1), (1, 1), (0, 0)))
    rhs_e, b_e, fine = lax.optimization_barrier((rhs_e, b_e, fine))
    totals = (sx * lax.axis_size("box"), sy * lax.axis_size("group"))
    inside = grid_mask(fine.shape, depth, ("box", "group"), totals)
    coefs = shared_faces(b_e)
    diag = sum(coefs)
    for sweep in range(SWEEPS):
        step = 2.0 / 3.0 * (rhs_e - apply_op(fine, padded_neighbours(jnp.pad(fine, 1)), coefs)) / diag
        fine = jnp.where(inside, fine + step, 0.0)
    res = rhs_e - apply_op(fine, padded_neighbours(jnp.pad(fine, 1)), coefs)
    own = (slice(depth, depth + sx), slice(depth, depth + sy))
    fine, res = fine[own], res[own]
    coarse_rhs = block_mean(res)
    coarse_b = block_mean(inv_density)
    corr = chebyshev_local(coarse_rhs, coarse_b)
    return fine + expand(corr, fine.shape)


def solution(mesh):
    return jax.shard_map(
        per_device,
        mesh=mesh,
        in_specs=(P("box", "group", None), P("box", "group", None), P("box", "group", None)),
        out_specs=P("box", "group", None),
        check_vma=False,
    )
```

```python
import jax
import jax.numpy as jnp
from jax import lax
from jax.sharding import PartitionSpec as P

SWEEPS = 2
CHEB = 8
HIGHEST = lax.Precision.HIGHEST


def shifted_pairs(count, hop):
    return [(i, i + hop) for i in range(count - hop)]


def halo_from(block, axis, dim, width, hop):
    count = lax.axis_size(axis)
    n = block.shape[dim]
    if hop >= count:
        shape = list(block.shape)
        shape[dim] = width
        zeros = jnp.zeros(shape, block.dtype)
        return zeros, zeros
    forward = shifted_pairs(count, hop)
    backward = [(t, s) for s, t in forward]
    low = lax.ppermute(lax.slice_in_dim(block, n - width, n, axis=dim), axis, forward)
    high = lax.ppermute(lax.slice_in_dim(block, 0, width, axis=dim), axis, backward)
    return low, high


def deep_extend(block, axis, dim, depth):
    n = block.shape[dim]
    lows, highs = [], []
    need, hop = depth, 1
    while need > 0:
        width = min(n, need)
        low, high = halo_from(block, axis, dim, width, hop)
        lows.insert(0, low)
        highs.append(high)
        need -= width
        hop += 1
    return jnp.concatenate(lows + [block] + highs, axis=dim)


def packed_halo(fields, depths):
    top = max(depths)
    assert top <= fields[0].shape[0] and top <= fields[0].shape[1]
    offs = [sum(depths[:k]) for k in range(len(depths))]
    up = lambda f, d, dim: lax.slice_in_dim(f, f.shape[dim] - d, f.shape[dim], axis=dim)
    down = lambda f, d, dim: lax.slice_in_dim(f, 0, d, axis=dim)
    nb, ng = lax.axis_size("box"), lax.axis_size("group")
    fb, bb = shifted_pairs(nb, 1), [(t, s) for s, t in shifted_pairs(nb, 1)]
    fg, bg = shifted_pairs(ng, 1), [(t, s) for s, t in shifted_pairs(ng, 1)]

    def send(pieces, axis, pairs, dim):
        msg = jnp.concatenate(pieces, axis=dim)
        if not pairs:
            return jnp.zeros_like(msg)
        return lax.ppermute(msg, axis, pairs)

    xl = send([up(f, d, 0) for f, d in zip(fields, depths)], "box", fb, 0)
    xh = send([down(f, d, 0) for f, d in zip(fields, depths)], "box", bb, 0)
    yl = send([up(f, d, 1) for f, d in zip(fields, depths)], "group", fg, 1)
    yh = send([down(f, d, 1) for f, d in zip(fields, depths)], "group", bg, 1)
    width = yl.shape[1]
    low = send([up(yl, top, 0), up(yh, top, 0)], "box", fb, 1)
    high = send([down(yl, top, 0), down(yh, top, 0)], "box", bb, 1)
    out = []
    for f, d, o in zip(fields, depths, offs):
        ys = slice(o, o + d)
        ys2 = slice(width + o, width + o + d)
        rows = [
            jnp.concatenate([low[top - d:, ys], xl[o:o + d], low[top - d:, ys2]], axis=1),
            jnp.concatenate([yl[:, ys], f, yh[:, ys]], axis=1),
            jnp.concatenate([high[:d, ys], xh[o:o + d], high[:d, ys2]], axis=1),
        ]
        out.append(jnp.concatenate(rows, axis=0))
    return out


def shift_z(field, side):
    zeros = jnp.zeros_like(field[:, :, :1])
    if side < 0:
        return jnp.concatenate([zeros, field[:, :, :-1]], axis=2)
    return jnp.concatenate([field[:, :, 1:], zeros], axis=2)


def padded_neighbours(padded):
    return [
        padded[:-2, 1:-1, 1:-1],
        padded[2:, 1:-1, 1:-1],
        padded[1:-1, :-2, 1:-1],
        padded[1:-1, 2:, 1:-1],
        padded[1:-1, 1:-1, :-2],
        padded[1:-1, 1:-1, 2:],
    ]


def coefs_of(field, nears):
    return [jnp.where(near > 0, 2.0 * field * near / (field + near), field) for near in nears]


def apply_op(field, nears, coefs):
    total = jnp.zeros_like(field)
    for coef, near in zip(coefs, nears):
        total = total + coef * (field - near)
    return total


def group_matrix(n, k):
    rows = lax.broadcasted_iota(jnp.int32, (n, n // k), 0) // k
    cols = lax.broadcasted_iota(jnp.int32, (n, n // k), 1)
    return (rows == cols).astype(jnp.float32)


def block_mean(field):
    sx, sy, sz = field.shape
    fx = field.reshape(sx // 4, 4, sy, sz).sum(axis=1)
    fz = jnp.einsum("xyz,zc->xyc", fx, group_matrix(sz, 4), precision=HIGHEST)
    fy = jnp.einsum("xyc,yb->xbc", fz, group_matrix(sy, 4), precision=HIGHEST)
    return fy * (1.0 / 64.0)


def expand(coarse, shape):
    sx, sy, sz = shape
    cz = jnp.einsum("xbc,zc->xbz", coarse, group_matrix(sz, 4), precision=HIGHEST)
    cy = jnp.einsum("xbz,yb->xyz", cz, group_matrix(sy, 4), precision=HIGHEST)
    return jnp.broadcast_to(cy[:, None], (sx // 4, 4, sy, sz)).reshape(sx, sy, sz)


def inside_mask(shape, depth, totals):
    ex, ey, ez = shape
    cx, cy = ex - 2 * depth, ey - 2 * depth
    gx = lax.axis_index("box") * cx - depth + lax.broadcasted_iota(jnp.int32, shape, 0)
    gy = lax.axis_index("group") * cy - depth + lax.broadcasted_iota(jnp.int32, shape, 1)
    return (gx >= 0) & (gx < totals[0]) & (gy >= 0) & (gy < totals[1])


def chebyshev_local(rhs_c, b_c):
    depth = CHEB
    cx, cy, cz = rhs_c.shape
    both = jnp.stack([b_c, rhs_c])
    both = deep_extend(both, "box", 1, depth)
    both = deep_extend(both, "group", 2, depth)
    b_ext, rhs_ext = both[0], both[1]
    totals = (cx * lax.axis_size("box"), cy * lax.axis_size("group"))
    inside = inside_mask(b_ext.shape, depth, totals)
    coefs = [c * 0.0625 for c in coefs_of(b_ext, padded_neighbours(jnp.pad(b_ext, 1)))]
    diag = sum(coefs)
    inv_diag = jnp.where(inside, 1.0 / jnp.where(inside, diag, 1.0), 0.0)

    low, high = (0.05, 2.0)
    theta = (high + low) / 2.0
    delta = (high - low) / 2.0
    sigma = theta / delta
    rho = 1.0 / sigma
    solution = jnp.zeros_like(rhs_ext)
    remain = jnp.where(inside, rhs_ext, 0.0)
    direction = remain * inv_diag / theta
    for step in range(CHEB):
        solution = solution + direction
        if step + 1 < CHEB:
            nears = padded_neighbours(jnp.pad(direction, 1))
            remain = remain - apply_op(direction, nears, coefs)
            rho_next = 1.0 / (2.0 * sigma - rho)
            direction = rho_next * rho * direction + 2.0 * rho_next / delta * remain * inv_diag
            rho = rho_next
    return solution[depth:depth + cx, depth:depth + cy]


def grid_mask(shape, depth, axes, totals):
    inside = None
    for dim, (axis, total) in enumerate(zip(axes, totals)):
        own = shape[dim] - 2 * depth
        g = lax.axis_index(axis) * own - depth + lax.broadcasted_iota(jnp.int32, shape, dim)
        ok = (g >= 0) & (g < total)
        inside = ok if inside is None else inside & ok
    return inside


def shared_faces(b):
    def face(a, n):
        return jnp.where((a > 0) & (n > 0), 2.0 * a * n / (a + n), a + n)

    nears = padded_neighbours(jnp.pad(b, 1))
    lx, ly, lz = face(b, nears[0]), face(b, nears[2]), face(b, nears[4])
    hx = jnp.pad(lx, ((0, 1), (0, 0), (0, 0)))[1:]
    hy = jnp.pad(ly, ((0, 0), (0, 1), (0, 0)))[:, 1:]
    hz = jnp.pad(lz, ((0, 0), (0, 0), (0, 1)))[:, :, 1:]
    top = lax.broadcasted_iota(jnp.int32, b.shape, 2) == b.shape[2] - 1
    return [lx, hx, ly, hy, lz, jnp.where(top, b, hz)]


def low_faces(b):
    faces = []
    for dim in range(3):
        n = b.shape[dim]
        lo = lax.slice_in_dim(b, 0, n - 1, axis=dim)
        hi = lax.slice_in_dim(b, 1, n, axis=dim)
        inner = jnp.where((lo > 0) & (hi > 0), 2.0 * hi * lo / (hi + lo), hi + lo)
        faces.append(jnp.concatenate([lax.slice_in_dim(b, 0, 1, axis=dim), inner], axis=dim))
    return faces


def face_pairs(b, faces):
    pairs = []
    for dim, lo in enumerate(faces):
        n = b.shape[dim]
        hi = jnp.concatenate(
            [lax.slice_in_dim(lo, 1, n, axis=dim), lax.slice_in_dim(b, n - 1, n, axis=dim)], axis=dim
        )
        pairs += [lo, hi]
    return pairs


def per_device(right_side, inv_density, pressure):
    depth = SWEEPS + 1
    sx, sy, sz = pressure.shape
    rhs_e, b_e, fine = packed_halo([right_side, inv_density, pressure], [depth - 1, depth, depth])
    rhs_e = jnp.pad(rhs_e, ((1, 1), (1, 1), (0, 0)))
    rhs_e, b_e, fine = lax.optimization_barrier((rhs_e, b_e, fine))
    totals = (sx * lax.axis_size("box"), sy * lax.axis_size("group"))
    inside = grid_mask(fine.shape, depth, ("box", "group"), totals)
    coefs = shared_faces(b_e)
    diag = sum(coefs)
    for sweep in range(SWEEPS):
        step = 2.0 / 3.0 * (rhs_e - apply_op(fine, padded_neighbours(jnp.pad(fine, 1)), coefs)) / diag
        fine = jnp.where(inside, fine + step, 0.0)
    own = (slice(depth, depth + sx), slice(depth, depth + sy))
    core = fine[own]
    nears = [
        fine[depth - 1:depth - 1 + sx, depth:depth + sy],
        fine[depth + 1:depth + 1 + sx, depth:depth + sy],
        fine[depth:depth + sx, depth - 1:depth - 1 + sy],
        fine[depth:depth + sx, depth + 1:depth + 1 + sy],
        shift_z(core, -1),
        shift_z(core, 1),
    ]
    res = right_side - apply_op(core, nears, [c[own] for c in coefs])
    fine, res = lax.optimization_barrier((core, res))
    coarse_rhs = block_mean(res)
    coarse_b = block_mean(inv_density)
    corr = chebyshev_local(coarse_rhs, coarse_b)
    return fine + expand(corr, fine.shape)


def solution(mesh):
    return jax.shard_map(
        per_device,
        mesh=mesh,
        in_specs=(P("box", "group", None), P("box", "group", None), P("box", "group", None)),
        out_specs=P("box", "group", None),
        check_vma=False,
    )
```

```python
import jax
import jax.numpy as jnp
from jax import lax
from jax.sharding import PartitionSpec as P

SWEEPS = 2
CHEB = 8
HIGHEST = lax.Precision.HIGHEST


def shifted_pairs(count, hop):
    return [(i, i + hop) for i in range(count - hop)]


def halo_from(block, axis, dim, width, hop):
    count = lax.axis_size(axis)
    n = block.shape[dim]
    if hop >= count:
        shape = list(block.shape)
        shape[dim] = width
        zeros = jnp.zeros(shape, block.dtype)
        return zeros, zeros
    forward = shifted_pairs(count, hop)
    backward = [(t, s) for s, t in forward]
    low = lax.ppermute(lax.slice_in_dim(block, n - width, n, axis=dim), axis, forward)
    high = lax.ppermute(lax.slice_in_dim(block, 0, width, axis=dim), axis, backward)
    return low, high


def deep_extend(block, axis, dim, depth):
    n = block.shape[dim]
    lows, highs = [], []
    need, hop = depth, 1
    while need > 0:
        width = min(n, need)
        low, high = halo_from(block, axis, dim, width, hop)
        lows.insert(0, low)
        highs.append(high)
        need -= width
        hop += 1
    return jnp.concatenate(lows + [block] + highs, axis=dim)


def packed_halo(fields, depths):
    top = max(depths)
    assert top <= fields[0].shape[0] and top <= fields[0].shape[1]
    offs = [sum(depths[:k]) for k in range(len(depths))]
    up = lambda f, d, dim: lax.slice_in_dim(f, f.shape[dim] - d, f.shape[dim], axis=dim)
    down = lambda f, d, dim: lax.slice_in_dim(f, 0, d, axis=dim)
    nb, ng = lax.axis_size("box"), lax.axis_size("group")
    fb, bb = shifted_pairs(nb, 1), [(t, s) for s, t in shifted_pairs(nb, 1)]
    fg, bg = shifted_pairs(ng, 1), [(t, s) for s, t in shifted_pairs(ng, 1)]

    def send(pieces, axis, pairs, dim):
        msg = jnp.concatenate(pieces, axis=dim)
        if not pairs:
            return jnp.zeros_like(msg)
        return lax.ppermute(msg, axis, pairs)

    xl = send([up(f, d, 0) for f, d in zip(fields, depths)], "box", fb, 0)
    xh = send([down(f, d, 0) for f, d in zip(fields, depths)], "box", bb, 0)
    yl = send([up(f, d, 1) for f, d in zip(fields, depths)], "group", fg, 1)
    yh = send([down(f, d, 1) for f, d in zip(fields, depths)], "group", bg, 1)
    low = send([up(yl, top, 0), up(yh, top, 0)], "box", fb, 1)
    high = send([down(yl, top, 0), down(yh, top, 0)], "box", bb, 1)
    total = sum(depths)
    out = []
    for f, d, o in zip(fields, depths, offs):
        lo_win = slice(o + d - top, o + d)
        hi_win = slice(o, o + top)
        assert lo_win.start >= 0 and hi_win.stop <= total
        hi_win2 = slice(total + hi_win.start, total + hi_win.stop)
        rows = [
            jnp.concatenate([low[:, lo_win], xl[lo_win], low[:, hi_win2]], axis=1),
            jnp.concatenate([yl[:, lo_win], f, yh[:, hi_win]], axis=1),
            jnp.concatenate([high[:, lo_win], xh[hi_win], high[:, hi_win2]], axis=1),
        ]
        out.append(jnp.concatenate(rows, axis=0))
    return out


def shift_z(field, side):
    zeros = jnp.zeros_like(field[:, :, :1])
    if side < 0:
        return jnp.concatenate([zeros, field[:, :, :-1]], axis=2)
    return jnp.concatenate([field[:, :, 1:], zeros], axis=2)


def padded_neighbours(padded):
    return [
        padded[:-2, 1:-1, 1:-1],
        padded[2:, 1:-1, 1:-1],
        padded[1:-1, :-2, 1:-1],
        padded[1:-1, 2:, 1:-1],
        padded[1:-1, 1:-1, :-2],
        padded[1:-1, 1:-1, 2:],
    ]


def coefs_of(field, nears):
    return [jnp.where(near > 0, 2.0 * field * near / (field + near), field) for near in nears]


def apply_op(field, nears, coefs):
    total = jnp.zeros_like(field)
    for coef, near in zip(coefs, nears):
        total = total + coef * (field - near)
    return total


def group_matrix(n, k):
    rows = lax.broadcasted_iota(jnp.int32, (n, n // k), 0) // k
    cols = lax.broadcasted_iota(jnp.int32, (n, n // k), 1)
    return (rows == cols).astype(jnp.float32)


def block_mean(field):
    sx, sy, sz = field.shape
    fx = field.reshape(sx // 4, 4, sy, sz).sum(axis=1)
    fz = jnp.einsum("xyz,zc->xyc", fx, group_matrix(sz, 4), precision=HIGHEST)
    fy = jnp.einsum("xyc,yb->xbc", fz, group_matrix(sy, 4), precision=HIGHEST)
    return fy * (1.0 / 64.0)


def expand(coarse, shape):
    sx, sy, sz = shape
    cz = jnp.einsum("xbc,zc->xbz", coarse, group_matrix(sz, 4), precision=HIGHEST)
    cy = jnp.einsum("xbz,yb->xyz", cz, group_matrix(sy, 4), precision=HIGHEST)
    return jnp.broadcast_to(cy[:, None], (sx // 4, 4, sy, sz)).reshape(sx, sy, sz)


def inside_mask(shape, depth, totals):
    ex, ey, ez = shape
    cx, cy = ex - 2 * depth, ey - 2 * depth
    gx = lax.axis_index("box") * cx - depth + lax.broadcasted_iota(jnp.int32, shape, 0)
    gy = lax.axis_index("group") * cy - depth + lax.broadcasted_iota(jnp.int32, shape, 1)
    return (gx >= 0) & (gx < totals[0]) & (gy >= 0) & (gy < totals[1])


def chebyshev_local(rhs_c, b_c):
    depth = CHEB
    cx, cy, cz = rhs_c.shape
    both = jnp.stack([b_c, rhs_c])
    both = deep_extend(both, "box", 1, depth)
    both = deep_extend(both, "group", 2, depth)
    b_ext, rhs_ext = both[0], both[1]
    totals = (cx * lax.axis_size("box"), cy * lax.axis_size("group"))
    inside = inside_mask(b_ext.shape, depth, totals)
    coefs = [c * 0.0625 for c in coefs_of(b_ext, padded_neighbours(jnp.pad(b_ext, 1)))]
    diag = sum(coefs)
    inv_diag = jnp.where(inside, 1.0 / jnp.where(inside, diag, 1.0), 0.0)

    low, high = (0.05, 2.0)
    theta = (high + low) / 2.0
    delta = (high - low) / 2.0
    sigma = theta / delta
    rho = 1.0 / sigma
    solution = jnp.zeros_like(rhs_ext)
    remain = jnp.where(inside, rhs_ext, 0.0)
    direction = remain * inv_diag / theta
    for step in range(CHEB):
        solution = solution + direction
        if step + 1 < CHEB:
            nears = padded_neighbours(jnp.pad(direction, 1))
            remain = remain - apply_op(direction, nears, coefs)
            rho_next = 1.0 / (2.0 * sigma - rho)
            direction = rho_next * rho * direction + 2.0 * rho_next / delta * remain * inv_diag
            rho = rho_next
    return solution[depth:depth + cx, depth:depth + cy]


def grid_mask(shape, depth, axes, totals):
    inside = None
    for dim, (axis, total) in enumerate(zip(axes, totals)):
        own = shape[dim] - 2 * depth
        g = lax.axis_index(axis) * own - depth + lax.broadcasted_iota(jnp.int32, shape, dim)
        ok = (g >= 0) & (g < total)
        inside = ok if inside is None else inside & ok
    return inside


def shared_faces(b):
    def face(a, n):
        return jnp.where((a > 0) & (n > 0), 2.0 * a * n / (a + n), a + n)

    nears = padded_neighbours(jnp.pad(b, 1))
    lx, ly, lz = face(b, nears[0]), face(b, nears[2]), face(b, nears[4])
    hx = jnp.pad(lx, ((0, 1), (0, 0), (0, 0)))[1:]
    hy = jnp.pad(ly, ((0, 0), (0, 1), (0, 0)))[:, 1:]
    hz = jnp.pad(lz, ((0, 0), (0, 0), (0, 1)))[:, :, 1:]
    top = lax.broadcasted_iota(jnp.int32, b.shape, 2) == b.shape[2] - 1
    return [lx, hx, ly, hy, lz, jnp.where(top, b, hz)]


def low_faces(b):
    faces = []
    for dim in range(3):
        n = b.shape[dim]
        lo = lax.slice_in_dim(b, 0, n - 1, axis=dim)
        hi = lax.slice_in_dim(b, 1, n, axis=dim)
        inner = jnp.where((lo > 0) & (hi > 0), 2.0 * hi * lo / (hi + lo), hi + lo)
        faces.append(jnp.concatenate([lax.slice_in_dim(b, 0, 1, axis=dim), inner], axis=dim))
    return faces


def face_pairs(b, faces):
    pairs = []
    for dim, lo in enumerate(faces):
        n = b.shape[dim]
        hi = jnp.concatenate(
            [lax.slice_in_dim(lo, 1, n, axis=dim), lax.slice_in_dim(b, n - 1, n, axis=dim)], axis=dim
        )
        pairs += [lo, hi]
    return pairs


def per_device(right_side, inv_density, pressure):
    depth = SWEEPS + 1
    sx, sy, sz = pressure.shape
    b_e, rhs_e, fine = packed_halo([inv_density, right_side, pressure], [depth, depth - 1, depth])
    rhs_e, b_e, fine = lax.optimization_barrier((rhs_e, b_e, fine))
    totals = (sx * lax.axis_size("box"), sy * lax.axis_size("group"))
    inside = grid_mask(fine.shape, depth, ("box", "group"), totals)
    coefs = shared_faces(b_e)
    diag = sum(coefs)
    for sweep in range(SWEEPS):
        step = 2.0 / 3.0 * (rhs_e - apply_op(fine, padded_neighbours(jnp.pad(fine, 1)), coefs)) / diag
        fine = jnp.where(inside, fine + step, 0.0)
    own = (slice(depth, depth + sx), slice(depth, depth + sy))
    core = fine[own]
    nears = [
        fine[depth - 1:depth - 1 + sx, depth:depth + sy],
        fine[depth + 1:depth + 1 + sx, depth:depth + sy],
        fine[depth:depth + sx, depth - 1:depth - 1 + sy],
        fine[depth:depth + sx, depth + 1:depth + 1 + sy],
        shift_z(core, -1),
        shift_z(core, 1),
    ]
    res = right_side - apply_op(core, nears, [c[own] for c in coefs])
    fine, res = lax.optimization_barrier((core, res))
    coarse_rhs = block_mean(res)
    coarse_b = block_mean(inv_density)
    corr = chebyshev_local(coarse_rhs, coarse_b)
    return fine + expand(corr, fine.shape)


def solution(mesh):
    return jax.shard_map(
        per_device,
        mesh=mesh,
        in_specs=(P("box", "group", None), P("box", "group", None), P("box", "group", None)),
        out_specs=P("box", "group", None),
        check_vma=False,
    )
```

```python
import jax
import jax.numpy as jnp
from jax import lax
from jax.sharding import PartitionSpec as P

SWEEPS = 2
CHEB = 8
HIGHEST = lax.Precision.HIGHEST


def shifted_pairs(count, hop):
    return [(i, i + hop) for i in range(count - hop)]


def halo_from(block, axis, dim, width, hop):
    count = lax.axis_size(axis)
    n = block.shape[dim]
    if hop >= count:
        shape = list(block.shape)
        shape[dim] = width
        zeros = jnp.zeros(shape, block.dtype)
        return zeros, zeros
    forward = shifted_pairs(count, hop)
    backward = [(t, s) for s, t in forward]
    low = lax.ppermute(lax.slice_in_dim(block, n - width, n, axis=dim), axis, forward)
    high = lax.ppermute(lax.slice_in_dim(block, 0, width, axis=dim), axis, backward)
    return low, high


def deep_extend(block, axis, dim, depth):
    n = block.shape[dim]
    lows, highs = [], []
    need, hop = depth, 1
    while need > 0:
        width = min(n, need)
        low, high = halo_from(block, axis, dim, width, hop)
        lows.insert(0, low)
        highs.append(high)
        need -= width
        hop += 1
    return jnp.concatenate(lows + [block] + highs, axis=dim)


def packed_halo(fields, depths):
    top = max(depths)
    assert top <= fields[0].shape[0] and top <= fields[0].shape[1]
    offs = [sum(depths[:k]) for k in range(len(depths))]
    up = lambda f, d, dim: lax.slice_in_dim(f, f.shape[dim] - d, f.shape[dim], axis=dim)
    down = lambda f, d, dim: lax.slice_in_dim(f, 0, d, axis=dim)
    nb, ng = lax.axis_size("box"), lax.axis_size("group")
    fb, bb = shifted_pairs(nb, 1), [(t, s) for s, t in shifted_pairs(nb, 1)]
    fg, bg = shifted_pairs(ng, 1), [(t, s) for s, t in shifted_pairs(ng, 1)]

    def send(pieces, axis, pairs, dim):
        msg = jnp.concatenate(pieces, axis=dim)
        if not pairs:
            return jnp.zeros_like(msg)
        return lax.ppermute(msg, axis, pairs)

    xl = send([up(f, d, 0) for f, d in zip(fields, depths)], "box", fb, 0)
    xh = send([down(f, d, 0) for f, d in zip(fields, depths)], "box", bb, 0)
    yl = send([up(f, d, 1) for f, d in zip(fields, depths)], "group", fg, 1)
    yh = send([down(f, d, 1) for f, d in zip(fields, depths)], "group", bg, 1)
    low = send([up(yl, top, 0), up(yh, top, 0)], "box", fb, 1)
    high = send([down(yl, top, 0), down(yh, top, 0)], "box", bb, 1)
    total = sum(depths)
    out = []
    for f, d, o in zip(fields, depths, offs):
        lo_win = slice(o + d - top, o + d)
        hi_win = slice(o, o + top)
        assert lo_win.start >= 0 and hi_win.stop <= total
        hi_win2 = slice(total + hi_win.start, total + hi_win.stop)
        rows = [
            jnp.concatenate([low[:, lo_win], xl[lo_win], low[:, hi_win2]], axis=1),
            jnp.concatenate([yl[:, lo_win], f, yh[:, hi_win]], axis=1),
            jnp.concatenate([high[:, lo_win], xh[hi_win], high[:, hi_win2]], axis=1),
        ]
        out.append(jnp.concatenate(rows, axis=0))
    return out


def shift_z(field, side):
    zeros = jnp.zeros_like(field[:, :, :1])
    if side < 0:
        return jnp.concatenate([zeros, field[:, :, :-1]], axis=2)
    return jnp.concatenate([field[:, :, 1:], zeros], axis=2)


def padded_neighbours(padded):
    return [
        padded[:-2, 1:-1, 1:-1],
        padded[2:, 1:-1, 1:-1],
        padded[1:-1, :-2, 1:-1],
        padded[1:-1, 2:, 1:-1],
        padded[1:-1, 1:-1, :-2],
        padded[1:-1, 1:-1, 2:],
    ]


def coefs_of(field, nears):
    return [jnp.where(near > 0, 2.0 * field * near / (field + near), field) for near in nears]


def apply_op(field, nears, coefs):
    total = jnp.zeros_like(field)
    for coef, near in zip(coefs, nears):
        total = total + coef * (field - near)
    return total


def group_matrix(n, k):
    rows = lax.broadcasted_iota(jnp.int32, (n, n // k), 0) // k
    cols = lax.broadcasted_iota(jnp.int32, (n, n // k), 1)
    return (rows == cols).astype(jnp.float32)


def block_mean(field):
    sx, sy, sz = field.shape
    fx = field.reshape(sx // 4, 4, sy, sz).sum(axis=1)
    fz = jnp.einsum("xyz,zc->xyc", fx, group_matrix(sz, 4), precision=HIGHEST)
    fy = jnp.einsum("xyc,yb->xbc", fz, group_matrix(sy, 4), precision=HIGHEST)
    return fy * (1.0 / 64.0)


def expand(coarse, shape):
    sx, sy, sz = shape
    cz = jnp.einsum("xbc,zc->xbz", coarse, group_matrix(sz, 4), precision=HIGHEST)
    cy = jnp.einsum("xbz,yb->xyz", cz, group_matrix(sy, 4), precision=HIGHEST)
    return jnp.broadcast_to(cy[:, None], (sx // 4, 4, sy, sz)).reshape(sx, sy, sz)


def inside_mask(shape, depth, totals):
    ex, ey, ez = shape
    cx, cy = ex - 2 * depth, ey - 2 * depth
    gx = lax.axis_index("box") * cx - depth + lax.broadcasted_iota(jnp.int32, shape, 0)
    gy = lax.axis_index("group") * cy - depth + lax.broadcasted_iota(jnp.int32, shape, 1)
    return (gx >= 0) & (gx < totals[0]) & (gy >= 0) & (gy < totals[1])


def chebyshev_local(rhs_c, b_c):
    depth = CHEB
    cx, cy, cz = rhs_c.shape
    both = jnp.stack([b_c, rhs_c])
    both = deep_extend(both, "box", 1, depth)
    both = deep_extend(both, "group", 2, depth)
    b_ext, rhs_ext = both[0], both[1]
    totals = (cx * lax.axis_size("box"), cy * lax.axis_size("group"))
    inside = inside_mask(b_ext.shape, depth, totals)
    coefs = [c * 0.0625 for c in coefs_of(b_ext, padded_neighbours(jnp.pad(b_ext, 1)))]
    diag = sum(coefs)
    inv_diag = jnp.where(inside, 1.0 / jnp.where(inside, diag, 1.0), 0.0)

    low, high = (0.05, 2.0)
    theta = (high + low) / 2.0
    delta = (high - low) / 2.0
    sigma = theta / delta
    rho = 1.0 / sigma
    solution = jnp.zeros_like(rhs_ext)
    remain = jnp.where(inside, rhs_ext, 0.0)
    direction = remain * inv_diag / theta
    for step in range(CHEB):
        solution = solution + direction
        if step + 1 < CHEB:
            nears = padded_neighbours(jnp.pad(direction, 1))
            remain = remain - apply_op(direction, nears, coefs)
            rho_next = 1.0 / (2.0 * sigma - rho)
            direction = rho_next * rho * direction + 2.0 * rho_next / delta * remain * inv_diag
            rho = rho_next
    return solution[depth:depth + cx, depth:depth + cy]


def grid_mask(shape, depth, axes, totals):
    inside = None
    for dim, (axis, total) in enumerate(zip(axes, totals)):
        own = shape[dim] - 2 * depth
        g = lax.axis_index(axis) * own - depth + lax.broadcasted_iota(jnp.int32, shape, dim)
        ok = (g >= 0) & (g < total)
        inside = ok if inside is None else inside & ok
    return inside


def shared_faces(b):
    def face(a, n):
        return jnp.where((a > 0) & (n > 0), 2.0 * a * n / (a + n), a + n)

    nears = padded_neighbours(jnp.pad(b, 1))
    lx, ly, lz = face(b, nears[0]), face(b, nears[2]), face(b, nears[4])
    hx = jnp.pad(lx, ((0, 1), (0, 0), (0, 0)))[1:]
    hy = jnp.pad(ly, ((0, 0), (0, 1), (0, 0)))[:, 1:]
    hz = jnp.pad(lz, ((0, 0), (0, 0), (0, 1)))[:, :, 1:]
    top = lax.broadcasted_iota(jnp.int32, b.shape, 2) == b.shape[2] - 1
    return [lx, hx, ly, hy, lz, jnp.where(top, b, hz)]


def low_faces(b):
    faces = []
    for dim in range(3):
        n = b.shape[dim]
        lo = lax.slice_in_dim(b, 0, n - 1, axis=dim)
        hi = lax.slice_in_dim(b, 1, n, axis=dim)
        inner = jnp.where((lo > 0) & (hi > 0), 2.0 * hi * lo / (hi + lo), hi + lo)
        faces.append(jnp.concatenate([lax.slice_in_dim(b, 0, 1, axis=dim), inner], axis=dim))
    return faces


def face_pairs(b, faces):
    pairs = []
    for dim, lo in enumerate(faces):
        n = b.shape[dim]
        hi = jnp.concatenate(
            [lax.slice_in_dim(lo, 1, n, axis=dim), lax.slice_in_dim(b, n - 1, n, axis=dim)], axis=dim
        )
        pairs += [lo, hi]
    return pairs


def per_device(right_side, inv_density, pressure):
    depth = SWEEPS + 1
    sx, sy, sz = pressure.shape
    b_e, rhs_e, fine = packed_halo([inv_density, right_side, pressure], [depth, depth - 1, depth])
    rhs_e, b_e, fine = lax.optimization_barrier((rhs_e, b_e, fine))
    totals = (sx * lax.axis_size("box"), sy * lax.axis_size("group"))
    inside = grid_mask(fine.shape, depth, ("box", "group"), totals)
    coefs = shared_faces(b_e)
    diag = sum(coefs)
    ex = fine.shape[0]
    for sweep in range(SWEEPS):
        part = slice(sweep + 1, ex - sweep - 1)
        prev = fine
        centre = prev[1:-1]
        rows = jnp.pad(centre, ((0, 0), (1, 1), (0, 0)))
        nears = [prev[:-2], prev[2:], rows[:, :-2], rows[:, 2:], shift_z(centre, -1), shift_z(centre, 1)]
        cut = [c[part] for c in coefs]
        step = 2.0 / 3.0 * (rhs_e[part] - apply_op(centre, nears, cut)) / diag[part]
        fine = jnp.where(inside[part], centre + step, 0.0)
    first = depth - SWEEPS
    own = (slice(depth, depth + sx), slice(depth, depth + sy))
    core = fine[first:first + sx, depth:depth + sy]
    nears = [
        fine[first - 1:first - 1 + sx, depth:depth + sy],
        fine[first + 1:first + 1 + sx, depth:depth + sy],
        fine[first:first + sx, depth - 1:depth - 1 + sy],
        fine[first:first + sx, depth + 1:depth + 1 + sy],
        shift_z(core, -1),
        shift_z(core, 1),
    ]
    res = right_side - apply_op(core, nears, [c[own] for c in coefs])
    fine, res = lax.optimization_barrier((core, res))
    coarse_rhs = block_mean(res)
    coarse_b = block_mean(inv_density)
    corr = chebyshev_local(coarse_rhs, coarse_b)
    return fine + expand(corr, fine.shape)


def solution(mesh):
    return jax.shard_map(
        per_device,
        mesh=mesh,
        in_specs=(P("box", "group", None), P("box", "group", None), P("box", "group", None)),
        out_specs=P("box", "group", None),
        check_vma=False,
    )
```

```python
import jax
import jax.numpy as jnp
from jax import lax
from jax.sharding import PartitionSpec as P

SWEEPS = 2
CHEB = 8
HIGHEST = lax.Precision.HIGHEST


def shifted_pairs(count, hop):
    return [(i, i + hop) for i in range(count - hop)]


def halo_from(block, axis, dim, width, hop):
    count = lax.axis_size(axis)
    n = block.shape[dim]
    if hop >= count:
        shape = list(block.shape)
        shape[dim] = width
        zeros = jnp.zeros(shape, block.dtype)
        return zeros, zeros
    forward = shifted_pairs(count, hop)
    backward = [(t, s) for s, t in forward]
    low = lax.ppermute(lax.slice_in_dim(block, n - width, n, axis=dim), axis, forward)
    high = lax.ppermute(lax.slice_in_dim(block, 0, width, axis=dim), axis, backward)
    return low, high


def deep_extend(block, axis, dim, depth):
    n = block.shape[dim]
    lows, highs = [], []
    need, hop = depth, 1
    while need > 0:
        width = min(n, need)
        low, high = halo_from(block, axis, dim, width, hop)
        lows.insert(0, low)
        highs.append(high)
        need -= width
        hop += 1
    return jnp.concatenate(lows + [block] + highs, axis=dim)


def packed_halo(fields, depths):
    top = max(depths)
    assert top <= fields[0].shape[0] and top <= fields[0].shape[1]
    offs = [sum(depths[:k]) for k in range(len(depths))]
    up = lambda f, d, dim: lax.slice_in_dim(f, f.shape[dim] - d, f.shape[dim], axis=dim)
    down = lambda f, d, dim: lax.slice_in_dim(f, 0, d, axis=dim)
    nb, ng = lax.axis_size("box"), lax.axis_size("group")
    fb, bb = shifted_pairs(nb, 1), [(t, s) for s, t in shifted_pairs(nb, 1)]
    fg, bg = shifted_pairs(ng, 1), [(t, s) for s, t in shifted_pairs(ng, 1)]

    def send(pieces, axis, pairs, dim):
        msg = jnp.concatenate(pieces, axis=dim)
        if not pairs:
            return jnp.zeros_like(msg)
        return lax.ppermute(msg, axis, pairs)

    xl = send([up(f, d, 0) for f, d in zip(fields, depths)], "box", fb, 0)
    xh = send([down(f, d, 0) for f, d in zip(fields, depths)], "box", bb, 0)
    yl = send([up(f, d, 1) for f, d in zip(fields, depths)], "group", fg, 1)
    yh = send([down(f, d, 1) for f, d in zip(fields, depths)], "group", bg, 1)
    low = send([up(yl, top, 0), up(yh, top, 0)], "box", fb, 1)
    high = send([down(yl, top, 0), down(yh, top, 0)], "box", bb, 1)
    total = sum(depths)
    out = []
    for f, d, o in zip(fields, depths, offs):
        lo_win = slice(o + d - top, o + d)
        hi_win = slice(o, o + top)
        assert lo_win.start >= 0 and hi_win.stop <= total
        hi_win2 = slice(total + hi_win.start, total + hi_win.stop)
        rows = [
            jnp.concatenate([low[:, lo_win], xl[lo_win], low[:, hi_win2]], axis=1),
            jnp.concatenate([yl[:, lo_win], f, yh[:, hi_win]], axis=1),
            jnp.concatenate([high[:, lo_win], xh[hi_win], high[:, hi_win2]], axis=1),
        ]
        out.append(jnp.concatenate(rows, axis=0))
    return out


def shift_z(field, side):
    zeros = jnp.zeros_like(field[:, :, :1])
    if side < 0:
        return jnp.concatenate([zeros, field[:, :, :-1]], axis=2)
    return jnp.concatenate([field[:, :, 1:], zeros], axis=2)


def padded_neighbours(padded):
    return [
        padded[:-2, 1:-1, 1:-1],
        padded[2:, 1:-1, 1:-1],
        padded[1:-1, :-2, 1:-1],
        padded[1:-1, 2:, 1:-1],
        padded[1:-1, 1:-1, :-2],
        padded[1:-1, 1:-1, 2:],
    ]


def coefs_of(field, nears):
    return [jnp.where(near > 0, 2.0 * field * near / (field + near), field) for near in nears]


def apply_op(field, nears, coefs):
    total = jnp.zeros_like(field)
    for coef, near in zip(coefs, nears):
        total = total + coef * (field - near)
    return total


def group_matrix(n, k):
    rows = lax.broadcasted_iota(jnp.int32, (n, n // k), 0) // k
    cols = lax.broadcasted_iota(jnp.int32, (n, n // k), 1)
    return (rows == cols).astype(jnp.float32)


def block_mean(field):
    sx, sy, sz = field.shape
    fx = field.reshape(sx // 4, 4, sy, sz).sum(axis=1)
    fz = jnp.einsum("xyz,zc->xyc", fx, group_matrix(sz, 4), precision=HIGHEST)
    fy = jnp.einsum("xyc,yb->xbc", fz, group_matrix(sy, 4), precision=HIGHEST)
    return fy * (1.0 / 64.0)


def expand(coarse, shape):
    sx, sy, sz = shape
    cz = jnp.einsum("xbc,zc->xbz", coarse, group_matrix(sz, 4), precision=HIGHEST)
    cy = jnp.einsum("xbz,yb->xyz", cz, group_matrix(sy, 4), precision=HIGHEST)
    return jnp.broadcast_to(cy[:, None], (sx // 4, 4, sy, sz)).reshape(sx, sy, sz)


def inside_mask(shape, depth, totals):
    ex, ey, ez = shape
    cx, cy = ex - 2 * depth, ey - 2 * depth
    gx = lax.axis_index("box") * cx - depth + lax.broadcasted_iota(jnp.int32, shape, 0)
    gy = lax.axis_index("group") * cy - depth + lax.broadcasted_iota(jnp.int32, shape, 1)
    return (gx >= 0) & (gx < totals[0]) & (gy >= 0) & (gy < totals[1])


def chebyshev_local(rhs_c, b_c):
    depth = CHEB
    cx, cy, cz = rhs_c.shape
    both = jnp.stack([b_c, rhs_c])
    both = deep_extend(both, "box", 1, depth)
    both = deep_extend(both, "group", 2, depth)
    b_ext, rhs_ext = both[0], both[1]
    totals = (cx * lax.axis_size("box"), cy * lax.axis_size("group"))
    inside = inside_mask(b_ext.shape, depth, totals)
    coefs = [c * 0.0625 for c in coefs_of(b_ext, padded_neighbours(jnp.pad(b_ext, 1)))]
    diag = sum(coefs)
    inv_diag = jnp.where(inside, 1.0 / jnp.where(inside, diag, 1.0), 0.0)

    low, high = (0.05, 2.0)
    theta = (high + low) / 2.0
    delta = (high - low) / 2.0
    sigma = theta / delta
    rho = 1.0 / sigma
    solution = jnp.zeros_like(rhs_ext)
    remain = jnp.where(inside, rhs_ext, 0.0)
    direction = remain * inv_diag / theta
    for step in range(CHEB):
        solution = solution + direction
        if step + 1 < CHEB:
            nears = padded_neighbours(jnp.pad(direction, 1))
            remain = remain - apply_op(direction, nears, coefs)
            rho_next = 1.0 / (2.0 * sigma - rho)
            direction = rho_next * rho * direction + 2.0 * rho_next / delta * remain * inv_diag
            rho = rho_next
    return solution[depth:depth + cx, depth:depth + cy]


def grid_mask(shape, depth, axes, totals):
    inside = None
    for dim, (axis, total) in enumerate(zip(axes, totals)):
        own = shape[dim] - 2 * depth
        g = lax.axis_index(axis) * own - depth + lax.broadcasted_iota(jnp.int32, shape, dim)
        ok = (g >= 0) & (g < total)
        inside = ok if inside is None else inside & ok
    return inside


def shared_faces(b):
    def face(a, n):
        return jnp.where((a > 0) & (n > 0), 2.0 * a * n / (a + n), a + n)

    nears = padded_neighbours(jnp.pad(b, 1))
    lx, ly, lz = face(b, nears[0]), face(b, nears[2]), face(b, nears[4])
    hx = jnp.pad(lx, ((0, 1), (0, 0), (0, 0)))[1:]
    hy = jnp.pad(ly, ((0, 0), (0, 1), (0, 0)))[:, 1:]
    hz = jnp.pad(lz, ((0, 0), (0, 0), (0, 1)))[:, :, 1:]
    top = lax.broadcasted_iota(jnp.int32, b.shape, 2) == b.shape[2] - 1
    return [lx, hx, ly, hy, lz, jnp.where(top, b, hz)]


def low_faces(b):
    faces = []
    for dim in range(3):
        n = b.shape[dim]
        lo = lax.slice_in_dim(b, 0, n - 1, axis=dim)
        hi = lax.slice_in_dim(b, 1, n, axis=dim)
        inner = jnp.where((lo > 0) & (hi > 0), 2.0 * hi * lo / (hi + lo), hi + lo)
        faces.append(jnp.concatenate([lax.slice_in_dim(b, 0, 1, axis=dim), inner], axis=dim))
    return faces


def face_pairs(b, faces):
    pairs = []
    for dim, lo in enumerate(faces):
        n = b.shape[dim]
        hi = jnp.concatenate(
            [lax.slice_in_dim(lo, 1, n, axis=dim), lax.slice_in_dim(b, n - 1, n, axis=dim)], axis=dim
        )
        pairs += [lo, hi]
    return pairs


def per_device(right_side, inv_density, pressure):
    depth = SWEEPS + 1
    sx, sy, sz = pressure.shape
    b_e, rhs_e, fine = packed_halo([inv_density, right_side, pressure], [depth, depth - 1, depth])
    rhs_e, b_e, fine = lax.optimization_barrier((rhs_e, b_e, fine))
    totals = (sx * lax.axis_size("box"), sy * lax.axis_size("group"))
    inside = grid_mask(fine.shape, depth, ("box", "group"), totals)
    coefs = shared_faces(b_e)
    diag = sum(coefs)
    weight = jnp.where(inside, 2.0 / 3.0 / jnp.where(inside, diag, 1.0), 0.0)
    lift = weight * rhs_e
    for sweep in range(SWEEPS):
        pull = sum(c * n for c, n in zip(coefs, padded_neighbours(jnp.pad(fine, 1))))
        fine = jnp.where(inside, fine * (1.0 / 3.0) + lift + weight * pull, 0.0)
    own = (slice(depth, depth + sx), slice(depth, depth + sy))
    core = fine[own]
    nears = [
        fine[depth - 1:depth - 1 + sx, depth:depth + sy],
        fine[depth + 1:depth + 1 + sx, depth:depth + sy],
        fine[depth:depth + sx, depth - 1:depth - 1 + sy],
        fine[depth:depth + sx, depth + 1:depth + 1 + sy],
        shift_z(core, -1),
        shift_z(core, 1),
    ]
    res = right_side - apply_op(core, nears, [c[own] for c in coefs])
    fine, res = lax.optimization_barrier((core, res))
    coarse_rhs = block_mean(res)
    coarse_b = block_mean(inv_density)
    corr = chebyshev_local(coarse_rhs, coarse_b)
    return fine + expand(corr, fine.shape)


def solution(mesh):
    return jax.shard_map(
        per_device,
        mesh=mesh,
        in_specs=(P("box", "group", None), P("box", "group", None), P("box", "group", None)),
        out_specs=P("box", "group", None),
        check_vma=False,
    )
```

```python
import jax
import jax.numpy as jnp
from jax import lax
from jax.sharding import PartitionSpec as P

SWEEPS = 2
CHEB = 8
HIGHEST = lax.Precision.HIGHEST


def shifted_pairs(count, hop):
    return [(i, i + hop) for i in range(count - hop)]


def halo_from(block, axis, dim, width, hop):
    count = lax.axis_size(axis)
    n = block.shape[dim]
    if hop >= count:
        shape = list(block.shape)
        shape[dim] = width
        zeros = jnp.zeros(shape, block.dtype)
        return zeros, zeros
    forward = shifted_pairs(count, hop)
    backward = [(t, s) for s, t in forward]
    low = lax.ppermute(lax.slice_in_dim(block, n - width, n, axis=dim), axis, forward)
    high = lax.ppermute(lax.slice_in_dim(block, 0, width, axis=dim), axis, backward)
    return low, high


def deep_extend(block, axis, dim, depth):
    n = block.shape[dim]
    lows, highs = [], []
    need, hop = depth, 1
    while need > 0:
        width = min(n, need)
        low, high = halo_from(block, axis, dim, width, hop)
        lows.insert(0, low)
        highs.append(high)
        need -= width
        hop += 1
    return jnp.concatenate(lows + [block] + highs, axis=dim)


def packed_halo(fields, depths):
    top = max(depths)
    assert top <= fields[0].shape[0] and top <= fields[0].shape[1]
    offs = [sum(depths[:k]) for k in range(len(depths))]
    up = lambda f, d, dim: lax.slice_in_dim(f, f.shape[dim] - d, f.shape[dim], axis=dim)
    down = lambda f, d, dim: lax.slice_in_dim(f, 0, d, axis=dim)
    nb, ng = lax.axis_size("box"), lax.axis_size("group")
    fb, bb = shifted_pairs(nb, 1), [(t, s) for s, t in shifted_pairs(nb, 1)]
    fg, bg = shifted_pairs(ng, 1), [(t, s) for s, t in shifted_pairs(ng, 1)]

    def send(pieces, axis, pairs, dim):
        msg = jnp.concatenate(pieces, axis=dim)
        if not pairs:
            return jnp.zeros_like(msg)
        return lax.ppermute(msg, axis, pairs)

    xl = send([up(f, d, 0) for f, d in zip(fields, depths)], "box", fb, 0)
    xh = send([down(f, d, 0) for f, d in zip(fields, depths)], "box", bb, 0)
    yl = send([up(f, d, 1) for f, d in zip(fields, depths)], "group", fg, 1)
    yh = send([down(f, d, 1) for f, d in zip(fields, depths)], "group", bg, 1)
    low = send([up(yl, top, 0), up(yh, top, 0)], "box", fb, 1)
    high = send([down(yl, top, 0), down(yh, top, 0)], "box", bb, 1)
    total = sum(depths)
    out = []
    for f, d, o in zip(fields, depths, offs):
        lo_win = slice(o + d - top, o + d)
        hi_win = slice(o, o + top)
        assert lo_win.start >= 0 and hi_win.stop <= total
        hi_win2 = slice(total + hi_win.start, total + hi_win.stop)
        rows = [
            jnp.concatenate([low[:, lo_win], xl[lo_win], low[:, hi_win2]], axis=1),
            jnp.concatenate([yl[:, lo_win], f, yh[:, hi_win]], axis=1),
            jnp.concatenate([high[:, lo_win], xh[hi_win], high[:, hi_win2]], axis=1),
        ]
        out.append(jnp.concatenate(rows, axis=0))
    return out


def shift_z(field, side):
    zeros = jnp.zeros_like(field[:, :, :1])
    if side < 0:
        return jnp.concatenate([zeros, field[:, :, :-1]], axis=2)
    return jnp.concatenate([field[:, :, 1:], zeros], axis=2)


def padded_neighbours(padded):
    return [
        padded[:-2, 1:-1, 1:-1],
        padded[2:, 1:-1, 1:-1],
        padded[1:-1, :-2, 1:-1],
        padded[1:-1, 2:, 1:-1],
        padded[1:-1, 1:-1, :-2],
        padded[1:-1, 1:-1, 2:],
    ]


def coefs_of(field, nears):
    return [jnp.where(near > 0, 2.0 * field * near / (field + near), field) for near in nears]


def apply_op(field, nears, coefs):
    total = jnp.zeros_like(field)
    for coef, near in zip(coefs, nears):
        total = total + coef * (field - near)
    return total


def group_matrix(n, k):
    rows = lax.broadcasted_iota(jnp.int32, (n, n // k), 0) // k
    cols = lax.broadcasted_iota(jnp.int32, (n, n // k), 1)
    return (rows == cols).astype(jnp.float32)


def block_mean(field):
    sx, sy, sz = field.shape
    fx = field.reshape(sx // 4, 4, sy, sz).sum(axis=1)
    fz = jnp.einsum("xyz,zc->xyc", fx, group_matrix(sz, 4), precision=HIGHEST)
    fy = jnp.einsum("xyc,yb->xbc", fz, group_matrix(sy, 4), precision=HIGHEST)
    return fy * (1.0 / 64.0)


def expand(coarse, shape):
    sx, sy, sz = shape
    cz = jnp.einsum("xbc,zc->xbz", coarse, group_matrix(sz, 4), precision=HIGHEST)
    cy = jnp.einsum("xbz,yb->xyz", cz, group_matrix(sy, 4), precision=HIGHEST)
    return jnp.broadcast_to(cy[:, None], (sx // 4, 4, sy, sz)).reshape(sx, sy, sz)


def inside_mask(shape, depth, totals):
    ex, ey, ez = shape
    cx, cy = ex - 2 * depth, ey - 2 * depth
    gx = lax.axis_index("box") * cx - depth + lax.broadcasted_iota(jnp.int32, shape, 0)
    gy = lax.axis_index("group") * cy - depth + lax.broadcasted_iota(jnp.int32, shape, 1)
    return (gx >= 0) & (gx < totals[0]) & (gy >= 0) & (gy < totals[1])


def chebyshev_local(rhs_c, b_c):
    depth = CHEB
    cx, cy, cz = rhs_c.shape
    both = jnp.stack([b_c, rhs_c])
    both = deep_extend(both, "box", 1, depth)
    both = deep_extend(both, "group", 2, depth)
    b_ext, rhs_ext = both[0], both[1]
    totals = (cx * lax.axis_size("box"), cy * lax.axis_size("group"))
    inside = inside_mask(b_ext.shape, depth, totals)
    coefs = [c * 0.0625 for c in coefs_of(b_ext, padded_neighbours(jnp.pad(b_ext, 1)))]
    diag = sum(coefs)
    inv_diag = jnp.where(inside, 1.0 / jnp.where(inside, diag, 1.0), 0.0)

    low, high = (0.05, 2.0)
    theta = (high + low) / 2.0
    delta = (high - low) / 2.0
    sigma = theta / delta
    rho = 1.0 / sigma
    solution = jnp.zeros_like(rhs_ext)
    remain = jnp.where(inside, rhs_ext, 0.0)
    direction = remain * inv_diag / theta
    for step in range(CHEB):
        solution = solution + direction
        if step + 1 < CHEB:
            nears = padded_neighbours(jnp.pad(direction, 1))
            remain = remain - apply_op(direction, nears, coefs)
            rho_next = 1.0 / (2.0 * sigma - rho)
            direction = rho_next * rho * direction + 2.0 * rho_next / delta * remain * inv_diag
            rho = rho_next
    return solution[depth:depth + cx, depth:depth + cy]


def grid_mask(shape, depth, axes, totals):
    inside = None
    for dim, (axis, total) in enumerate(zip(axes, totals)):
        own = shape[dim] - 2 * depth
        g = lax.axis_index(axis) * own - depth + lax.broadcasted_iota(jnp.int32, shape, dim)
        ok = (g >= 0) & (g < total)
        inside = ok if inside is None else inside & ok
    return inside


def shared_faces(b):
    def face(a, n):
        return jnp.where((a > 0) & (n > 0), 2.0 * a * n / (a + n), a + n)

    nears = padded_neighbours(jnp.pad(b, 1))
    lx, ly, lz = face(b, nears[0]), face(b, nears[2]), face(b, nears[4])
    hx = jnp.pad(lx, ((0, 1), (0, 0), (0, 0)))[1:]
    hy = jnp.pad(ly, ((0, 0), (0, 1), (0, 0)))[:, 1:]
    hz = jnp.pad(lz, ((0, 0), (0, 0), (0, 1)))[:, :, 1:]
    top = lax.broadcasted_iota(jnp.int32, b.shape, 2) == b.shape[2] - 1
    return [lx, hx, ly, hy, lz, jnp.where(top, b, hz)]


def low_faces(b):
    faces = []
    for dim in range(3):
        n = b.shape[dim]
        lo = lax.slice_in_dim(b, 0, n - 1, axis=dim)
        hi = lax.slice_in_dim(b, 1, n, axis=dim)
        inner = jnp.where((lo > 0) & (hi > 0), 2.0 * hi * lo / (hi + lo), hi + lo)
        faces.append(jnp.concatenate([lax.slice_in_dim(b, 0, 1, axis=dim), inner], axis=dim))
    return faces


def face_pairs(b, faces):
    pairs = []
    for dim, lo in enumerate(faces):
        n = b.shape[dim]
        hi = jnp.concatenate(
            [lax.slice_in_dim(lo, 1, n, axis=dim), lax.slice_in_dim(b, n - 1, n, axis=dim)], axis=dim
        )
        pairs += [lo, hi]
    return pairs


def per_device(right_side, inv_density, pressure):
    depth = SWEEPS + 1
    sx, sy, sz = pressure.shape
    b_e, rhs_e, fine = packed_halo([inv_density, right_side, pressure], [depth, depth - 1, depth])
    rhs_e, b_e, fine = lax.optimization_barrier((rhs_e, b_e, fine))
    totals = (sx * lax.axis_size("box"), sy * lax.axis_size("group"))
    inside = grid_mask(fine.shape, depth, ("box", "group"), totals)
    coefs = shared_faces(b_e)
    diag = sum(coefs)
    weight = jnp.where(inside, 2.0 / 3.0 / jnp.where(inside, diag, 1.0), 0.0)
    lift = weight * rhs_e
    plain = coefs[:5] + [jnp.pad(coefs[4], ((0, 0), (0, 0), (0, 1)))[:, :, 1:]]
    for sweep in range(SWEEPS):
        pull = sum(c * n for c, n in zip(plain, padded_neighbours(jnp.pad(fine, 1))))
        fine = jnp.where(inside, fine * (1.0 / 3.0) + lift + weight * pull, 0.0)
    own = (slice(depth, depth + sx), slice(depth, depth + sy))
    core = fine[own]
    nears = [
        fine[depth - 1:depth - 1 + sx, depth:depth + sy],
        fine[depth + 1:depth + 1 + sx, depth:depth + sy],
        fine[depth:depth + sx, depth - 1:depth - 1 + sy],
        fine[depth:depth + sx, depth + 1:depth + 1 + sy],
        shift_z(core, -1),
        shift_z(core, 1),
    ]
    res = right_side - apply_op(core, nears, [c[own] for c in coefs])
    fine, res = lax.optimization_barrier((core, res))
    coarse_rhs = block_mean(res)
    coarse_b = block_mean(inv_density)
    corr = chebyshev_local(coarse_rhs, coarse_b)
    return fine + expand(corr, fine.shape)


def solution(mesh):
    return jax.shard_map(
        per_device,
        mesh=mesh,
        in_specs=(P("box", "group", None), P("box", "group", None), P("box", "group", None)),
        out_specs=P("box", "group", None),
        check_vma=False,
    )
```

```python
import jax
import jax.numpy as jnp
from jax import lax
from jax.sharding import PartitionSpec as P

SWEEPS = 2
CHEB = 8
HIGHEST = lax.Precision.HIGHEST


def shifted_pairs(count, hop):
    return [(i, i + hop) for i in range(count - hop)]


def halo_from(block, axis, dim, width, hop):
    count = lax.axis_size(axis)
    n = block.shape[dim]
    if hop >= count:
        shape = list(block.shape)
        shape[dim] = width
        zeros = jnp.zeros(shape, block.dtype)
        return zeros, zeros
    forward = shifted_pairs(count, hop)
    backward = [(t, s) for s, t in forward]
    low = lax.ppermute(lax.slice_in_dim(block, n - width, n, axis=dim), axis, forward)
    high = lax.ppermute(lax.slice_in_dim(block, 0, width, axis=dim), axis, backward)
    return low, high


def deep_extend(block, axis, dim, depth):
    n = block.shape[dim]
    lows, highs = [], []
    need, hop = depth, 1
    while need > 0:
        width = min(n, need)
        low, high = halo_from(block, axis, dim, width, hop)
        lows.insert(0, low)
        highs.append(high)
        need -= width
        hop += 1
    return jnp.concatenate(lows + [block] + highs, axis=dim)


def packed_halo(fields, depths):
    top = max(depths)
    assert top <= fields[0].shape[0] and top <= fields[0].shape[1]
    offs = [sum(depths[:k]) for k in range(len(depths))]
    up = lambda f, d, dim: lax.slice_in_dim(f, f.shape[dim] - d, f.shape[dim], axis=dim)
    down = lambda f, d, dim: lax.slice_in_dim(f, 0, d, axis=dim)
    nb, ng = lax.axis_size("box"), lax.axis_size("group")
    fb, bb = shifted_pairs(nb, 1), [(t, s) for s, t in shifted_pairs(nb, 1)]
    fg, bg = shifted_pairs(ng, 1), [(t, s) for s, t in shifted_pairs(ng, 1)]

    def send(pieces, axis, pairs, dim):
        msg = jnp.concatenate(pieces, axis=dim)
        if not pairs:
            return jnp.zeros_like(msg)
        return lax.ppermute(msg, axis, pairs)

    xl = send([up(f, d, 0) for f, d in zip(fields, depths)], "box", fb, 0)
    xh = send([down(f, d, 0) for f, d in zip(fields, depths)], "box", bb, 0)
    yl = send([up(f, d, 1) for f, d in zip(fields, depths)], "group", fg, 1)
    yh = send([down(f, d, 1) for f, d in zip(fields, depths)], "group", bg, 1)
    low = send([up(yl, top, 0), up(yh, top, 0)], "box", fb, 1)
    high = send([down(yl, top, 0), down(yh, top, 0)], "box", bb, 1)
    total = sum(depths)
    out = []
    for f, d, o in zip(fields, depths, offs):
        lo_win = slice(o + d - top, o + d)
        hi_win = slice(o, o + top)
        assert lo_win.start >= 0 and hi_win.stop <= total
        hi_win2 = slice(total + hi_win.start, total + hi_win.stop)
        rows = [
            jnp.concatenate([low[:, lo_win], xl[lo_win], low[:, hi_win2]], axis=1),
            jnp.concatenate([yl[:, lo_win], f, yh[:, hi_win]], axis=1),
            jnp.concatenate([high[:, lo_win], xh[hi_win], high[:, hi_win2]], axis=1),
        ]
        out.append(jnp.concatenate(rows, axis=0))
    return out


def shift_z(field, side):
    zeros = jnp.zeros_like(field[:, :, :1])
    if side < 0:
        return jnp.concatenate([zeros, field[:, :, :-1]], axis=2)
    return jnp.concatenate([field[:, :, 1:], zeros], axis=2)


def padded_neighbours(padded):
    return [
        padded[:-2, 1:-1, 1:-1],
        padded[2:, 1:-1, 1:-1],
        padded[1:-1, :-2, 1:-1],
        padded[1:-1, 2:, 1:-1],
        padded[1:-1, 1:-1, :-2],
        padded[1:-1, 1:-1, 2:],
    ]


def coefs_of(field, nears):
    return [jnp.where(near > 0, 2.0 * field * near / (field + near), field) for near in nears]


def apply_op(field, nears, coefs):
    total = jnp.zeros_like(field)
    for coef, near in zip(coefs, nears):
        total = total + coef * (field - near)
    return total


def group_matrix(n, k):
    rows = lax.broadcasted_iota(jnp.int32, (n, n // k), 0) // k
    cols = lax.broadcasted_iota(jnp.int32, (n, n // k), 1)
    return (rows == cols).astype(jnp.float32)


def block_mean(field):
    sx, sy, sz = field.shape
    fx = field.reshape(sx // 4, 4, sy, sz).sum(axis=1)
    fz = jnp.einsum("xyz,zc->xyc", fx, group_matrix(sz, 4), precision=HIGHEST)
    fy = jnp.einsum("xyc,yb->xbc", fz, group_matrix(sy, 4), precision=HIGHEST)
    return fy * (1.0 / 64.0)


def expand(coarse, shape):
    sx, sy, sz = shape
    cz = jnp.einsum("xbc,zc->xbz", coarse, group_matrix(sz, 4), precision=HIGHEST)
    cy = jnp.einsum("xbz,yb->xyz", cz, group_matrix(sy, 4), precision=HIGHEST)
    return jnp.broadcast_to(cy[:, None], (sx // 4, 4, sy, sz)).reshape(sx, sy, sz)


def inside_mask(shape, depth, totals):
    ex, ey, ez = shape
    cx, cy = ex - 2 * depth, ey - 2 * depth
    gx = lax.axis_index("box") * cx - depth + lax.broadcasted_iota(jnp.int32, shape, 0)
    gy = lax.axis_index("group") * cy - depth + lax.broadcasted_iota(jnp.int32, shape, 1)
    return (gx >= 0) & (gx < totals[0]) & (gy >= 0) & (gy < totals[1])


def pair_extend(block, depth):
    nb = lax.axis_size("box")
    n = block.shape[1]
    odd = lax.axis_index("box") % 2
    partner = lax.ppermute(block, "box", [(i, i ^ 1) for i in range(nb)])
    pair = jnp.where(odd == 0, jnp.concatenate([block, partner], axis=1),
                     jnp.concatenate([partner, block], axis=1))
    low = lax.ppermute(pair, "box", shifted_pairs(nb, 2))
    high = lax.ppermute(pair, "box", [(t, s) for s, t in shifted_pairs(nb, 2)])
    span = jnp.concatenate([low, pair, high], axis=1)
    start = 2 * n - depth + odd * n
    return lax.dynamic_slice_in_dim(span, start, n + 2 * depth, axis=1)


def chebyshev_local(rhs_c, b_c):
    depth = CHEB
    cx, cy, cz = rhs_c.shape
    both = jnp.stack([b_c, rhs_c])
    nb = lax.axis_size("box")
    if nb % 2 == 0 and nb > 2 and cx < depth <= 2 * cx:
        both = pair_extend(both, depth)
    else:
        both = deep_extend(both, "box", 1, depth)
    both = deep_extend(both, "group", 2, depth)
    b_ext, rhs_ext = both[0], both[1]
    totals = (cx * lax.axis_size("box"), cy * lax.axis_size("group"))
    inside = inside_mask(b_ext.shape, depth, totals)
    coefs = [c * 0.0625 for c in coefs_of(b_ext, padded_neighbours(jnp.pad(b_ext, 1)))]
    diag = sum(coefs)
    inv_diag = jnp.where(inside, 1.0 / jnp.where(inside, diag, 1.0), 0.0)

    low, high = (0.05, 2.0)
    theta = (high + low) / 2.0
    delta = (high - low) / 2.0
    sigma = theta / delta
    rho = 1.0 / sigma
    solution = jnp.zeros_like(rhs_ext)
    remain = jnp.where(inside, rhs_ext, 0.0)
    direction = remain * inv_diag / theta
    for step in range(CHEB):
        solution = solution + direction
        if step + 1 < CHEB:
            nears = padded_neighbours(jnp.pad(direction, 1))
            remain = remain - apply_op(direction, nears, coefs)
            rho_next = 1.0 / (2.0 * sigma - rho)
            direction = rho_next * rho * direction + 2.0 * rho_next / delta * remain * inv_diag
            rho = rho_next
    return solution[depth:depth + cx, depth:depth + cy]


def grid_mask(shape, depth, axes, totals):
    inside = None
    for dim, (axis, total) in enumerate(zip(axes, totals)):
        own = shape[dim] - 2 * depth
        g = lax.axis_index(axis) * own - depth + lax.broadcasted_iota(jnp.int32, shape, dim)
        ok = (g >= 0) & (g < total)
        inside = ok if inside is None else inside & ok
    return inside


def shared_faces(b):
    def face(a, n):
        return jnp.where((a > 0) & (n > 0), 2.0 * a * n / (a + n), a + n)

    nears = padded_neighbours(jnp.pad(b, 1))
    lx, ly, lz = face(b, nears[0]), face(b, nears[2]), face(b, nears[4])
    hx = jnp.pad(lx, ((0, 1), (0, 0), (0, 0)))[1:]
    hy = jnp.pad(ly, ((0, 0), (0, 1), (0, 0)))[:, 1:]
    hz = jnp.pad(lz, ((0, 0), (0, 0), (0, 1)))[:, :, 1:]
    top = lax.broadcasted_iota(jnp.int32, b.shape, 2) == b.shape[2] - 1
    return [lx, hx, ly, hy, lz, jnp.where(top, b, hz)]


def low_faces(b):
    faces = []
    for dim in range(3):
        n = b.shape[dim]
        lo = lax.slice_in_dim(b, 0, n - 1, axis=dim)
        hi = lax.slice_in_dim(b, 1, n, axis=dim)
        inner = jnp.where((lo > 0) & (hi > 0), 2.0 * hi * lo / (hi + lo), hi + lo)
        faces.append(jnp.concatenate([lax.slice_in_dim(b, 0, 1, axis=dim), inner], axis=dim))
    return faces


def face_pairs(b, faces):
    pairs = []
    for dim, lo in enumerate(faces):
        n = b.shape[dim]
        hi = jnp.concatenate(
            [lax.slice_in_dim(lo, 1, n, axis=dim), lax.slice_in_dim(b, n - 1, n, axis=dim)], axis=dim
        )
        pairs += [lo, hi]
    return pairs


def per_device(right_side, inv_density, pressure):
    depth = SWEEPS + 1
    sx, sy, sz = pressure.shape
    b_e, rhs_e, fine = packed_halo([inv_density, right_side, pressure], [depth, depth - 1, depth])
    rhs_e, b_e, fine = lax.optimization_barrier((rhs_e, b_e, fine))
    totals = (sx * lax.axis_size("box"), sy * lax.axis_size("group"))
    inside = grid_mask(fine.shape, depth, ("box", "group"), totals)
    coefs = shared_faces(b_e)
    diag = sum(coefs)
    for sweep in range(SWEEPS):
        step = 2.0 / 3.0 * (rhs_e - apply_op(fine, padded_neighbours(jnp.pad(fine, 1)), coefs)) / diag
        fine = jnp.where(inside, fine + step, 0.0)
    own = (slice(depth, depth + sx), slice(depth, depth + sy))
    core = fine[own]
    nears = [
        fine[depth - 1:depth - 1 + sx, depth:depth + sy],
        fine[depth + 1:depth + 1 + sx, depth:depth + sy],
        fine[depth:depth + sx, depth - 1:depth - 1 + sy],
        fine[depth:depth + sx, depth + 1:depth + 1 + sy],
        shift_z(core, -1),
        shift_z(core, 1),
    ]
    res = right_side - apply_op(core, nears, [c[own] for c in coefs])
    fine, res = lax.optimization_barrier((core, res))
    coarse_rhs = block_mean(res)
    coarse_b = block_mean(inv_density)
    corr = chebyshev_local(coarse_rhs, coarse_b)
    return fine + expand(corr, fine.shape)


def solution(mesh):
    return jax.shard_map(
        per_device,
        mesh=mesh,
        in_specs=(P("box", "group", None), P("box", "group", None), P("box", "group", None)),
        out_specs=P("box", "group", None),
        check_vma=False,
    )
```

```python
import jax
import jax.numpy as jnp
from jax import lax
from jax.sharding import PartitionSpec as P

SWEEPS = 2
CHEB = 8
HIGHEST = lax.Precision.HIGHEST


def shifted_pairs(count, hop):
    return [(i, i + hop) for i in range(count - hop)]


def halo_from(block, axis, dim, width, hop):
    count = lax.axis_size(axis)
    n = block.shape[dim]
    if hop >= count:
        shape = list(block.shape)
        shape[dim] = width
        zeros = jnp.zeros(shape, block.dtype)
        return zeros, zeros
    forward = shifted_pairs(count, hop)
    backward = [(t, s) for s, t in forward]
    low = lax.ppermute(lax.slice_in_dim(block, n - width, n, axis=dim), axis, forward)
    high = lax.ppermute(lax.slice_in_dim(block, 0, width, axis=dim), axis, backward)
    return low, high


def deep_extend(block, axis, dim, depth):
    n = block.shape[dim]
    lows, highs = [], []
    need, hop = depth, 1
    while need > 0:
        width = min(n, need)
        low, high = halo_from(block, axis, dim, width, hop)
        lows.insert(0, low)
        highs.append(high)
        need -= width
        hop += 1
    return jnp.concatenate(lows + [block] + highs, axis=dim)


def packed_halo(fields, depths):
    top = max(depths)
    assert top <= fields[0].shape[0] and top <= fields[0].shape[1]
    offs = [sum(depths[:k]) for k in range(len(depths))]
    up = lambda f, d, dim: lax.slice_in_dim(f, f.shape[dim] - d, f.shape[dim], axis=dim)
    down = lambda f, d, dim: lax.slice_in_dim(f, 0, d, axis=dim)
    nb, ng = lax.axis_size("box"), lax.axis_size("group")
    fb, bb = shifted_pairs(nb, 1), [(t, s) for s, t in shifted_pairs(nb, 1)]
    fg, bg = shifted_pairs(ng, 1), [(t, s) for s, t in shifted_pairs(ng, 1)]

    def send(pieces, axis, pairs, dim):
        msg = jnp.concatenate(pieces, axis=dim)
        if not pairs:
            return jnp.zeros_like(msg)
        return lax.ppermute(msg, axis, pairs)

    xl = send([up(f, d, 0) for f, d in zip(fields, depths)], "box", fb, 0)
    xh = send([down(f, d, 0) for f, d in zip(fields, depths)], "box", bb, 0)
    yl = send([up(f, d, 1) for f, d in zip(fields, depths)], "group", fg, 1)
    yh = send([down(f, d, 1) for f, d in zip(fields, depths)], "group", bg, 1)
    low = send([up(yl, top, 0), up(yh, top, 0)], "box", fb, 1)
    high = send([down(yl, top, 0), down(yh, top, 0)], "box", bb, 1)
    total = sum(depths)
    out = []
    for f, d, o in zip(fields, depths, offs):
        lo_win = slice(o + d - top, o + d)
        hi_win = slice(o, o + top)
        assert lo_win.start >= 0 and hi_win.stop <= total
        hi_win2 = slice(total + hi_win.start, total + hi_win.stop)
        rows = [
            jnp.concatenate([low[:, lo_win], xl[lo_win], low[:, hi_win2]], axis=1),
            jnp.concatenate([yl[:, lo_win], f, yh[:, hi_win]], axis=1),
            jnp.concatenate([high[:, lo_win], xh[hi_win], high[:, hi_win2]], axis=1),
        ]
        out.append(jnp.concatenate(rows, axis=0))
    return out


def shift_z(field, side):
    zeros = jnp.zeros_like(field[:, :, :1])
    if side < 0:
        return jnp.concatenate([zeros, field[:, :, :-1]], axis=2)
    return jnp.concatenate([field[:, :, 1:], zeros], axis=2)


def padded_neighbours(padded):
    return [
        padded[:-2, 1:-1, 1:-1],
        padded[2:, 1:-1, 1:-1],
        padded[1:-1, :-2, 1:-1],
        padded[1:-1, 2:, 1:-1],
        padded[1:-1, 1:-1, :-2],
        padded[1:-1, 1:-1, 2:],
    ]


def coefs_of(field, nears):
    return [jnp.where(near > 0, 2.0 * field * near / (field + near), field) for near in nears]


def apply_op(field, nears, coefs):
    total = jnp.zeros_like(field)
    for coef, near in zip(coefs, nears):
        total = total + coef * (field - near)
    return total


def group_matrix(n, k):
    rows = lax.broadcasted_iota(jnp.int32, (n, n // k), 0) // k
    cols = lax.broadcasted_iota(jnp.int32, (n, n // k), 1)
    return (rows == cols).astype(jnp.float32)


def block_mean(field):
    sx, sy, sz = field.shape
    fx = field.reshape(sx // 4, 4, sy, sz).sum(axis=1)
    fz = jnp.einsum("xyz,zc->xyc", fx, group_matrix(sz, 4), precision=HIGHEST)
    fy = jnp.einsum("xyc,yb->xbc", fz, group_matrix(sy, 4), precision=HIGHEST)
    return fy * (1.0 / 64.0)


def expand(coarse, shape):
    sx, sy, sz = shape
    cz = jnp.einsum("xbc,zc->xbz", coarse, group_matrix(sz, 4), precision=HIGHEST)
    cy = jnp.einsum("xbz,yb->xyz", cz, group_matrix(sy, 4), precision=HIGHEST)
    return jnp.broadcast_to(cy[:, None], (sx // 4, 4, sy, sz)).reshape(sx, sy, sz)


def inside_mask(shape, depth, totals):
    ex, ey, ez = shape
    cx, cy = ex - 2 * depth, ey - 2 * depth
    gx = lax.axis_index("box") * cx - depth + lax.broadcasted_iota(jnp.int32, shape, 0)
    gy = lax.axis_index("group") * cy - depth + lax.broadcasted_iota(jnp.int32, shape, 1)
    return (gx >= 0) & (gx < totals[0]) & (gy >= 0) & (gy < totals[1])


def pair_extend(block, depth):
    nb = lax.axis_size("box")
    n = block.shape[1]
    odd = lax.axis_index("box") % 2
    partner = lax.ppermute(block, "box", [(i, i ^ 1) for i in range(nb)])
    pair = jnp.where(odd == 0, jnp.concatenate([block, partner], axis=1),
                     jnp.concatenate([partner, block], axis=1))
    low = lax.ppermute(pair, "box", shifted_pairs(nb, 2))
    high = lax.ppermute(pair, "box", [(t, s) for s, t in shifted_pairs(nb, 2)])
    span = jnp.concatenate([low, pair, high], axis=1)
    start = 2 * n - depth + odd * n
    return lax.dynamic_slice_in_dim(span, start, n + 2 * depth, axis=1)


def chebyshev_local(rhs_c, b_c):
    depth = CHEB
    cx, cy, cz = rhs_c.shape
    both = jnp.stack([b_c, rhs_c])
    nb = lax.axis_size("box")
    if nb % 2 == 0 and nb > 2 and cx < depth <= 2 * cx:
        both = pair_extend(both, depth)
    else:
        both = deep_extend(both, "box", 1, depth)
    both = deep_extend(both, "group", 2, depth)
    b_ext, rhs_ext = both[0], both[1]
    totals = (cx * lax.axis_size("box"), cy * lax.axis_size("group"))
    inside = inside_mask(b_ext.shape, depth, totals)
    coefs = [c * 0.0625 for c in coefs_of(b_ext, padded_neighbours(jnp.pad(b_ext, 1)))]
    diag = sum(coefs)
    inv_diag = jnp.where(inside, 1.0 / jnp.where(inside, diag, 1.0), 0.0)

    low, high = (0.05, 2.0)
    theta = (high + low) / 2.0
    delta = (high - low) / 2.0
    sigma = theta / delta
    rho = 1.0 / sigma
    solution = jnp.zeros_like(rhs_ext)
    remain = jnp.where(inside, rhs_ext, 0.0)
    direction = remain * inv_diag / theta
    for step in range(CHEB):
        solution = solution + direction
        if step + 1 < CHEB:
            nears = padded_neighbours(jnp.pad(direction, 1))
            remain = remain - apply_op(direction, nears, coefs)
            rho_next = 1.0 / (2.0 * sigma - rho)
            direction = rho_next * rho * direction + 2.0 * rho_next / delta * remain * inv_diag
            rho = rho_next
    return solution[depth:depth + cx, depth:depth + cy]


def grid_mask(shape, depth, axes, totals):
    inside = None
    for dim, (axis, total) in enumerate(zip(axes, totals)):
        own = shape[dim] - 2 * depth
        g = lax.axis_index(axis) * own - depth + lax.broadcasted_iota(jnp.int32, shape, dim)
        ok = (g >= 0) & (g < total)
        inside = ok if inside is None else inside & ok
    return inside


def shared_faces(b):
    def face(a, n):
        return jnp.where((a > 0) & (n > 0), 2.0 * a * n / (a + n), a + n)

    nears = padded_neighbours(jnp.pad(b, 1))
    lx, ly, lz = face(b, nears[0]), face(b, nears[2]), face(b, nears[4])
    hx = jnp.pad(lx, ((0, 1), (0, 0), (0, 0)))[1:]
    hy = jnp.pad(ly, ((0, 0), (0, 1), (0, 0)))[:, 1:]
    hz = jnp.pad(lz, ((0, 0), (0, 0), (0, 1)))[:, :, 1:]
    top = lax.broadcasted_iota(jnp.int32, b.shape, 2) == b.shape[2] - 1
    return [lx, hx, ly, hy, lz, jnp.where(top, b, hz)]


def low_faces(b):
    faces = []
    for dim in range(3):
        n = b.shape[dim]
        lo = lax.slice_in_dim(b, 0, n - 1, axis=dim)
        hi = lax.slice_in_dim(b, 1, n, axis=dim)
        inner = jnp.where((lo > 0) & (hi > 0), 2.0 * hi * lo / (hi + lo), hi + lo)
        faces.append(jnp.concatenate([lax.slice_in_dim(b, 0, 1, axis=dim), inner], axis=dim))
    return faces


def face_pairs(b, faces):
    pairs = []
    for dim, lo in enumerate(faces):
        n = b.shape[dim]
        hi = jnp.concatenate(
            [lax.slice_in_dim(lo, 1, n, axis=dim), lax.slice_in_dim(b, n - 1, n, axis=dim)], axis=dim
        )
        pairs += [lo, hi]
    return pairs


def per_device(right_side, inv_density, pressure):
    depth = SWEEPS + 1
    sx, sy, sz = pressure.shape
    b_e, rhs_e, fine = packed_halo([inv_density, right_side, pressure], [depth, depth - 1, depth])
    rhs_e, b_e, fine = lax.optimization_barrier((rhs_e, b_e, fine))
    totals = (sx * lax.axis_size("box"), sy * lax.axis_size("group"))
    inside = grid_mask(fine.shape, depth, ("box", "group"), totals)
    coefs = shared_faces(b_e)
    diag = sum(coefs)
    weight = jnp.where(inside, 2.0 / 3.0 / jnp.where(inside, diag, 1.0), 0.0)
    lift = weight * rhs_e
    plain = coefs[:5] + [jnp.pad(coefs[4], ((0, 0), (0, 0), (0, 1)))[:, :, 1:]]
    for sweep in range(SWEEPS):
        pull = sum(c * n for c, n in zip(plain, padded_neighbours(jnp.pad(fine, 1))))
        fine = jnp.where(inside, fine * (1.0 / 3.0) + lift + weight * pull, 0.0)
    own = (slice(depth, depth + sx), slice(depth, depth + sy))
    core = fine[own]
    nears = [
        fine[depth - 1:depth - 1 + sx, depth:depth + sy],
        fine[depth + 1:depth + 1 + sx, depth:depth + sy],
        fine[depth:depth + sx, depth - 1:depth - 1 + sy],
        fine[depth:depth + sx, depth + 1:depth + 1 + sy],
        shift_z(core, -1),
        shift_z(core, 1),
    ]
    res = right_side - apply_op(core, nears, [c[own] for c in coefs])
    fine, res = lax.optimization_barrier((core, res))
    coarse_rhs = block_mean(res)
    coarse_b = block_mean(inv_density)
    corr = chebyshev_local(coarse_rhs, coarse_b)
    return fine + expand(corr, fine.shape)


def solution(mesh):
    return jax.shard_map(
        per_device,
        mesh=mesh,
        in_specs=(P("box", "group", None), P("box", "group", None), P("box", "group", None)),
        out_specs=P("box", "group", None),
        check_vma=False,
    )
```

```python
import jax
import jax.numpy as jnp
from jax import lax
from jax.sharding import PartitionSpec as P

SWEEPS = 2
CHEB = 8
HIGHEST = lax.Precision.HIGHEST


def shifted_pairs(count, hop):
    return [(i, i + hop) for i in range(count - hop)]


def halo_from(block, axis, dim, width, hop):
    count = lax.axis_size(axis)
    n = block.shape[dim]
    if hop >= count:
        shape = list(block.shape)
        shape[dim] = width
        zeros = jnp.zeros(shape, block.dtype)
        return zeros, zeros
    forward = shifted_pairs(count, hop)
    backward = [(t, s) for s, t in forward]
    low = lax.ppermute(lax.slice_in_dim(block, n - width, n, axis=dim), axis, forward)
    high = lax.ppermute(lax.slice_in_dim(block, 0, width, axis=dim), axis, backward)
    return low, high


def deep_extend(block, axis, dim, depth):
    n = block.shape[dim]
    lows, highs = [], []
    need, hop = depth, 1
    while need > 0:
        width = min(n, need)
        low, high = halo_from(block, axis, dim, width, hop)
        lows.insert(0, low)
        highs.append(high)
        need -= width
        hop += 1
    return jnp.concatenate(lows + [block] + highs, axis=dim)


def packed_halo(fields, depths):
    top = max(depths)
    assert top <= fields[0].shape[0] and top <= fields[0].shape[1]
    offs = [sum(depths[:k]) for k in range(len(depths))]
    up = lambda f, d, dim: lax.slice_in_dim(f, f.shape[dim] - d, f.shape[dim], axis=dim)
    down = lambda f, d, dim: lax.slice_in_dim(f, 0, d, axis=dim)
    nb, ng = lax.axis_size("box"), lax.axis_size("group")
    fb, bb = shifted_pairs(nb, 1), [(t, s) for s, t in shifted_pairs(nb, 1)]
    fg, bg = shifted_pairs(ng, 1), [(t, s) for s, t in shifted_pairs(ng, 1)]

    def send(pieces, axis, pairs, dim):
        msg = jnp.concatenate(pieces, axis=dim)
        if not pairs:
            return jnp.zeros_like(msg)
        return lax.ppermute(msg, axis, pairs)

    xl = send([up(f, d, 0) for f, d in zip(fields, depths)], "box", fb, 0)
    xh = send([down(f, d, 0) for f, d in zip(fields, depths)], "box", bb, 0)
    yl = send([up(f, d, 1) for f, d in zip(fields, depths)], "group", fg, 1)
    yh = send([down(f, d, 1) for f, d in zip(fields, depths)], "group", bg, 1)
    low = send([up(yl, top, 0), up(yh, top, 0)], "box", fb, 1)
    high = send([down(yl, top, 0), down(yh, top, 0)], "box", bb, 1)
    total = sum(depths)
    out = []
    for f, d, o in zip(fields, depths, offs):
        lo_win = slice(o + d - top, o + d)
        hi_win = slice(o, o + top)
        assert lo_win.start >= 0 and hi_win.stop <= total
        hi_win2 = slice(total + hi_win.start, total + hi_win.stop)
        rows = [
            jnp.concatenate([low[:, lo_win], xl[lo_win], low[:, hi_win2]], axis=1),
            jnp.concatenate([yl[:, lo_win], f, yh[:, hi_win]], axis=1),
            jnp.concatenate([high[:, lo_win], xh[hi_win], high[:, hi_win2]], axis=1),
        ]
        out.append(jnp.concatenate(rows, axis=0))
    return out


def shift_z(field, side):
    zeros = jnp.zeros_like(field[:, :, :1])
    if side < 0:
        return jnp.concatenate([zeros, field[:, :, :-1]], axis=2)
    return jnp.concatenate([field[:, :, 1:], zeros], axis=2)


def padded_neighbours(padded):
    return [
        padded[:-2, 1:-1, 1:-1],
        padded[2:, 1:-1, 1:-1],
        padded[1:-1, :-2, 1:-1],
        padded[1:-1, 2:, 1:-1],
        padded[1:-1, 1:-1, :-2],
        padded[1:-1, 1:-1, 2:],
    ]


def coefs_of(field, nears):
    return [jnp.where(near > 0, 2.0 * field * near / (field + near), field) for near in nears]


def apply_op(field, nears, coefs):
    total = jnp.zeros_like(field)
    for coef, near in zip(coefs, nears):
        total = total + coef * (field - near)
    return total


def group_matrix(n, k):
    rows = lax.broadcasted_iota(jnp.int32, (n, n // k), 0) // k
    cols = lax.broadcasted_iota(jnp.int32, (n, n // k), 1)
    return (rows == cols).astype(jnp.float32)


def block_mean(field):
    sx, sy, sz = field.shape
    fx = field.reshape(sx // 4, 4, sy, sz).sum(axis=1)
    fz = jnp.einsum("xyz,zc->xyc", fx, group_matrix(sz, 4), precision=HIGHEST)
    fy = jnp.einsum("xyc,yb->xbc", fz, group_matrix(sy, 4), precision=HIGHEST)
    return fy * (1.0 / 64.0)


def expand(coarse, shape):
    sx, sy, sz = shape
    cz = jnp.einsum("xbc,zc->xbz", coarse, group_matrix(sz, 4), precision=HIGHEST)
    cy = jnp.einsum("xbz,yb->xyz", cz, group_matrix(sy, 4), precision=HIGHEST)
    return jnp.broadcast_to(cy[:, None], (sx // 4, 4, sy, sz)).reshape(sx, sy, sz)


def inside_mask(shape, depth, totals):
    ex, ey, ez = shape
    cx, cy = ex - 2 * depth, ey - 2 * depth
    gx = lax.axis_index("box") * cx - depth + lax.broadcasted_iota(jnp.int32, shape, 0)
    gy = lax.axis_index("group") * cy - depth + lax.broadcasted_iota(jnp.int32, shape, 1)
    return (gx >= 0) & (gx < totals[0]) & (gy >= 0) & (gy < totals[1])


def pair_extend(block, depth):
    nb = lax.axis_size("box")
    n = block.shape[1]
    odd = lax.axis_index("box") % 2
    partner = lax.ppermute(block, "box", [(i, i ^ 1) for i in range(nb)])
    pair = jnp.where(odd == 0, jnp.concatenate([block, partner], axis=1),
                     jnp.concatenate([partner, block], axis=1))
    pair = deep_extend(pair, "group", 2, depth)
    low = lax.ppermute(pair, "box", shifted_pairs(nb, 2))
    high = lax.ppermute(pair, "box", [(t, s) for s, t in shifted_pairs(nb, 2)])
    span = jnp.concatenate([low, pair, high], axis=1)
    start = 2 * n - depth + odd * n
    return lax.dynamic_slice_in_dim(span, start, n + 2 * depth, axis=1)


def chebyshev_local(rhs_c, b_c):
    depth = CHEB
    cx, cy, cz = rhs_c.shape
    both = jnp.stack([b_c, rhs_c])
    nb = lax.axis_size("box")
    if nb % 2 == 0 and nb > 2 and cx < depth <= 2 * cx:
        both = pair_extend(both, depth)
    else:
        both = deep_extend(deep_extend(both, "box", 1, depth), "group", 2, depth)
    b_ext, rhs_ext = both[0], both[1]
    totals = (cx * lax.axis_size("box"), cy * lax.axis_size("group"))
    inside = inside_mask(b_ext.shape, depth, totals)
    coefs = [c * 0.0625 for c in coefs_of(b_ext, padded_neighbours(jnp.pad(b_ext, 1)))]
    diag = sum(coefs)
    inv_diag = jnp.where(inside, 1.0 / jnp.where(inside, diag, 1.0), 0.0)

    low, high = (0.05, 2.0)
    theta = (high + low) / 2.0
    delta = (high - low) / 2.0
    sigma = theta / delta
    rho = 1.0 / sigma
    solution = jnp.zeros_like(rhs_ext)
    remain = jnp.where(inside, rhs_ext, 0.0)
    direction = remain * inv_diag / theta
    for step in range(CHEB):
        solution = solution + direction
        if step + 1 < CHEB:
            nears = padded_neighbours(jnp.pad(direction, 1))
            remain = remain - apply_op(direction, nears, coefs)
            rho_next = 1.0 / (2.0 * sigma - rho)
            direction = rho_next * rho * direction + 2.0 * rho_next / delta * remain * inv_diag
            rho = rho_next
    return solution[depth:depth + cx, depth:depth + cy]


def grid_mask(shape, depth, axes, totals):
    inside = None
    for dim, (axis, total) in enumerate(zip(axes, totals)):
        own = shape[dim] - 2 * depth
        g = lax.axis_index(axis) * own - depth + lax.broadcasted_iota(jnp.int32, shape, dim)
        ok = (g >= 0) & (g < total)
        inside = ok if inside is None else inside & ok
    return inside


def shared_faces(b):
    def face(a, n):
        return jnp.where((a > 0) & (n > 0), 2.0 * a * n / (a + n), a + n)

    nears = padded_neighbours(jnp.pad(b, 1))
    lx, ly, lz = face(b, nears[0]), face(b, nears[2]), face(b, nears[4])
    hx = jnp.pad(lx, ((0, 1), (0, 0), (0, 0)))[1:]
    hy = jnp.pad(ly, ((0, 0), (0, 1), (0, 0)))[:, 1:]
    hz = jnp.pad(lz, ((0, 0), (0, 0), (0, 1)))[:, :, 1:]
    top = lax.broadcasted_iota(jnp.int32, b.shape, 2) == b.shape[2] - 1
    return [lx, hx, ly, hy, lz, jnp.where(top, b, hz)]


def low_faces(b):
    faces = []
    for dim in range(3):
        n = b.shape[dim]
        lo = lax.slice_in_dim(b, 0, n - 1, axis=dim)
        hi = lax.slice_in_dim(b, 1, n, axis=dim)
        inner = jnp.where((lo > 0) & (hi > 0), 2.0 * hi * lo / (hi + lo), hi + lo)
        faces.append(jnp.concatenate([lax.slice_in_dim(b, 0, 1, axis=dim), inner], axis=dim))
    return faces


def face_pairs(b, faces):
    pairs = []
    for dim, lo in enumerate(faces):
        n = b.shape[dim]
        hi = jnp.concatenate(
            [lax.slice_in_dim(lo, 1, n, axis=dim), lax.slice_in_dim(b, n - 1, n, axis=dim)], axis=dim
        )
        pairs += [lo, hi]
    return pairs


def per_device(right_side, inv_density, pressure):
    depth = SWEEPS + 1
    sx, sy, sz = pressure.shape
    b_e, rhs_e, fine = packed_halo([inv_density, right_side, pressure], [depth, depth - 1, depth])
    rhs_e, b_e, fine = lax.optimization_barrier((rhs_e, b_e, fine))
    totals = (sx * lax.axis_size("box"), sy * lax.axis_size("group"))
    inside = grid_mask(fine.shape, depth, ("box", "group"), totals)
    coefs = shared_faces(b_e)
    diag = sum(coefs)
    for sweep in range(SWEEPS):
        step = 2.0 / 3.0 * (rhs_e - apply_op(fine, padded_neighbours(jnp.pad(fine, 1)), coefs)) / diag
        fine = jnp.where(inside, fine + step, 0.0)
    own = (slice(depth, depth + sx), slice(depth, depth + sy))
    core = fine[own]
    nears = [
        fine[depth - 1:depth - 1 + sx, depth:depth + sy],
        fine[depth + 1:depth + 1 + sx, depth:depth + sy],
        fine[depth:depth + sx, depth - 1:depth - 1 + sy],
        fine[depth:depth + sx, depth + 1:depth + 1 + sy],
        shift_z(core, -1),
        shift_z(core, 1),
    ]
    res = right_side - apply_op(core, nears, [c[own] for c in coefs])
    fine, res = lax.optimization_barrier((core, res))
    coarse_rhs = block_mean(res)
    coarse_b = block_mean(inv_density)
    corr = chebyshev_local(coarse_rhs, coarse_b)
    return fine + expand(corr, fine.shape)


def solution(mesh):
    return jax.shard_map(
        per_device,
        mesh=mesh,
        in_specs=(P("box", "group", None), P("box", "group", None), P("box", "group", None)),
        out_specs=P("box", "group", None),
        check_vma=False,
    )
```

```python
import jax
import jax.numpy as jnp
from jax import lax
from jax.sharding import PartitionSpec as P

SWEEPS = 2
CHEB = 8
HIGHEST = lax.Precision.HIGHEST


def shifted_pairs(count, hop):
    return [(i, i + hop) for i in range(count - hop)]


def halo_from(block, axis, dim, width, hop):
    count = lax.axis_size(axis)
    n = block.shape[dim]
    if hop >= count:
        shape = list(block.shape)
        shape[dim] = width
        zeros = jnp.zeros(shape, block.dtype)
        return zeros, zeros
    forward = shifted_pairs(count, hop)
    backward = [(t, s) for s, t in forward]
    low = lax.ppermute(lax.slice_in_dim(block, n - width, n, axis=dim), axis, forward)
    high = lax.ppermute(lax.slice_in_dim(block, 0, width, axis=dim), axis, backward)
    return low, high


def deep_extend(block, axis, dim, depth):
    n = block.shape[dim]
    lows, highs = [], []
    need, hop = depth, 1
    while need > 0:
        width = min(n, need)
        low, high = halo_from(block, axis, dim, width, hop)
        lows.insert(0, low)
        highs.append(high)
        need -= width
        hop += 1
    return jnp.concatenate(lows + [block] + highs, axis=dim)


def packed_halo(fields, depths):
    top = max(depths)
    assert top <= fields[0].shape[0] and top <= fields[0].shape[1]
    offs = [sum(depths[:k]) for k in range(len(depths))]
    up = lambda f, d, dim: lax.slice_in_dim(f, f.shape[dim] - d, f.shape[dim], axis=dim)
    down = lambda f, d, dim: lax.slice_in_dim(f, 0, d, axis=dim)
    nb, ng = lax.axis_size("box"), lax.axis_size("group")
    fb, bb = shifted_pairs(nb, 1), [(t, s) for s, t in shifted_pairs(nb, 1)]
    fg, bg = shifted_pairs(ng, 1), [(t, s) for s, t in shifted_pairs(ng, 1)]

    def send(pieces, axis, pairs, dim):
        msg = jnp.concatenate(pieces, axis=dim)
        if not pairs:
            return jnp.zeros_like(msg)
        return lax.ppermute(msg, axis, pairs)

    def send_split(pieces, axis, pairs, dim):
        msg = jnp.concatenate(pieces, axis=dim)
        half = msg.shape[2] // 2
        parts = [msg[:, :, :half], msg[:, :, half:]]
        return jnp.concatenate([send([p], axis, pairs, dim) for p in parts], axis=2)

    xl = send_split([up(f, d, 0) for f, d in zip(fields, depths)], "box", fb, 0)
    xh = send_split([down(f, d, 0) for f, d in zip(fields, depths)], "box", bb, 0)
    yl = send([up(f, d, 1) for f, d in zip(fields, depths)], "group", fg, 1)
    yh = send([down(f, d, 1) for f, d in zip(fields, depths)], "group", bg, 1)
    low = send([up(yl, top, 0), up(yh, top, 0)], "box", fb, 1)
    high = send([down(yl, top, 0), down(yh, top, 0)], "box", bb, 1)
    total = sum(depths)
    out = []
    for f, d, o in zip(fields, depths, offs):
        lo_win = slice(o + d - top, o + d)
        hi_win = slice(o, o + top)
        assert lo_win.start >= 0 and hi_win.stop <= total
        hi_win2 = slice(total + hi_win.start, total + hi_win.stop)
        rows = [
            jnp.concatenate([low[:, lo_win], xl[lo_win], low[:, hi_win2]], axis=1),
            jnp.concatenate([yl[:, lo_win], f, yh[:, hi_win]], axis=1),
            jnp.concatenate([high[:, lo_win], xh[hi_win], high[:, hi_win2]], axis=1),
        ]
        out.append(jnp.concatenate(rows, axis=0))
    return out


def shift_z(field, side):
    zeros = jnp.zeros_like(field[:, :, :1])
    if side < 0:
        return jnp.concatenate([zeros, field[:, :, :-1]], axis=2)
    return jnp.concatenate([field[:, :, 1:], zeros], axis=2)


def padded_neighbours(padded):
    return [
        padded[:-2, 1:-1, 1:-1],
        padded[2:, 1:-1, 1:-1],
        padded[1:-1, :-2, 1:-1],
        padded[1:-1, 2:, 1:-1],
        padded[1:-1, 1:-1, :-2],
        padded[1:-1, 1:-1, 2:],
    ]


def coefs_of(field, nears):
    return [jnp.where(near > 0, 2.0 * field * near / (field + near), field) for near in nears]


def apply_op(field, nears, coefs):
    total = jnp.zeros_like(field)
    for coef, near in zip(coefs, nears):
        total = total + coef * (field - near)
    return total


def group_matrix(n, k):
    rows = lax.broadcasted_iota(jnp.int32, (n, n // k), 0) // k
    cols = lax.broadcasted_iota(jnp.int32, (n, n // k), 1)
    return (rows == cols).astype(jnp.float32)


def block_mean(field):
    sx, sy, sz = field.shape
    fx = field.reshape(sx // 4, 4, sy, sz).sum(axis=1)
    fz = jnp.einsum("xyz,zc->xyc", fx, group_matrix(sz, 4), precision=HIGHEST)
    fy = jnp.einsum("xyc,yb->xbc", fz, group_matrix(sy, 4), precision=HIGHEST)
    return fy * (1.0 / 64.0)


def expand(coarse, shape):
    sx, sy, sz = shape
    cz = jnp.einsum("xbc,zc->xbz", coarse, group_matrix(sz, 4), precision=HIGHEST)
    cy = jnp.einsum("xbz,yb->xyz", cz, group_matrix(sy, 4), precision=HIGHEST)
    return jnp.broadcast_to(cy[:, None], (sx // 4, 4, sy, sz)).reshape(sx, sy, sz)


def inside_mask(shape, depth, totals):
    ex, ey, ez = shape
    cx, cy = ex - 2 * depth, ey - 2 * depth
    gx = lax.axis_index("box") * cx - depth + lax.broadcasted_iota(jnp.int32, shape, 0)
    gy = lax.axis_index("group") * cy - depth + lax.broadcasted_iota(jnp.int32, shape, 1)
    return (gx >= 0) & (gx < totals[0]) & (gy >= 0) & (gy < totals[1])


def pair_extend(block, depth):
    nb = lax.axis_size("box")
    n = block.shape[1]
    odd = lax.axis_index("box") % 2
    partner = lax.ppermute(block, "box", [(i, i ^ 1) for i in range(nb)])
    pair = jnp.where(odd == 0, jnp.concatenate([block, partner], axis=1),
                     jnp.concatenate([partner, block], axis=1))
    low = lax.ppermute(pair, "box", shifted_pairs(nb, 2))
    high = lax.ppermute(pair, "box", [(t, s) for s, t in shifted_pairs(nb, 2)])
    span = jnp.concatenate([low, pair, high], axis=1)
    start = 2 * n - depth + odd * n
    return lax.dynamic_slice_in_dim(span, start, n + 2 * depth, axis=1)


def chebyshev_local(rhs_c, b_c):
    depth = CHEB
    cx, cy, cz = rhs_c.shape
    both = jnp.stack([b_c, rhs_c])
    nb = lax.axis_size("box")
    if nb % 2 == 0 and nb > 2 and cx < depth <= 2 * cx:
        both = pair_extend(both, depth)
    else:
        both = deep_extend(both, "box", 1, depth)
    both = deep_extend(both, "group", 2, depth)
    b_ext, rhs_ext = both[0], both[1]
    totals = (cx * lax.axis_size("box"), cy * lax.axis_size("group"))
    inside = inside_mask(b_ext.shape, depth, totals)
    coefs = [c * 0.0625 for c in coefs_of(b_ext, padded_neighbours(jnp.pad(b_ext, 1)))]
    diag = sum(coefs)
    inv_diag = jnp.where(inside, 1.0 / jnp.where(inside, diag, 1.0), 0.0)

    low, high = (0.05, 2.0)
    theta = (high + low) / 2.0
    delta = (high - low) / 2.0
    sigma = theta / delta
    rho = 1.0 / sigma
    solution = jnp.zeros_like(rhs_ext)
    remain = jnp.where(inside, rhs_ext, 0.0)
    direction = remain * inv_diag / theta
    for step in range(CHEB):
        solution = solution + direction
        if step + 1 < CHEB:
            nears = padded_neighbours(jnp.pad(direction, 1))
            remain = remain - apply_op(direction, nears, coefs)
            rho_next = 1.0 / (2.0 * sigma - rho)
            direction = rho_next * rho * direction + 2.0 * rho_next / delta * remain * inv_diag
            rho = rho_next
    return solution[depth:depth + cx, depth:depth + cy]


def grid_mask(shape, depth, axes, totals):
    inside = None
    for dim, (axis, total) in enumerate(zip(axes, totals)):
        own = shape[dim] - 2 * depth
        g = lax.axis_index(axis) * own - depth + lax.broadcasted_iota(jnp.int32, shape, dim)
        ok = (g >= 0) & (g < total)
        inside = ok if inside is None else inside & ok
    return inside


def shared_faces(b):
    def face(a, n):
        return jnp.where((a > 0) & (n > 0), 2.0 * a * n / (a + n), a + n)

    nears = padded_neighbours(jnp.pad(b, 1))
    lx, ly, lz = face(b, nears[0]), face(b, nears[2]), face(b, nears[4])
    hx = jnp.pad(lx, ((0, 1), (0, 0), (0, 0)))[1:]
    hy = jnp.pad(ly, ((0, 0), (0, 1), (0, 0)))[:, 1:]
    hz = jnp.pad(lz, ((0, 0), (0, 0), (0, 1)))[:, :, 1:]
    top = lax.broadcasted_iota(jnp.int32, b.shape, 2) == b.shape[2] - 1
    return [lx, hx, ly, hy, lz, jnp.where(top, b, hz)]


def low_faces(b):
    faces = []
    for dim in range(3):
        n = b.shape[dim]
        lo = lax.slice_in_dim(b, 0, n - 1, axis=dim)
        hi = lax.slice_in_dim(b, 1, n, axis=dim)
        inner = jnp.where((lo > 0) & (hi > 0), 2.0 * hi * lo / (hi + lo), hi + lo)
        faces.append(jnp.concatenate([lax.slice_in_dim(b, 0, 1, axis=dim), inner], axis=dim))
    return faces


def face_pairs(b, faces):
    pairs = []
    for dim, lo in enumerate(faces):
        n = b.shape[dim]
        hi = jnp.concatenate(
            [lax.slice_in_dim(lo, 1, n, axis=dim), lax.slice_in_dim(b, n - 1, n, axis=dim)], axis=dim
        )
        pairs += [lo, hi]
    return pairs


def per_device(right_side, inv_density, pressure):
    depth = SWEEPS + 1
    sx, sy, sz = pressure.shape
    b_e, rhs_e, fine = packed_halo([inv_density, right_side, pressure], [depth, depth - 1, depth])
    rhs_e, b_e, fine = lax.optimization_barrier((rhs_e, b_e, fine))
    totals = (sx * lax.axis_size("box"), sy * lax.axis_size("group"))
    inside = grid_mask(fine.shape, depth, ("box", "group"), totals)
    coefs = shared_faces(b_e)
    diag = sum(coefs)
    for sweep in range(SWEEPS):
        step = 2.0 / 3.0 * (rhs_e - apply_op(fine, padded_neighbours(jnp.pad(fine, 1)), coefs)) / diag
        fine = jnp.where(inside, fine + step, 0.0)
    own = (slice(depth, depth + sx), slice(depth, depth + sy))
    core = fine[own]
    nears = [
        fine[depth - 1:depth - 1 + sx, depth:depth + sy],
        fine[depth + 1:depth + 1 + sx, depth:depth + sy],
        fine[depth:depth + sx, depth - 1:depth - 1 + sy],
        fine[depth:depth + sx, depth + 1:depth + 1 + sy],
        shift_z(core, -1),
        shift_z(core, 1),
    ]
    res = right_side - apply_op(core, nears, [c[own] for c in coefs])
    fine, res = lax.optimization_barrier((core, res))
    coarse_rhs = block_mean(res)
    coarse_b = block_mean(inv_density)
    corr = chebyshev_local(coarse_rhs, coarse_b)
    return fine + expand(corr, fine.shape)


def solution(mesh):
    return jax.shard_map(
        per_device,
        mesh=mesh,
        in_specs=(P("box", "group", None), P("box", "group", None), P("box", "group", None)),
        out_specs=P("box", "group", None),
        check_vma=False,
    )
```

```python
import jax
import jax.numpy as jnp
from jax import lax
from jax.sharding import PartitionSpec as P

SWEEPS = 2
CHEB = 8
HIGHEST = lax.Precision.HIGHEST


def shifted_pairs(count, hop):
    return [(i, i + hop) for i in range(count - hop)]


def halo_from(block, axis, dim, width, hop):
    count = lax.axis_size(axis)
    n = block.shape[dim]
    if hop >= count:
        shape = list(block.shape)
        shape[dim] = width
        zeros = jnp.zeros(shape, block.dtype)
        return zeros, zeros
    forward = shifted_pairs(count, hop)
    backward = [(t, s) for s, t in forward]
    low = lax.ppermute(lax.slice_in_dim(block, n - width, n, axis=dim), axis, forward)
    high = lax.ppermute(lax.slice_in_dim(block, 0, width, axis=dim), axis, backward)
    return low, high


def deep_extend(block, axis, dim, depth):
    n = block.shape[dim]
    lows, highs = [], []
    need, hop = depth, 1
    while need > 0:
        width = min(n, need)
        low, high = halo_from(block, axis, dim, width, hop)
        lows.insert(0, low)
        highs.append(high)
        need -= width
        hop += 1
    return jnp.concatenate(lows + [block] + highs, axis=dim)


def packed_halo(fields, depths):
    top = max(depths)
    assert top <= fields[0].shape[0] and top <= fields[0].shape[1]
    offs = [sum(depths[:k]) for k in range(len(depths))]
    up = lambda f, d, dim: lax.slice_in_dim(f, f.shape[dim] - d, f.shape[dim], axis=dim)
    down = lambda f, d, dim: lax.slice_in_dim(f, 0, d, axis=dim)
    nb, ng = lax.axis_size("box"), lax.axis_size("group")
    fb, bb = shifted_pairs(nb, 1), [(t, s) for s, t in shifted_pairs(nb, 1)]
    fg, bg = shifted_pairs(ng, 1), [(t, s) for s, t in shifted_pairs(ng, 1)]

    def send(pieces, axis, pairs, dim):
        msg = jnp.concatenate(pieces, axis=dim)
        if not pairs:
            return jnp.zeros_like(msg)
        return lax.ppermute(msg, axis, pairs)

    xl = send([up(f, d, 0) for f, d in zip(fields, depths)], "box", fb, 0)
    xh = send([down(f, d, 0) for f, d in zip(fields, depths)], "box", bb, 0)
    yl = send([up(f, d, 1) for f, d in zip(fields, depths)], "group", fg, 1)
    yh = send([down(f, d, 1) for f, d in zip(fields, depths)], "group", bg, 1)
    low = send([up(yl, top, 0), up(yh, top, 0)], "box", fb, 1)
    high = send([down(yl, top, 0), down(yh, top, 0)], "box", bb, 1)
    total = sum(depths)
    out = []
    for f, d, o in zip(fields, depths, offs):
        lo_win = slice(o + d - top, o + d)
        hi_win = slice(o, o + top)
        assert lo_win.start >= 0 and hi_win.stop <= total
        hi_win2 = slice(total + hi_win.start, total + hi_win.stop)
        rows = [
            jnp.concatenate([low[:, lo_win], xl[lo_win], low[:, hi_win2]], axis=1),
            jnp.concatenate([yl[:, lo_win], f, yh[:, hi_win]], axis=1),
            jnp.concatenate([high[:, lo_win], xh[hi_win], high[:, hi_win2]], axis=1),
        ]
        out.append(jnp.concatenate(rows, axis=0))
    return out


def shift_z(field, side):
    zeros = jnp.zeros_like(field[:, :, :1])
    if side < 0:
        return jnp.concatenate([zeros, field[:, :, :-1]], axis=2)
    return jnp.concatenate([field[:, :, 1:], zeros], axis=2)


def padded_neighbours(padded):
    return [
        padded[:-2, 1:-1, 1:-1],
        padded[2:, 1:-1, 1:-1],
        padded[1:-1, :-2, 1:-1],
        padded[1:-1, 2:, 1:-1],
        padded[1:-1, 1:-1, :-2],
        padded[1:-1, 1:-1, 2:],
    ]


def coefs_of(field, nears):
    return [jnp.where(near > 0, 2.0 * field * near / (field + near), field) for near in nears]


def apply_op(field, nears, coefs):
    total = jnp.zeros_like(field)
    for coef, near in zip(coefs, nears):
        total = total + coef * (field - near)
    return total


def group_matrix(n, k):
    rows = lax.broadcasted_iota(jnp.int32, (n, n // k), 0) // k
    cols = lax.broadcasted_iota(jnp.int32, (n, n // k), 1)
    return (rows == cols).astype(jnp.float32)


def block_mean(field):
    sx, sy, sz = field.shape
    fx = field.reshape(sx // 4, 4, sy, sz).sum(axis=1)
    fz = jnp.einsum("xyz,zc->xyc", fx, group_matrix(sz, 4), precision=HIGHEST)
    fy = jnp.einsum("xyc,yb->xbc", fz, group_matrix(sy, 4), precision=HIGHEST)
    return fy * (1.0 / 64.0)


def expand(coarse, shape):
    sx, sy, sz = shape
    cz = jnp.einsum("xbc,zc->xbz", coarse, group_matrix(sz, 4), precision=HIGHEST)
    cy = jnp.einsum("xbz,yb->xyz", cz, group_matrix(sy, 4), precision=HIGHEST)
    return jnp.broadcast_to(cy[:, None], (sx // 4, 4, sy, sz)).reshape(sx, sy, sz)


def inside_mask(shape, depth, totals):
    ex, ey, ez = shape
    cx, cy = ex - 2 * depth, ey - 2 * depth
    gx = lax.axis_index("box") * cx - depth + lax.broadcasted_iota(jnp.int32, shape, 0)
    gy = lax.axis_index("group") * cy - depth + lax.broadcasted_iota(jnp.int32, shape, 1)
    return (gx >= 0) & (gx < totals[0]) & (gy >= 0) & (gy < totals[1])


def pair_extend(block, depth):
    nb = lax.axis_size("box")
    n = block.shape[1]
    odd = lax.axis_index("box") % 2
    partner = lax.ppermute(block, "box", [(i, i ^ 1) for i in range(nb)])
    pair = jnp.where(odd == 0, jnp.concatenate([block, partner], axis=1),
                     jnp.concatenate([partner, block], axis=1))
    low = lax.ppermute(pair, "box", shifted_pairs(nb, 2))
    high = lax.ppermute(pair, "box", [(t, s) for s, t in shifted_pairs(nb, 2)])
    span = jnp.concatenate([low, pair, high], axis=1)
    start = 2 * n - depth + odd * n
    return lax.dynamic_slice_in_dim(span, start, n + 2 * depth, axis=1)


def chebyshev_local(rhs_c, b_c):
    depth = CHEB
    cx, cy, cz = rhs_c.shape
    both = jnp.stack([b_c, rhs_c])
    nb = lax.axis_size("box")
    if nb % 2 == 0 and nb > 2 and cx < depth <= 2 * cx:
        both = pair_extend(both, depth)
    else:
        both = deep_extend(both, "box", 1, depth)
    edge = jnp.zeros_like(both[:, :1, :depth])
    inner = deep_extend(both[:, 1:-1], "group", 2, depth)
    both = jnp.concatenate([
        jnp.concatenate([edge, both[:, :1], edge], axis=2),
        inner,
        jnp.concatenate([edge, both[:, -1:], edge], axis=2),
    ], axis=1)
    b_ext, rhs_ext = both[0], both[1]
    totals = (cx * lax.axis_size("box"), cy * lax.axis_size("group"))
    inside = inside_mask(b_ext.shape, depth, totals)
    coefs = [c * 0.0625 for c in coefs_of(b_ext, padded_neighbours(jnp.pad(b_ext, 1)))]
    diag = sum(coefs)
    inv_diag = jnp.where(inside, 1.0 / jnp.where(inside, diag, 1.0), 0.0)

    low, high = (0.05, 2.0)
    theta = (high + low) / 2.0
    delta = (high - low) / 2.0
    sigma = theta / delta
    rho = 1.0 / sigma
    solution = jnp.zeros_like(rhs_ext)
    remain = jnp.where(inside, rhs_ext, 0.0)
    direction = remain * inv_diag / theta
    for step in range(CHEB):
        solution = solution + direction
        if step + 1 < CHEB:
            nears = padded_neighbours(jnp.pad(direction, 1))
            remain = remain - apply_op(direction, nears, coefs)
            rho_next = 1.0 / (2.0 * sigma - rho)
            direction = rho_next * rho * direction + 2.0 * rho_next / delta * remain * inv_diag
            rho = rho_next
    return solution[depth:depth + cx, depth:depth + cy]


def grid_mask(shape, depth, axes, totals):
    inside = None
    for dim, (axis, total) in enumerate(zip(axes, totals)):
        own = shape[dim] - 2 * depth
        g = lax.axis_index(axis) * own - depth + lax.broadcasted_iota(jnp.int32, shape, dim)
        ok = (g >= 0) & (g < total)
        inside = ok if inside is None else inside & ok
    return inside


def shared_faces(b):
    def face(a, n):
        return jnp.where((a > 0) & (n > 0), 2.0 * a * n / (a + n), a + n)

    nears = padded_neighbours(jnp.pad(b, 1))
    lx, ly, lz = face(b, nears[0]), face(b, nears[2]), face(b, nears[4])
    hx = jnp.pad(lx, ((0, 1), (0, 0), (0, 0)))[1:]
    hy = jnp.pad(ly, ((0, 0), (0, 1), (0, 0)))[:, 1:]
    hz = jnp.pad(lz, ((0, 0), (0, 0), (0, 1)))[:, :, 1:]
    top = lax.broadcasted_iota(jnp.int32, b.shape, 2) == b.shape[2] - 1
    return [lx, hx, ly, hy, lz, jnp.where(top, b, hz)]


def low_faces(b):
    faces = []
    for dim in range(3):
        n = b.shape[dim]
        lo = lax.slice_in_dim(b, 0, n - 1, axis=dim)
        hi = lax.slice_in_dim(b, 1, n, axis=dim)
        inner = jnp.where((lo > 0) & (hi > 0), 2.0 * hi * lo / (hi + lo), hi + lo)
        faces.append(jnp.concatenate([lax.slice_in_dim(b, 0, 1, axis=dim), inner], axis=dim))
    return faces


def face_pairs(b, faces):
    pairs = []
    for dim, lo in enumerate(faces):
        n = b.shape[dim]
        hi = jnp.concatenate(
            [lax.slice_in_dim(lo, 1, n, axis=dim), lax.slice_in_dim(b, n - 1, n, axis=dim)], axis=dim
        )
        pairs += [lo, hi]
    return pairs


def per_device(right_side, inv_density, pressure):
    depth = SWEEPS + 1
    sx, sy, sz = pressure.shape
    b_e, rhs_e, fine = packed_halo([inv_density, right_side, pressure], [depth, depth - 1, depth])
    rhs_e, b_e, fine = lax.optimization_barrier((rhs_e, b_e, fine))
    totals = (sx * lax.axis_size("box"), sy * lax.axis_size("group"))
    inside = grid_mask(fine.shape, depth, ("box", "group"), totals)
    coefs = shared_faces(b_e)
    diag = sum(coefs)
    for sweep in range(SWEEPS):
        step = 2.0 / 3.0 * (rhs_e - apply_op(fine, padded_neighbours(jnp.pad(fine, 1)), coefs)) / diag
        fine = jnp.where(inside, fine + step, 0.0)
    own = (slice(depth, depth + sx), slice(depth, depth + sy))
    core = fine[own]
    nears = [
        fine[depth - 1:depth - 1 + sx, depth:depth + sy],
        fine[depth + 1:depth + 1 + sx, depth:depth + sy],
        fine[depth:depth + sx, depth - 1:depth - 1 + sy],
        fine[depth:depth + sx, depth + 1:depth + 1 + sy],
        shift_z(core, -1),
        shift_z(core, 1),
    ]
    res = right_side - apply_op(core, nears, [c[own] for c in coefs])
    fine, res = lax.optimization_barrier((core, res))
    coarse_rhs = block_mean(res)
    coarse_b = block_mean(inv_density)
    corr = chebyshev_local(coarse_rhs, coarse_b)
    return fine + expand(corr, fine.shape)


def solution(mesh):
    return jax.shard_map(
        per_device,
        mesh=mesh,
        in_specs=(P("box", "group", None), P("box", "group", None), P("box", "group", None)),
        out_specs=P("box", "group", None),
        check_vma=False,
    )
```

```python
import jax
import jax.numpy as jnp
from jax import lax
from jax.sharding import PartitionSpec as P

SWEEPS = 2
CHEB = 8
HIGHEST = lax.Precision.HIGHEST


def shifted_pairs(count, hop):
    return [(i, i + hop) for i in range(count - hop)]


def halo_from(block, axis, dim, width, hop):
    count = lax.axis_size(axis)
    n = block.shape[dim]
    if hop >= count:
        shape = list(block.shape)
        shape[dim] = width
        zeros = jnp.zeros(shape, block.dtype)
        return zeros, zeros
    forward = shifted_pairs(count, hop)
    backward = [(t, s) for s, t in forward]
    low = lax.ppermute(lax.slice_in_dim(block, n - width, n, axis=dim), axis, forward)
    high = lax.ppermute(lax.slice_in_dim(block, 0, width, axis=dim), axis, backward)
    return low, high


def deep_extend(block, axis, dim, depth):
    n = block.shape[dim]
    lows, highs = [], []
    need, hop = depth, 1
    while need > 0:
        width = min(n, need)
        low, high = halo_from(block, axis, dim, width, hop)
        lows.insert(0, low)
        highs.append(high)
        need -= width
        hop += 1
    return jnp.concatenate(lows + [block] + highs, axis=dim)


def packed_halo(fields, depths):
    top = max(depths)
    assert top <= fields[0].shape[0] and top <= fields[0].shape[1]
    offs = [sum(depths[:k]) for k in range(len(depths))]
    up = lambda f, d, dim: lax.slice_in_dim(f, f.shape[dim] - d, f.shape[dim], axis=dim)
    down = lambda f, d, dim: lax.slice_in_dim(f, 0, d, axis=dim)
    nb, ng = lax.axis_size("box"), lax.axis_size("group")
    fb, bb = shifted_pairs(nb, 1), [(t, s) for s, t in shifted_pairs(nb, 1)]
    fg, bg = shifted_pairs(ng, 1), [(t, s) for s, t in shifted_pairs(ng, 1)]

    def send(pieces, axis, pairs, dim):
        msg = jnp.concatenate(pieces, axis=dim)
        if not pairs:
            return jnp.zeros_like(msg)
        return lax.ppermute(msg, axis, pairs)

    xl = send([up(f, d, 0) for f, d in zip(fields, depths)], "box", fb, 0)
    xh = send([down(f, d, 0) for f, d in zip(fields, depths)], "box", bb, 0)
    yl = send([up(f, d, 1) for f, d in zip(fields, depths)], "group", fg, 1)
    yh = send([down(f, d, 1) for f, d in zip(fields, depths)], "group", bg, 1)
    low = send([up(yl, top, 0), up(yh, top, 0)], "box", fb, 1)
    high = send([down(yl, top, 0), down(yh, top, 0)], "box", bb, 1)
    total = sum(depths)
    out = []
    for f, d, o in zip(fields, depths, offs):
        lo_win = slice(o + d - top, o + d)
        hi_win = slice(o, o + top)
        assert lo_win.start >= 0 and hi_win.stop <= total
        hi_win2 = slice(total + hi_win.start, total + hi_win.stop)
        rows = [
            jnp.concatenate([low[:, lo_win], xl[lo_win], low[:, hi_win2]], axis=1),
            jnp.concatenate([yl[:, lo_win], f, yh[:, hi_win]], axis=1),
            jnp.concatenate([high[:, lo_win], xh[hi_win], high[:, hi_win2]], axis=1),
        ]
        out.append(jnp.concatenate(rows, axis=0))
    return out


def shift_z(field, side):
    zeros = jnp.zeros_like(field[:, :, :1])
    if side < 0:
        return jnp.concatenate([zeros, field[:, :, :-1]], axis=2)
    return jnp.concatenate([field[:, :, 1:], zeros], axis=2)


def padded_neighbours(padded):
    return [
        padded[:-2, 1:-1, 1:-1],
        padded[2:, 1:-1, 1:-1],
        padded[1:-1, :-2, 1:-1],
        padded[1:-1, 2:, 1:-1],
        padded[1:-1, 1:-1, :-2],
        padded[1:-1, 1:-1, 2:],
    ]


def coefs_of(field, nears):
    return [jnp.where(near > 0, 2.0 * field * near / (field + near), field) for near in nears]


def apply_op(field, nears, coefs):
    total = jnp.zeros_like(field)
    for coef, near in zip(coefs, nears):
        total = total + coef * (field - near)
    return total


def group_matrix(n, k):
    rows = lax.broadcasted_iota(jnp.int32, (n, n // k), 0) // k
    cols = lax.broadcasted_iota(jnp.int32, (n, n // k), 1)
    return (rows == cols).astype(jnp.float32)


def block_mean(field):
    sx, sy, sz = field.shape
    fx = field.reshape(sx // 4, 4, sy, sz).sum(axis=1)
    fz = jnp.einsum("xyz,zc->xyc", fx, group_matrix(sz, 4), precision=HIGHEST)
    fy = jnp.einsum("xyc,yb->xbc", fz, group_matrix(sy, 4), precision=HIGHEST)
    return fy * (1.0 / 64.0)


def expand(coarse, shape):
    sx, sy, sz = shape
    cz = jnp.einsum("xbc,zc->xbz", coarse, group_matrix(sz, 4), precision=HIGHEST)
    cy = jnp.einsum("xbz,yb->xyz", cz, group_matrix(sy, 4), precision=HIGHEST)
    return jnp.broadcast_to(cy[:, None], (sx // 4, 4, sy, sz)).reshape(sx, sy, sz)


def inside_mask(shape, depth, totals):
    ex, ey, ez = shape
    cx, cy = ex - 2 * depth, ey - 2 * depth
    gx = lax.axis_index("box") * cx - depth + lax.broadcasted_iota(jnp.int32, shape, 0)
    gy = lax.axis_index("group") * cy - depth + lax.broadcasted_iota(jnp.int32, shape, 1)
    return (gx >= 0) & (gx < totals[0]) & (gy >= 0) & (gy < totals[1])


def pair_extend(block, depth):
    nb = lax.axis_size("box")
    n = block.shape[1]
    odd = lax.axis_index("box") % 2
    partner = lax.ppermute(block, "box", [(i, i ^ 1) for i in range(nb)])
    pair = jnp.where(odd == 0, jnp.concatenate([block, partner], axis=1),
                     jnp.concatenate([partner, block], axis=1))
    low = lax.ppermute(pair, "box", shifted_pairs(nb, 2))
    high = lax.ppermute(pair, "box", [(t, s) for s, t in shifted_pairs(nb, 2)])
    span = jnp.concatenate([low, pair, high], axis=1)
    start = 2 * n - depth + odd * n
    return lax.dynamic_slice_in_dim(span, start, n + 2 * depth, axis=1)


def chebyshev_local(rhs_c, b_c):
    depth = CHEB
    cx, cy, cz = rhs_c.shape
    both = jnp.stack([b_c, rhs_c])
    nb = lax.axis_size("box")
    if nb % 2 == 0 and nb > 2 and cx < depth <= 2 * cx:
        both = pair_extend(both, depth)
    else:
        both = deep_extend(both, "box", 1, depth)
    both = deep_extend(both, "group", 2, depth)
    b_ext, rhs_ext = both[0], both[1]
    totals = (cx * lax.axis_size("box"), cy * lax.axis_size("group"))
    inside = inside_mask(b_ext.shape, depth, totals)
    coefs = [c * 0.0625 for c in coefs_of(b_ext, padded_neighbours(jnp.pad(b_ext, 1)))]
    diag = sum(coefs)
    inv_diag = jnp.where(inside, 1.0 / jnp.where(inside, diag, 1.0), 0.0)

    low, high = (0.05, 2.0)
    theta = (high + low) / 2.0
    delta = (high - low) / 2.0
    sigma = theta / delta
    rho = 1.0 / sigma
    solution = jnp.zeros_like(rhs_ext)
    remain = jnp.where(inside, rhs_ext, 0.0)
    direction = remain * inv_diag / theta
    for step in range(CHEB):
        solution = solution + direction
        if step + 1 < CHEB:
            nears = padded_neighbours(jnp.pad(direction, 1))
            remain = remain - apply_op(direction, nears, coefs)
            rho_next = 1.0 / (2.0 * sigma - rho)
            direction = rho_next * rho * direction + 2.0 * rho_next / delta * remain * inv_diag
            rho = rho_next
    return solution[depth:depth + cx, depth:depth + cy]


def grid_mask(shape, depth, axes, totals):
    inside = None
    for dim, (axis, total) in enumerate(zip(axes, totals)):
        own = shape[dim] - 2 * depth
        g = lax.axis_index(axis) * own - depth + lax.broadcasted_iota(jnp.int32, shape, dim)
        ok = (g >= 0) & (g < total)
        inside = ok if inside is None else inside & ok
    return inside


def shared_faces(b):
    def face(a, n):
        return jnp.where((a > 0) & (n > 0), 2.0 * a * n / (a + n), a + n)

    nears = padded_neighbours(jnp.pad(b, 1))
    lx, ly, lz = face(b, nears[0]), face(b, nears[2]), face(b, nears[4])
    hx = jnp.pad(lx, ((0, 1), (0, 0), (0, 0)))[1:]
    hy = jnp.pad(ly, ((0, 0), (0, 1), (0, 0)))[:, 1:]
    hz = jnp.pad(lz, ((0, 0), (0, 0), (0, 1)))[:, :, 1:]
    top = lax.broadcasted_iota(jnp.int32, b.shape, 2) == b.shape[2] - 1
    return [lx, hx, ly, hy, lz, jnp.where(top, b, hz)]


def low_faces(b):
    faces = []
    for dim in range(3):
        n = b.shape[dim]
        lo = lax.slice_in_dim(b, 0, n - 1, axis=dim)
        hi = lax.slice_in_dim(b, 1, n, axis=dim)
        inner = jnp.where((lo > 0) & (hi > 0), 2.0 * hi * lo / (hi + lo), hi + lo)
        faces.append(jnp.concatenate([lax.slice_in_dim(b, 0, 1, axis=dim), inner], axis=dim))
    return faces


def face_pairs(b, faces):
    pairs = []
    for dim, lo in enumerate(faces):
        n = b.shape[dim]
        hi = jnp.concatenate(
            [lax.slice_in_dim(lo, 1, n, axis=dim), lax.slice_in_dim(b, n - 1, n, axis=dim)], axis=dim
        )
        pairs += [lo, hi]
    return pairs


def per_device(right_side, inv_density, pressure):
    depth = SWEEPS + 1
    sx, sy, sz = pressure.shape
    b_e, rhs_e, fine = packed_halo([inv_density, right_side, pressure], [depth, depth - 1, depth])
    rhs_e, b_e, fine = lax.optimization_barrier((rhs_e, b_e, fine))
    totals = (sx * lax.axis_size("box"), sy * lax.axis_size("group"))
    inside = grid_mask(fine.shape, depth, ("box", "group"), totals)
    coefs = shared_faces(b_e)
    diag = sum(coefs)
    for sweep in range(SWEEPS):
        step = 2.0 / 3.0 * (rhs_e - apply_op(fine, padded_neighbours(jnp.pad(fine, 1)), coefs)) / diag
        fine = jnp.where(inside, fine + step, 0.0)
    own = (slice(depth, depth + sx), slice(depth, depth + sy))
    core = fine[own]
    nears = [
        fine[depth - 1:depth - 1 + sx, depth:depth + sy],
        fine[depth + 1:depth + 1 + sx, depth:depth + sy],
        fine[depth:depth + sx, depth - 1:depth - 1 + sy],
        fine[depth:depth + sx, depth + 1:depth + 1 + sy],
        shift_z(core, -1),
        shift_z(core, 1),
    ]
    res = right_side - apply_op(core, nears, [c[own] for c in coefs])
    fine, res = core, lax.optimization_barrier(res)
    coarse_rhs = block_mean(res)
    coarse_b = block_mean(inv_density)
    corr = chebyshev_local(coarse_rhs, coarse_b)
    return fine + expand(corr, fine.shape)


def solution(mesh):
    return jax.shard_map(
        per_device,
        mesh=mesh,
        in_specs=(P("box", "group", None), P("box", "group", None), P("box", "group", None)),
        out_specs=P("box", "group", None),
        check_vma=False,
    )
```

```python
import jax
import jax.numpy as jnp
from jax import lax
from jax.sharding import PartitionSpec as P

SWEEPS = 2
CHEB = 8
HIGHEST = lax.Precision.HIGHEST


def shifted_pairs(count, hop):
    return [(i, i + hop) for i in range(count - hop)]


def halo_from(block, axis, dim, width, hop):
    count = lax.axis_size(axis)
    n = block.shape[dim]
    if hop >= count:
        shape = list(block.shape)
        shape[dim] = width
        zeros = jnp.zeros(shape, block.dtype)
        return zeros, zeros
    forward = shifted_pairs(count, hop)
    backward = [(t, s) for s, t in forward]
    low = lax.ppermute(lax.slice_in_dim(block, n - width, n, axis=dim), axis, forward)
    high = lax.ppermute(lax.slice_in_dim(block, 0, width, axis=dim), axis, backward)
    return low, high


def deep_extend(block, axis, dim, depth):
    n = block.shape[dim]
    lows, highs = [], []
    need, hop = depth, 1
    while need > 0:
        width = min(n, need)
        low, high = halo_from(block, axis, dim, width, hop)
        lows.insert(0, low)
        highs.append(high)
        need -= width
        hop += 1
    return jnp.concatenate(lows + [block] + highs, axis=dim)


def packed_halo(fields, depths):
    top = max(depths)
    assert top <= fields[0].shape[0] and top <= fields[0].shape[1]
    offs = [sum(depths[:k]) for k in range(len(depths))]
    up = lambda f, d, dim: lax.slice_in_dim(f, f.shape[dim] - d, f.shape[dim], axis=dim)
    down = lambda f, d, dim: lax.slice_in_dim(f, 0, d, axis=dim)
    nb, ng = lax.axis_size("box"), lax.axis_size("group")
    fb, bb = shifted_pairs(nb, 1), [(t, s) for s, t in shifted_pairs(nb, 1)]
    fg, bg = shifted_pairs(ng, 1), [(t, s) for s, t in shifted_pairs(ng, 1)]

    def send(pieces, axis, pairs, dim):
        msg = jnp.concatenate(pieces, axis=dim)
        if not pairs:
            return jnp.zeros_like(msg)
        return lax.ppermute(msg, axis, pairs)

    xl = send([up(f, d, 0) for f, d in zip(fields, depths)], "box", fb, 0)
    xh = send([down(f, d, 0) for f, d in zip(fields, depths)], "box", bb, 0)
    yl = send([up(f, d, 1) for f, d in zip(fields, depths)], "group", fg, 1)
    yh = send([down(f, d, 1) for f, d in zip(fields, depths)], "group", bg, 1)
    low = send([up(yl, top, 0), up(yh, top, 0)], "box", fb, 1)
    high = send([down(yl, top, 0), down(yh, top, 0)], "box", bb, 1)
    total = sum(depths)
    out = []
    for f, d, o in zip(fields, depths, offs):
        lo_win = slice(o + d - top, o + d)
        hi_win = slice(o, o + top)
        assert lo_win.start >= 0 and hi_win.stop <= total
        hi_win2 = slice(total + hi_win.start, total + hi_win.stop)
        rows = [
            jnp.concatenate([low[:, lo_win], xl[lo_win], low[:, hi_win2]], axis=1),
            jnp.concatenate([yl[:, lo_win], f, yh[:, hi_win]], axis=1),
            jnp.concatenate([high[:, lo_win], xh[hi_win], high[:, hi_win2]], axis=1),
        ]
        out.append(jnp.concatenate(rows, axis=0))
    return out


def shift_z(field, side):
    zeros = jnp.zeros_like(field[:, :, :1])
    if side < 0:
        return jnp.concatenate([zeros, field[:, :, :-1]], axis=2)
    return jnp.concatenate([field[:, :, 1:], zeros], axis=2)


def padded_neighbours(padded):
    return [
        padded[:-2, 1:-1, 1:-1],
        padded[2:, 1:-1, 1:-1],
        padded[1:-1, :-2, 1:-1],
        padded[1:-1, 2:, 1:-1],
        padded[1:-1, 1:-1, :-2],
        padded[1:-1, 1:-1, 2:],
    ]


def coefs_of(field, nears):
    return [jnp.where(near > 0, 2.0 * field * near / (field + near), field) for near in nears]


def apply_op(field, nears, coefs):
    total = jnp.zeros_like(field)
    for coef, near in zip(coefs, nears):
        total = total + coef * (field - near)
    return total


def group_matrix(n, k):
    rows = lax.broadcasted_iota(jnp.int32, (n, n // k), 0) // k
    cols = lax.broadcasted_iota(jnp.int32, (n, n // k), 1)
    return (rows == cols).astype(jnp.float32)


def block_mean(field):
    sx, sy, sz = field.shape
    fx = field.reshape(sx // 4, 4, sy, sz).sum(axis=1)
    fz = jnp.einsum("xyz,zc->xyc", fx, group_matrix(sz, 4), precision=HIGHEST)
    fy = jnp.einsum("xyc,yb->xbc", fz, group_matrix(sy, 4), precision=HIGHEST)
    return fy * (1.0 / 64.0)


def expand(coarse, shape):
    sx, sy, sz = shape
    cz = jnp.einsum("xbc,zc->xbz", coarse, group_matrix(sz, 4), precision=HIGHEST)
    cy = jnp.einsum("xbz,yb->xyz", cz, group_matrix(sy, 4), precision=HIGHEST)
    return jnp.broadcast_to(cy[:, None], (sx // 4, 4, sy, sz)).reshape(sx, sy, sz)


def inside_mask(shape, depth, totals):
    ex, ey, ez = shape
    cx, cy = ex - 2 * depth, ey - 2 * depth
    gx = lax.axis_index("box") * cx - depth + lax.broadcasted_iota(jnp.int32, shape, 0)
    gy = lax.axis_index("group") * cy - depth + lax.broadcasted_iota(jnp.int32, shape, 1)
    return (gx >= 0) & (gx < totals[0]) & (gy >= 0) & (gy < totals[1])


def pair_extend(block, depth):
    nb = lax.axis_size("box")
    n = block.shape[1]
    odd = lax.axis_index("box") % 2
    partner = lax.ppermute(block, "box", [(i, i ^ 1) for i in range(nb)])
    pair = jnp.where(odd == 0, jnp.concatenate([block, partner], axis=1),
                     jnp.concatenate([partner, block], axis=1))
    low = lax.ppermute(pair, "box", shifted_pairs(nb, 2))
    high = lax.ppermute(pair, "box", [(t, s) for s, t in shifted_pairs(nb, 2)])
    span = jnp.concatenate([low, pair, high], axis=1)
    start = 2 * n - depth + odd * n
    return lax.dynamic_slice_in_dim(span, start, n + 2 * depth, axis=1)


def chebyshev_local(rhs_c, b_c):
    depth = CHEB
    cx, cy, cz = rhs_c.shape
    both = jnp.stack([b_c, rhs_c])
    nb = lax.axis_size("box")
    if nb % 2 == 0 and nb > 2 and cx < depth <= 2 * cx:
        both = pair_extend(both, depth)
    else:
        both = deep_extend(both, "box", 1, depth)
    both = deep_extend(both, "group", 2, depth)
    b_ext, rhs_ext = both[0], both[1]
    totals = (cx * lax.axis_size("box"), cy * lax.axis_size("group"))
    inside = inside_mask(b_ext.shape, depth, totals)
    coefs = [c * 0.0625 for c in coefs_of(b_ext, padded_neighbours(jnp.pad(b_ext, 1)))]
    diag = sum(coefs)
    inv_diag = jnp.where(inside, 1.0 / jnp.where(inside, diag, 1.0), 0.0)

    low, high = (0.05, 2.0)
    theta = (high + low) / 2.0
    delta = (high - low) / 2.0
    sigma = theta / delta
    rho = 1.0 / sigma
    solution = jnp.zeros_like(rhs_ext)
    remain = jnp.where(inside, rhs_ext, 0.0)
    direction = remain * inv_diag / theta
    for step in range(CHEB):
        solution = solution + direction
        if step + 1 < CHEB:
            nears = padded_neighbours(jnp.pad(direction, 1))
            remain = remain - apply_op(direction, nears, coefs)
            rho_next = 1.0 / (2.0 * sigma - rho)
            direction = rho_next * rho * direction + 2.0 * rho_next / delta * remain * inv_diag
            rho = rho_next
    return solution[depth:depth + cx, depth:depth + cy]


def grid_mask(shape, depth, axes, totals):
    inside = None
    for dim, (axis, total) in enumerate(zip(axes, totals)):
        own = shape[dim] - 2 * depth
        g = lax.axis_index(axis) * own - depth + lax.broadcasted_iota(jnp.int32, shape, dim)
        ok = (g >= 0) & (g < total)
        inside = ok if inside is None else inside & ok
    return inside


def shared_faces(b):
    def face(a, n):
        return jnp.where((a > 0) & (n > 0), 2.0 * a * n / (a + n), a + n)

    nears = padded_neighbours(jnp.pad(b, 1))
    lx, ly, lz = face(b, nears[0]), face(b, nears[2]), face(b, nears[4])
    hx = jnp.pad(lx, ((0, 1), (0, 0), (0, 0)))[1:]
    hy = jnp.pad(ly, ((0, 0), (0, 1), (0, 0)))[:, 1:]
    hz = jnp.pad(lz, ((0, 0), (0, 0), (0, 1)))[:, :, 1:]
    top = lax.broadcasted_iota(jnp.int32, b.shape, 2) == b.shape[2] - 1
    return [lx, hx, ly, hy, lz, jnp.where(top, b, hz)]


def low_faces(b):
    faces = []
    for dim in range(3):
        n = b.shape[dim]
        lo = lax.slice_in_dim(b, 0, n - 1, axis=dim)
        hi = lax.slice_in_dim(b, 1, n, axis=dim)
        inner = jnp.where((lo > 0) & (hi > 0), 2.0 * hi * lo / (hi + lo), hi + lo)
        faces.append(jnp.concatenate([lax.slice_in_dim(b, 0, 1, axis=dim), inner], axis=dim))
    return faces


def face_pairs(b, faces):
    pairs = []
    for dim, lo in enumerate(faces):
        n = b.shape[dim]
        hi = jnp.concatenate(
            [lax.slice_in_dim(lo, 1, n, axis=dim), lax.slice_in_dim(b, n - 1, n, axis=dim)], axis=dim
        )
        pairs += [lo, hi]
    return pairs


def per_device(right_side, inv_density, pressure):
    depth = SWEEPS + 1
    sx, sy, sz = pressure.shape
    b_e, rhs_e, fine = packed_halo([inv_density, right_side, pressure], [depth, depth - 1, depth])
    rhs_e, b_e, fine = lax.optimization_barrier((rhs_e, b_e, fine))
    totals = (sx * lax.axis_size("box"), sy * lax.axis_size("group"))
    inside = grid_mask(fine.shape, depth, ("box", "group"), totals)
    coefs = shared_faces(b_e)
    diag = sum(coefs)
    for sweep in range(SWEEPS):
        step = 2.0 / 3.0 * (rhs_e - apply_op(fine, padded_neighbours(jnp.pad(fine, 1)), coefs)) / diag
        fine = jnp.where(inside, fine + step, 0.0)
    own = (slice(depth, depth + sx), slice(depth, depth + sy))
    core = fine[own]
    nears = [
        fine[depth - 1:depth - 1 + sx, depth:depth + sy],
        fine[depth + 1:depth + 1 + sx, depth:depth + sy],
        fine[depth:depth + sx, depth - 1:depth - 1 + sy],
        fine[depth:depth + sx, depth + 1:depth + 1 + sy],
        shift_z(core, -1),
        shift_z(core, 1),
    ]
    res = right_side - apply_op(core, nears, [c[own] for c in coefs])
    fine = core
    coarse_rhs = block_mean(res)
    coarse_b = block_mean(inv_density)
    corr = chebyshev_local(coarse_rhs, coarse_b)
    return fine + expand(corr, fine.shape)


def solution(mesh):
    return jax.shard_map(
        per_device,
        mesh=mesh,
        in_specs=(P("box", "group", None), P("box", "group", None), P("box", "group", None)),
        out_specs=P("box", "group", None),
        check_vma=False,
    )
```

```python
import jax
import jax.numpy as jnp
from jax import lax
from jax.sharding import PartitionSpec as P

SWEEPS = 2
CHEB = 8
HIGHEST = lax.Precision.HIGHEST


def shifted_pairs(count, hop):
    return [(i, i + hop) for i in range(count - hop)]


def halo_from(block, axis, dim, width, hop):
    count = lax.axis_size(axis)
    n = block.shape[dim]
    if hop >= count:
        shape = list(block.shape)
        shape[dim] = width
        zeros = jnp.zeros(shape, block.dtype)
        return zeros, zeros
    forward = shifted_pairs(count, hop)
    backward = [(t, s) for s, t in forward]
    low = lax.ppermute(lax.slice_in_dim(block, n - width, n, axis=dim), axis, forward)
    high = lax.ppermute(lax.slice_in_dim(block, 0, width, axis=dim), axis, backward)
    return low, high


def deep_extend(block, axis, dim, depth):
    n = block.shape[dim]
    lows, highs = [], []
    need, hop = depth, 1
    while need > 0:
        width = min(n, need)
        low, high = halo_from(block, axis, dim, width, hop)
        lows.insert(0, low)
        highs.append(high)
        need -= width
        hop += 1
    return jnp.concatenate(lows + [block] + highs, axis=dim)


def packed_halo(fields, depths):
    top = max(depths)
    assert top <= fields[0].shape[0] and top <= fields[0].shape[1]
    offs = [sum(depths[:k]) for k in range(len(depths))]
    up = lambda f, d, dim: lax.slice_in_dim(f, f.shape[dim] - d, f.shape[dim], axis=dim)
    down = lambda f, d, dim: lax.slice_in_dim(f, 0, d, axis=dim)
    nb, ng = lax.axis_size("box"), lax.axis_size("group")
    fb, bb = shifted_pairs(nb, 1), [(t, s) for s, t in shifted_pairs(nb, 1)]
    fg, bg = shifted_pairs(ng, 1), [(t, s) for s, t in shifted_pairs(ng, 1)]

    def send(pieces, axis, pairs, dim):
        msg = jnp.concatenate(pieces, axis=dim)
        if not pairs:
            return jnp.zeros_like(msg)
        return lax.ppermute(msg, axis, pairs)

    xl = send([up(f, d, 0) for f, d in zip(fields, depths)], "box", fb, 0)
    xh = send([down(f, d, 0) for f, d in zip(fields, depths)], "box", bb, 0)
    yl = send([up(f, d, 1) for f, d in zip(fields, depths)], "group", fg, 1)
    yh = send([down(f, d, 1) for f, d in zip(fields, depths)], "group", bg, 1)
    low = send([up(yl, top, 0), up(yh, top, 0)], "box", fb, 1)
    high = send([down(yl, top, 0), down(yh, top, 0)], "box", bb, 1)
    total = sum(depths)
    out = []
    for f, d, o in zip(fields, depths, offs):
        lo_win = slice(o + d - top, o + d)
        hi_win = slice(o, o + top)
        assert lo_win.start >= 0 and hi_win.stop <= total
        hi_win2 = slice(total + hi_win.start, total + hi_win.stop)
        rows = [
            jnp.concatenate([low[:, lo_win], xl[lo_win], low[:, hi_win2]], axis=1),
            jnp.concatenate([yl[:, lo_win], f, yh[:, hi_win]], axis=1),
            jnp.concatenate([high[:, lo_win], xh[hi_win], high[:, hi_win2]], axis=1),
        ]
        out.append(jnp.concatenate(rows, axis=0))
    return out


def shift_z(field, side):
    zeros = jnp.zeros_like(field[:, :, :1])
    if side < 0:
        return jnp.concatenate([zeros, field[:, :, :-1]], axis=2)
    return jnp.concatenate([field[:, :, 1:], zeros], axis=2)


def padded_neighbours(padded):
    return [
        padded[:-2, 1:-1, 1:-1],
        padded[2:, 1:-1, 1:-1],
        padded[1:-1, :-2, 1:-1],
        padded[1:-1, 2:, 1:-1],
        padded[1:-1, 1:-1, :-2],
        padded[1:-1, 1:-1, 2:],
    ]


def coefs_of(field, nears):
    return [jnp.where(near > 0, 2.0 * field * near / (field + near), field) for near in nears]


def apply_op(field, nears, coefs):
    total = jnp.zeros_like(field)
    for coef, near in zip(coefs, nears):
        total = total + coef * (field - near)
    return total


def group_matrix(n, k):
    rows = lax.broadcasted_iota(jnp.int32, (n, n // k), 0) // k
    cols = lax.broadcasted_iota(jnp.int32, (n, n // k), 1)
    return (rows == cols).astype(jnp.float32)


def block_mean(field):
    sx, sy, sz = field.shape
    fx = field.reshape(sx // 4, 4, sy, sz).sum(axis=1)
    fz = jnp.einsum("xyz,zc->xyc", fx, group_matrix(sz, 4), precision=HIGHEST)
    fy = jnp.einsum("xyc,yb->xbc", fz, group_matrix(sy, 4), precision=HIGHEST)
    return fy * (1.0 / 64.0)


def expand(coarse, shape):
    sx, sy, sz = shape
    cz = jnp.einsum("xbc,zc->xbz", coarse, group_matrix(sz, 4), precision=HIGHEST)
    cy = jnp.einsum("xbz,yb->xyz", cz, group_matrix(sy, 4), precision=HIGHEST)
    return jnp.broadcast_to(cy[:, None], (sx // 4, 4, sy, sz)).reshape(sx, sy, sz)


def inside_mask(shape, depth, totals):
    ex, ey, ez = shape
    cx, cy = ex - 2 * depth, ey - 2 * depth
    gx = lax.axis_index("box") * cx - depth + lax.broadcasted_iota(jnp.int32, shape, 0)
    gy = lax.axis_index("group") * cy - depth + lax.broadcasted_iota(jnp.int32, shape, 1)
    return (gx >= 0) & (gx < totals[0]) & (gy >= 0) & (gy < totals[1])


def pair_extend(block, depth):
    nb = lax.axis_size("box")
    n = block.shape[1]
    odd = lax.axis_index("box") % 2
    partner = lax.ppermute(block, "box", [(i, i ^ 1) for i in range(nb)])
    pair = jnp.where(odd == 0, jnp.concatenate([block, partner], axis=1),
                     jnp.concatenate([partner, block], axis=1))
    low = lax.ppermute(pair, "box", shifted_pairs(nb, 2))
    high = lax.ppermute(pair, "box", [(t, s) for s, t in shifted_pairs(nb, 2)])
    span = jnp.concatenate([low, pair, high], axis=1)
    start = 2 * n - depth + odd * n
    return lax.dynamic_slice_in_dim(span, start, n + 2 * depth, axis=1)


def chebyshev_local(rhs_c, b_c):
    depth = CHEB
    cx, cy, cz = rhs_c.shape
    both = jnp.stack([b_c, rhs_c])
    nb = lax.axis_size("box")
    if nb % 2 == 0 and nb > 2 and cx < depth <= 2 * cx:
        both = pair_extend(both, depth)
    else:
        both = deep_extend(both, "box", 1, depth)
    both = deep_extend(both, "group", 2, depth)
    b_ext, rhs_ext = both[0], both[1]
    totals = (cx * lax.axis_size("box"), cy * lax.axis_size("group"))
    inside = inside_mask(b_ext.shape, depth, totals)
    coefs = [c * 0.0625 for c in coefs_of(b_ext, padded_neighbours(jnp.pad(b_ext, 1)))]
    diag = sum(coefs)
    inv_diag = jnp.where(inside, 1.0 / jnp.where(inside, diag, 1.0), 0.0)

    low, high = (0.05, 2.0)
    theta = (high + low) / 2.0
    delta = (high - low) / 2.0
    sigma = theta / delta
    rho = 1.0 / sigma
    solution = jnp.zeros_like(rhs_ext)
    remain = jnp.where(inside, rhs_ext, 0.0)
    direction = remain * inv_diag / theta
    for step in range(CHEB):
        solution = solution + direction
        if step + 1 < CHEB:
            nears = padded_neighbours(jnp.pad(direction, 1))
            remain = remain - apply_op(direction, nears, coefs)
            rho_next = 1.0 / (2.0 * sigma - rho)
            direction = rho_next * rho * direction + 2.0 * rho_next / delta * remain * inv_diag
            rho = rho_next
    return solution[depth:depth + cx, depth:depth + cy]


def grid_mask(shape, depth, axes, totals):
    inside = None
    for dim, (axis, total) in enumerate(zip(axes, totals)):
        own = shape[dim] - 2 * depth
        g = lax.axis_index(axis) * own - depth + lax.broadcasted_iota(jnp.int32, shape, dim)
        ok = (g >= 0) & (g < total)
        inside = ok if inside is None else inside & ok
    return inside


def shared_faces(b):
    def face(a, n):
        return jnp.where((a > 0) & (n > 0), 2.0 * a * n / (a + n), a + n)

    nears = padded_neighbours(jnp.pad(b, 1))
    lx, ly, lz = face(b, nears[0]), face(b, nears[2]), face(b, nears[4])
    hx = jnp.pad(lx, ((0, 1), (0, 0), (0, 0)))[1:]
    hy = jnp.pad(ly, ((0, 0), (0, 1), (0, 0)))[:, 1:]
    hz = jnp.pad(lz, ((0, 0), (0, 0), (0, 1)))[:, :, 1:]
    top = lax.broadcasted_iota(jnp.int32, b.shape, 2) == b.shape[2] - 1
    return [lx, hx, ly, hy, lz, jnp.where(top, b, hz)]


def low_faces(b):
    faces = []
    for dim in range(3):
        n = b.shape[dim]
        lo = lax.slice_in_dim(b, 0, n - 1, axis=dim)
        hi = lax.slice_in_dim(b, 1, n, axis=dim)
        inner = jnp.where((lo > 0) & (hi > 0), 2.0 * hi * lo / (hi + lo), hi + lo)
        faces.append(jnp.concatenate([lax.slice_in_dim(b, 0, 1, axis=dim), inner], axis=dim))
    return faces


def face_pairs(b, faces):
    pairs = []
    for dim, lo in enumerate(faces):
        n = b.shape[dim]
        hi = jnp.concatenate(
            [lax.slice_in_dim(lo, 1, n, axis=dim), lax.slice_in_dim(b, n - 1, n, axis=dim)], axis=dim
        )
        pairs += [lo, hi]
    return pairs


def per_device(right_side, inv_density, pressure):
    depth = SWEEPS + 1
    sx, sy, sz = pressure.shape
    b_e, rhs_e, fine = packed_halo([inv_density, right_side, pressure], [depth, depth - 1, depth])
    rhs_e, b_e, fine = lax.optimization_barrier((rhs_e, b_e, fine))
    totals = (sx * lax.axis_size("box"), sy * lax.axis_size("group"))
    inside = grid_mask(fine.shape, depth, ("box", "group"), totals)
    coefs = shared_faces(b_e)
    diag = sum(coefs)
    for sweep in range(SWEEPS):
        step = 2.0 / 3.0 * (rhs_e - apply_op(fine, padded_neighbours(jnp.pad(fine, 1)), coefs)) / diag
        fine = jnp.where(inside, fine + step, 0.0)
    own = (slice(depth, depth + sx), slice(depth, depth + sy))
    core = fine[own]
    nears = [
        fine[depth - 1:depth - 1 + sx, depth:depth + sy],
        fine[depth + 1:depth + 1 + sx, depth:depth + sy],
        fine[depth:depth + sx, depth - 1:depth - 1 + sy],
        fine[depth:depth + sx, depth + 1:depth + 1 + sy],
        shift_z(core, -1),
        shift_z(core, 1),
    ]
    res = right_side - apply_op(core, nears, [c[own] for c in coefs])
    fine, res = core, lax.optimization_barrier(res)
    coarse_rhs = block_mean(res)
    coarse_b = block_mean(b_e[own])
    corr = chebyshev_local(coarse_rhs, coarse_b)
    return fine + expand(corr, fine.shape)


def solution(mesh):
    return jax.shard_map(
        per_device,
        mesh=mesh,
        in_specs=(P("box", "group", None), P("box", "group", None), P("box", "group", None)),
        out_specs=P("box", "group", None),
        check_vma=False,
    )
```

```python
import jax
import jax.numpy as jnp
from jax import lax
from jax.sharding import PartitionSpec as P

SWEEPS = 2
CHEB = 8
HIGHEST = lax.Precision.HIGHEST


def shifted_pairs(count, hop):
    return [(i, i + hop) for i in range(count - hop)]


def halo_from(block, axis, dim, width, hop):
    count = lax.axis_size(axis)
    n = block.shape[dim]
    if hop >= count:
        shape = list(block.shape)
        shape[dim] = width
        zeros = jnp.zeros(shape, block.dtype)
        return zeros, zeros
    forward = shifted_pairs(count, hop)
    backward = [(t, s) for s, t in forward]
    low = lax.ppermute(lax.slice_in_dim(block, n - width, n, axis=dim), axis, forward)
    high = lax.ppermute(lax.slice_in_dim(block, 0, width, axis=dim), axis, backward)
    return low, high


def deep_extend(block, axis, dim, depth):
    n = block.shape[dim]
    lows, highs = [], []
    need, hop = depth, 1
    while need > 0:
        width = min(n, need)
        low, high = halo_from(block, axis, dim, width, hop)
        lows.insert(0, low)
        highs.append(high)
        need -= width
        hop += 1
    return jnp.concatenate(lows + [block] + highs, axis=dim)


def packed_halo(fields, depths):
    top = max(depths)
    assert top <= fields[0].shape[0] and top <= fields[0].shape[1]
    offs = [sum(depths[:k]) for k in range(len(depths))]
    up = lambda f, d, dim: lax.slice_in_dim(f, f.shape[dim] - d, f.shape[dim], axis=dim)
    down = lambda f, d, dim: lax.slice_in_dim(f, 0, d, axis=dim)
    nb, ng = lax.axis_size("box"), lax.axis_size("group")
    fb, bb = shifted_pairs(nb, 1), [(t, s) for s, t in shifted_pairs(nb, 1)]
    fg, bg = shifted_pairs(ng, 1), [(t, s) for s, t in shifted_pairs(ng, 1)]

    def send(pieces, axis, pairs, dim):
        msg = jnp.concatenate(pieces, axis=dim)
        if not pairs:
            return jnp.zeros_like(msg)
        return lax.ppermute(msg, axis, pairs)

    xl = send([up(f, d, 0) for f, d in zip(fields, depths)], "box", fb, 0)
    xh = send([down(f, d, 0) for f, d in zip(fields, depths)], "box", bb, 0)
    yl = send([up(f, d, 1) for f, d in zip(fields, depths)], "group", fg, 1)
    yh = send([down(f, d, 1) for f, d in zip(fields, depths)], "group", bg, 1)
    low = send([up(yl, top, 0), up(yh, top, 0)], "box", fb, 1)
    high = send([down(yl, top, 0), down(yh, top, 0)], "box", bb, 1)
    total = sum(depths)
    out = []
    for f, d, o in zip(fields, depths, offs):
        lo_win = slice(o + d - top, o + d)
        hi_win = slice(o, o + top)
        assert lo_win.start >= 0 and hi_win.stop <= total
        hi_win2 = slice(total + hi_win.start, total + hi_win.stop)
        rows = [
            jnp.concatenate([low[:, lo_win], xl[lo_win], low[:, hi_win2]], axis=1),
            jnp.concatenate([yl[:, lo_win], f, yh[:, hi_win]], axis=1),
            jnp.concatenate([high[:, lo_win], xh[hi_win], high[:, hi_win2]], axis=1),
        ]
        out.append(jnp.concatenate(rows, axis=0))
    return out


def shift_z(field, side):
    zeros = jnp.zeros_like(field[:, :, :1])
    if side < 0:
        return jnp.concatenate([zeros, field[:, :, :-1]], axis=2)
    return jnp.concatenate([field[:, :, 1:], zeros], axis=2)


def padded_neighbours(padded):
    return [
        padded[:-2, 1:-1, 1:-1],
        padded[2:, 1:-1, 1:-1],
        padded[1:-1, :-2, 1:-1],
        padded[1:-1, 2:, 1:-1],
        padded[1:-1, 1:-1, :-2],
        padded[1:-1, 1:-1, 2:],
    ]


def coefs_of(field, nears):
    return [jnp.where(near > 0, 2.0 * field * near / (field + near), field) for near in nears]


def apply_op(field, nears, coefs):
    total = jnp.zeros_like(field)
    for coef, near in zip(coefs, nears):
        total = total + coef * (field - near)
    return total


def group_matrix(n, k):
    rows = lax.broadcasted_iota(jnp.int32, (n, n // k), 0) // k
    cols = lax.broadcasted_iota(jnp.int32, (n, n // k), 1)
    return (rows == cols).astype(jnp.float32)


def block_mean(field):
    sx, sy, sz = field.shape
    fx = field.reshape(sx // 4, 4, sy, sz).sum(axis=1)
    fz = jnp.einsum("xyz,zc->xyc", fx, group_matrix(sz, 4), precision=HIGHEST)
    fy = jnp.einsum("xyc,yb->xbc", fz, group_matrix(sy, 4), precision=HIGHEST)
    return fy * (1.0 / 64.0)


def expand(coarse, shape):
    sx, sy, sz = shape
    cz = jnp.einsum("xbc,zc->xbz", coarse, group_matrix(sz, 4), precision=HIGHEST)
    cy = jnp.einsum("xbz,yb->xyz", cz, group_matrix(sy, 4), precision=HIGHEST)
    return jnp.broadcast_to(cy[:, None], (sx // 4, 4, sy, sz)).reshape(sx, sy, sz)


def inside_mask(shape, depth, totals):
    ex, ey, ez = shape
    cx, cy = ex - 2 * depth, ey - 2 * depth
    gx = lax.axis_index("box") * cx - depth + lax.broadcasted_iota(jnp.int32, shape, 0)
    gy = lax.axis_index("group") * cy - depth + lax.broadcasted_iota(jnp.int32, shape, 1)
    return (gx >= 0) & (gx < totals[0]) & (gy >= 0) & (gy < totals[1])


def pair_extend(block, depth):
    nb = lax.axis_size("box")
    n = block.shape[1]
    odd = lax.axis_index("box") % 2
    partner = lax.ppermute(block, "box", [(i, i ^ 1) for i in range(nb)])
    pair = jnp.where(odd == 0, jnp.concatenate([block, partner], axis=1),
                     jnp.concatenate([partner, block], axis=1))
    low = lax.ppermute(pair, "box", shifted_pairs(nb, 2))
    high = lax.ppermute(pair, "box", [(t, s) for s, t in shifted_pairs(nb, 2)])
    span = jnp.concatenate([low, pair, high], axis=1)
    start = 2 * n - depth + odd * n
    return lax.dynamic_slice_in_dim(span, start, n + 2 * depth, axis=1)


def chebyshev_local(rhs_c, b_c):
    depth = CHEB
    cx, cy, cz = rhs_c.shape
    both = jnp.stack([b_c, rhs_c])
    nb = lax.axis_size("box")
    if nb % 2 == 0 and nb > 2 and cx < depth <= 2 * cx:
        both = pair_extend(both, depth)
    else:
        both = deep_extend(both, "box", 1, depth)
    edge = jnp.zeros_like(both[:, :1, :depth])
    inner = deep_extend(both[:, 1:-1], "group", 2, depth)
    both = jnp.concatenate([
        jnp.concatenate([edge, both[:, :1], edge], axis=2),
        inner,
        jnp.concatenate([edge, both[:, -1:], edge], axis=2),
    ], axis=1)
    b_ext, rhs_ext = both[0], both[1]
    totals = (cx * lax.axis_size("box"), cy * lax.axis_size("group"))
    inside = inside_mask(b_ext.shape, depth, totals)
    coefs = [c * 0.0625 for c in coefs_of(b_ext, padded_neighbours(jnp.pad(b_ext, 1)))]
    diag = sum(coefs)
    inv_diag = jnp.where(inside, 1.0 / jnp.where(inside, diag, 1.0), 0.0)

    low, high = (0.05, 2.0)
    theta = (high + low) / 2.0
    delta = (high - low) / 2.0
    sigma = theta / delta
    rho = 1.0 / sigma
    solution = jnp.zeros_like(rhs_ext)
    remain = jnp.where(inside, rhs_ext, 0.0)
    direction = remain * inv_diag / theta
    for step in range(CHEB):
        solution = solution + direction
        if step + 1 < CHEB:
            nears = padded_neighbours(jnp.pad(direction, 1))
            remain = remain - apply_op(direction, nears, coefs)
            rho_next = 1.0 / (2.0 * sigma - rho)
            direction = rho_next * rho * direction + 2.0 * rho_next / delta * remain * inv_diag
            rho = rho_next
    return solution[depth:depth + cx, depth:depth + cy]


def grid_mask(shape, depth, axes, totals):
    inside = None
    for dim, (axis, total) in enumerate(zip(axes, totals)):
        own = shape[dim] - 2 * depth
        g = lax.axis_index(axis) * own - depth + lax.broadcasted_iota(jnp.int32, shape, dim)
        ok = (g >= 0) & (g < total)
        inside = ok if inside is None else inside & ok
    return inside


def shared_faces(b):
    def face(a, n):
        return jnp.where((a > 0) & (n > 0), 2.0 * a * n / (a + n), a + n)

    nears = padded_neighbours(jnp.pad(b, 1))
    lx, ly, lz = face(b, nears[0]), face(b, nears[2]), face(b, nears[4])
    hx = jnp.pad(lx, ((0, 1), (0, 0), (0, 0)))[1:]
    hy = jnp.pad(ly, ((0, 0), (0, 1), (0, 0)))[:, 1:]
    hz = jnp.pad(lz, ((0, 0), (0, 0), (0, 1)))[:, :, 1:]
    top = lax.broadcasted_iota(jnp.int32, b.shape, 2) == b.shape[2] - 1
    return [lx, hx, ly, hy, lz, jnp.where(top, b, hz)]


def low_faces(b):
    faces = []
    for dim in range(3):
        n = b.shape[dim]
        lo = lax.slice_in_dim(b, 0, n - 1, axis=dim)
        hi = lax.slice_in_dim(b, 1, n, axis=dim)
        inner = jnp.where((lo > 0) & (hi > 0), 2.0 * hi * lo / (hi + lo), hi + lo)
        faces.append(jnp.concatenate([lax.slice_in_dim(b, 0, 1, axis=dim), inner], axis=dim))
    return faces


def face_pairs(b, faces):
    pairs = []
    for dim, lo in enumerate(faces):
        n = b.shape[dim]
        hi = jnp.concatenate(
            [lax.slice_in_dim(lo, 1, n, axis=dim), lax.slice_in_dim(b, n - 1, n, axis=dim)], axis=dim
        )
        pairs += [lo, hi]
    return pairs


def per_device(right_side, inv_density, pressure):
    depth = SWEEPS + 1
    sx, sy, sz = pressure.shape
    b_e, rhs_e, fine = packed_halo([inv_density, right_side, pressure], [depth, depth - 1, depth])
    rhs_e, b_e, fine = lax.optimization_barrier((rhs_e, b_e, fine))
    totals = (sx * lax.axis_size("box"), sy * lax.axis_size("group"))
    inside = grid_mask(fine.shape, depth, ("box", "group"), totals)
    coefs = shared_faces(b_e)
    diag = sum(coefs)
    for sweep in range(SWEEPS):
        step = 2.0 / 3.0 * (rhs_e - apply_op(fine, padded_neighbours(jnp.pad(fine, 1)), coefs)) / diag
        fine = jnp.where(inside, fine + step, 0.0)
    own = (slice(depth, depth + sx), slice(depth, depth + sy))
    core = fine[own]
    nears = [
        fine[depth - 1:depth - 1 + sx, depth:depth + sy],
        fine[depth + 1:depth + 1 + sx, depth:depth + sy],
        fine[depth:depth + sx, depth - 1:depth - 1 + sy],
        fine[depth:depth + sx, depth + 1:depth + 1 + sy],
        shift_z(core, -1),
        shift_z(core, 1),
    ]
    res = right_side - apply_op(core, nears, [c[own] for c in coefs])
    fine, res = core, lax.optimization_barrier(res)
    coarse_rhs = block_mean(res)
    coarse_b = block_mean(inv_density)
    corr = chebyshev_local(coarse_rhs, coarse_b)
    return fine + expand(corr, fine.shape)


def solution(mesh):
    return jax.shard_map(
        per_device,
        mesh=mesh,
        in_specs=(P("box", "group", None), P("box", "group", None), P("box", "group", None)),
        out_specs=P("box", "group", None),
        check_vma=False,
    )
```
